128 devices in a mesh: req: 32 (over z, x, core), tp: 4 (over y).
Axes of the slice: x: 4, y: 4, z: 4, core: 2. Of those that a mesh axis runs over, the one named last changes fastest.
Arguments:
- tokens: bfloat16 [16512, 2048], P('req'), may hold values from -6 to 6
- layer_input: bfloat16 [16512, 256], P('req'), may hold values from -6 to 6
- input_gain: bfloat16 [2048], replicated, may hold values from 0.25 to 1.75
- q_weight: bfloat16 [2048, 2048], P(None, 'tp'), may hold values from -0.125 to 0.125
- k_weight: bfloat16 [2048, 512], replicated, may hold values from -0.125 to 0.125
- v_weight: bfloat16 [2048, 512], replicated, may hold values from -0.125 to 0.125
- q_gain: bfloat16 [256], replicated, may hold values from 0.099609375 to 1.8984375
- k_gain: bfloat16 [256], replicated, may hold values from 0.099609375 to 1.8984375
- o_weight: bfloat16 [2048, 2048], P('tp'), may hold values from -0.125 to 0.125
- attn_gain: bfloat16 [2048], replicated, may hold values from 0.25 to 1.75
- laurel_left: bfloat16 [2048, 64], replicated, may hold values from -0.125 to 0.125
- laurel_right: bfloat16 [64, 2048], replicated, may hold values from -0.75 to 0.75
- laurel_gain: bfloat16 [2048], replicated, may hold values from 0.25 to 1.75
- layer_gate: bfloat16 [2048, 256], replicated, may hold values from -0.125 to 0.125
- layer_proj: bfloat16 [256, 2048], replicated, may hold values from -0.375 to 0.375
- layer_gain: bfloat16 [2048], replicated, may hold values from 0.25 to 1.75
- piece_keys: bfloat16 [256, 1024, 512], P('req'), may hold values from -650 to 650
- piece_values: bfloat16 [256, 1024, 512], P('req'), may hold values from -6 to 6
- piece_owner: int32 [256], replicated, may hold values from 0 to 31, as said below
- piece_len: int32 [256], replicated, may hold values from 2 to 1024, as said below
- cache_keys: bfloat16 [128, 512, 512], P('req'), may hold values from -650 to 650
- cache_values: bfloat16 [128, 512, 512], P('req'), may hold values from -6 to 6
- cache_len: int32 [128], P('req'), may hold values from 2 to 512, as said below
Outputs:
- layer_out: bfloat16 [16512, 2048], P('req')
The draws below stay inside these ranges and needn't reach their ends.
Inputs may be any that keep to these rules, and one draw needn't show every extreme that they name: `piece_owner`: a piece of block b belongs to request (b - k) mod 32 for some k from 0 to 7; every block holds a piece of its own request and a piece with k = 7. `piece_len`: some piece is full. `cache_len`: some decode cache is full.
All inputs are finite; a program needn't handle non-finite values.
Results may differ from the reference program's by a relative error of at most 0.025.
Values may be sent and summed in bfloat16 or wider, within the bound.
No kernel may reach another device: no remote copies, remote signals or barrier semaphores. Data moves between devices by JAX's collectives and lax.ppermute only.
A program may use at most 192 MiB of HBM per device.

```python
import math
import jax
import jax.numpy as jnp
from jax import lax

D = 2048
H = 8
KVH = 2
HD = 256
RANK = 64
PLE = 256
CH = 512
DEC_DEV = 4
P_DEV = 8
PIECE = 1024
DCACHE = 512
REQUESTS = 32
ROWS = 516
TOKENS = 16512
PIECES = 256
DECODES = 128


def drawn(seed_key, row_count, length):
    base_key = jax.random.fold_in(seed_key, 0)
    base_draw = jnp.clip(jax.random.normal(base_key, (row_count, length, KVH * HD), jnp.float32), -6.0, 6.0)
    return base_draw.astype(jnp.bfloat16)


def forced_lengths(seed_key, row_count, most):
    draw_key, spot_key = jax.random.split(seed_key)
    lengths = jax.random.randint(draw_key, (row_count,), 2, most + 1)
    spot_index = jax.random.randint(spot_key, (), 0, row_count)
    return jnp.where(jnp.arange(row_count) == spot_index, most, lengths).astype(jnp.int32)


def draw_piece_keys(key, part):
    return drawn(key, PIECES, PIECE)


def draw_cache_keys(key, part):
    return drawn(key, DECODES, DCACHE)


def draw_piece_len(key, part):
    return forced_lengths(key, PIECES, PIECE)


def draw_cache_len(key, part):
    return forced_lengths(key, DECODES, DCACHE)


def draw_piece_owner(key, part):
    offset_key, first_key, second_key = jax.random.split(key, 3)
    offsets = jax.random.randint(offset_key, (REQUESTS, P_DEV), 0, P_DEV)
    first_slot = jax.random.randint(first_key, (REQUESTS, 1), 0, P_DEV)
    second_slot = (first_slot + jax.random.randint(second_key, (REQUESTS, 1), 1, P_DEV)) % P_DEV
    slot_ids = lax.broadcasted_iota(jnp.int32, (REQUESTS, P_DEV), 1)
    offsets = jnp.where(slot_ids == first_slot, 0, jnp.where(slot_ids == second_slot, P_DEV - 1, offsets))
    block_ids = lax.broadcasted_iota(jnp.int32, (REQUESTS, P_DEV), 0)
    return ((block_ids - offsets + REQUESTS) % REQUESTS).reshape(PIECES).astype(jnp.int32)


def shard_levels(rng, shape, cuts, smallest, high):
    def one(axis_at, shards_of):
        steps = jax.random.uniform(jax.random.fold_in(jax.random.fold_in(rng, 6), axis_at), (shards_of,), jnp.float32, smallest / len(cuts), high / len(cuts))
        return jnp.repeat(jnp.exp(steps), shape[axis_at] // shards_of).reshape((-1,) + (1,) * (len(shape) - axis_at - 1))

    factor_of = one(*cuts[0])
    for cut in cuts[1:]:
        factor_of = factor_of * one(*cut)
    return factor_of


def gaussian(own_key, shape, width, bound, cuts=(), kind=jnp.bfloat16):
    entries = width * jax.random.normal(own_key, shape, jnp.float32)
    if cuts:
        entries = entries * shard_levels(own_key, shape, cuts, -0.22, 0.18)
    return jnp.clip(entries, -bound, bound).astype(kind)


def setup_inputs(seed: int = 0) -> dict:
    arg_keys = jax.random.split(jax.random.key(seed), 24)
    tokens = gaussian(arg_keys[0], (TOKENS, D), 1.0, 6.0, ((0, 32),))
    layer_input = gaussian(arg_keys[1], (TOKENS, PLE), 1.0, 6.0, ((0, 32),))
    input_gain = jnp.clip(1.0 + 0.15 * jax.random.normal(arg_keys[2], (D,), jnp.float32), 0.25, 1.75).astype(jnp.bfloat16)
    q_weight = gaussian(arg_keys[3], (D, H * HD), D ** -0.5, 0.125, ((1, 4),))
    k_weight = gaussian(arg_keys[4], (D, KVH * HD), D ** -0.5, 0.125)
    v_weight = gaussian(arg_keys[5], (D, KVH * HD), D ** -0.5, 0.125)
    q_gain = jnp.clip(1.0 + 0.18 * jax.random.normal(arg_keys[6], (HD,), jnp.float32), 0.099609375, 1.8984375).astype(jnp.bfloat16)
    k_gain = jnp.clip(1.0 + 0.18 * jax.random.normal(arg_keys[7], (HD,), jnp.float32), 0.099609375, 1.8984375).astype(jnp.bfloat16)
    o_weight = gaussian(arg_keys[8], (H * HD, D), (H * HD) ** -0.5, 0.125, ((0, 4),))
    attn_gain = jnp.clip(1.0 + 0.15 * jax.random.normal(arg_keys[9], (D,), jnp.float32), 0.25, 1.75).astype(jnp.bfloat16)
    laurel_left = gaussian(arg_keys[10], (D, RANK), D ** -0.5, 0.125)
    laurel_right = gaussian(arg_keys[11], (RANK, D), RANK ** -0.5, 0.75)
    laurel_gain = jnp.clip(1.0 + 0.15 * jax.random.normal(arg_keys[12], (D,), jnp.float32), 0.25, 1.75).astype(jnp.bfloat16)
    layer_gate = gaussian(arg_keys[13], (D, PLE), D ** -0.5, 0.125)
    layer_proj = gaussian(arg_keys[14], (PLE, D), PLE ** -0.5, 0.375)
    layer_gain = jnp.clip(1.0 + 0.15 * jax.random.normal(arg_keys[15], (D,), jnp.float32), 0.25, 1.75).astype(jnp.bfloat16)
    piece_keys = draw_piece_keys(jax.random.fold_in(arg_keys[23], 71), 0)
    piece_values = gaussian(arg_keys[17], (PIECES, PIECE, KVH * HD), 1.0, 6.0, ((0, 32),))
    piece_owner = draw_piece_owner(jax.random.fold_in(arg_keys[23], 71), 0)
    piece_len = draw_piece_len(jax.random.fold_in(arg_keys[23], 71), 0)
    cache_keys = draw_cache_keys(jax.random.fold_in(arg_keys[23], 71), 0)
    cache_values = gaussian(arg_keys[21], (DECODES, DCACHE, KVH * HD), 1.0, 6.0, ((0, 32),))
    cache_len = draw_cache_len(jax.random.fold_in(arg_keys[23], 71), 0)
    return dict(tokens=tokens, layer_input=layer_input, input_gain=input_gain, q_weight=q_weight, k_weight=k_weight, v_weight=v_weight, q_gain=q_gain, k_gain=k_gain, o_weight=o_weight, attn_gain=attn_gain, laurel_left=laurel_left, laurel_right=laurel_right, laurel_gain=laurel_gain, layer_gate=layer_gate, layer_proj=layer_proj, layer_gain=layer_gain, piece_keys=piece_keys, piece_values=piece_values, piece_owner=piece_owner, piece_len=piece_len, cache_keys=cache_keys, cache_values=cache_values, cache_len=cache_len)


LOWEST = -1e+30

def rounded(x):
    return lax.optimization_barrier(x.astype(jnp.bfloat16))

def normed(x, scale_gain):
    return x * lax.rsqrt(lax.optimization_barrier(jnp.mean(x * x, axis=-1, keepdims=True)) + 1e-06) * scale_gain

def widened(x):
    return jnp.repeat(x, H // KVH, axis=-2)

def finish_rows(proj_sum, tok_float, tok_norm, extra_input, attn_gain, laurel_left, laurel_right, laurel_gain, layer_gate, layer_proj, layer_gain):
    laurel_low = jnp.dot(tok_norm, laurel_left, preferred_element_type=jnp.float32).astype(jnp.bfloat16)
    laurel_out = tok_norm.astype(jnp.float32) + normed(jnp.dot(laurel_low, laurel_right, preferred_element_type=jnp.float32), laurel_gain.astype(jnp.float32))
    mixture = (tok_float + normed(proj_sum, attn_gain.astype(jnp.float32)) + laurel_out) * (1.0 / math.sqrt(2.0))
    gate_act = jnp.dot(mixture.astype(jnp.bfloat16), layer_gate, preferred_element_type=jnp.float32)
    gate_out = (jax.nn.gelu(gate_act, approximate=True) * extra_input.astype(jnp.float32)).astype(jnp.bfloat16)
    return (mixture + normed(jnp.dot(gate_out, layer_proj, preferred_element_type=jnp.float32), layer_gain.astype(jnp.float32))).astype(jnp.bfloat16)

def reference(tokens, layer_input, input_gain, q_weight, k_weight, v_weight, q_gain, k_gain, o_weight, attn_gain, laurel_left, laurel_right, laurel_gain, layer_gate, layer_proj, layer_gain, piece_keys, piece_values, piece_owner, piece_len, cache_keys, cache_values, cache_len):
    highest_prec = lax.Precision.HIGHEST
    score_scale = 1.0 / math.sqrt(HD)
    tok_float = tokens.astype(jnp.float32)
    tok_norm = rounded(normed(tok_float, input_gain.astype(jnp.float32)))
    queries = rounded(normed(jnp.dot(tok_norm, q_weight, preferred_element_type=jnp.float32).reshape(TOKENS, H, HD), q_gain.astype(jnp.float32)))
    new_keys = rounded(normed(jnp.dot(tok_norm, k_weight, preferred_element_type=jnp.float32).reshape(TOKENS, KVH, HD), k_gain.astype(jnp.float32)))
    new_values = rounded(normed(jnp.dot(tok_norm, v_weight, preferred_element_type=jnp.float32).reshape(TOKENS, KVH, HD), 1.0))
    queries = queries.reshape(REQUESTS, ROWS, H, HD)
    new_keys = new_keys.reshape(REQUESTS, ROWS, KVH, HD)
    new_values = new_values.reshape(REQUESTS, ROWS, KVH, HD)
    span_q = queries[:, :CH]
    near_q = span_q.astype(jnp.float32)
    near_k = widened(new_keys[:, :CH]).astype(jnp.float32)
    near_v = widened(new_values[:, :CH]).astype(jnp.float32)
    near_scores = jnp.einsum('rihd,rjhd->rhij', near_q, near_k, precision=highest_prec) * score_scale
    causal = lax.broadcasted_iota(jnp.int32, (CH, CH), 1) <= lax.broadcasted_iota(jnp.int32, (CH, CH), 0)
    near_scores = jnp.where(causal, near_scores, LOWEST)
    near_top = lax.optimization_barrier(jnp.max(near_scores, axis=-1))
    near_exp = jnp.exp(near_scores - near_top[..., None])
    near_total = lax.optimization_barrier(jnp.sum(near_exp, axis=-1))
    near_sum = jnp.einsum('rhij,rjhd->rihd', rounded(near_exp).astype(jnp.float32), near_v, precision=highest_prec)
    near_top = jnp.transpose(near_top, (0, 2, 1))
    near_total = jnp.transpose(near_total, (0, 2, 1))

    def block_step(running, block_data):
        run_top, run_weight, run_sum = running
        blk_keys, blk_values, blk_owner, blk_len = block_data
        maxima, totals, numerators = ([], [], [])
        for slot_index in range(P_DEV):
            asked_rows = lax.dynamic_index_in_dim(span_q, blk_owner[slot_index], 0, keepdims=False).astype(jnp.float32)
            piece_key = widened(blk_keys[slot_index].reshape(PIECE, KVH, HD)).astype(jnp.float32)
            piece_value = widened(blk_values[slot_index].reshape(PIECE, KVH, HD)).astype(jnp.float32)
            piece_scores = jnp.einsum('ihd,jhd->hij', asked_rows, piece_key, precision=highest_prec) * score_scale
            is_valid = lax.broadcasted_iota(jnp.int32, (1, 1, PIECE), 2) < blk_len[slot_index]
            piece_scores = jnp.where(is_valid, piece_scores, LOWEST)
            piece_top = lax.optimization_barrier(jnp.max(piece_scores, axis=-1))
            piece_exp = jnp.exp(piece_scores - piece_top[..., None])
            maxima.append(piece_top.T)
            totals.append(lax.optimization_barrier(jnp.sum(piece_exp, axis=-1)).T)
            numerators.append(jnp.einsum('hij,jhd->ihd', rounded(piece_exp).astype(jnp.float32), piece_value, precision=highest_prec))
        maxima = jnp.stack(maxima)
        totals = jnp.stack(totals)
        numerators = jnp.stack(numerators)
        for slot_index in range(P_DEV):
            owner_id = blk_owner[slot_index]
            same_owner = (blk_owner == owner_id)[:, None, None]
            group_top = lax.optimization_barrier(jnp.max(jnp.where(same_owner, maxima, LOWEST), axis=0))
            factor = jnp.where(same_owner, jnp.exp(jnp.where(same_owner, maxima - group_top, 0.0)), 0.0)
            group_total = lax.optimization_barrier(jnp.sum(totals * factor, axis=0))
            group_out = rounded(lax.optimization_barrier(jnp.sum(numerators * factor[..., None], axis=0)) / group_total[..., None]).astype(jnp.float32)
            earlier = jnp.arange(P_DEV) < slot_index
            is_first = jnp.logical_not(jnp.any(jnp.logical_and(earlier, blk_owner == owner_id)))
            old_top = lax.dynamic_index_in_dim(run_top, owner_id, 0, keepdims=False)
            old_weight = lax.dynamic_index_in_dim(run_weight, owner_id, 0, keepdims=False)
            old_sum = lax.dynamic_index_in_dim(run_sum, owner_id, 0, keepdims=False)
            new_top = jnp.where(is_first, jnp.maximum(old_top, group_top), old_top)
            keep_scale = jnp.exp(old_top - new_top)
            added_weight = jnp.where(is_first, group_total * jnp.exp(group_top - new_top), 0.0)
            run_top = lax.dynamic_update_index_in_dim(run_top, new_top, owner_id, 0)
            run_weight = lax.dynamic_update_index_in_dim(run_weight, old_weight * keep_scale + added_weight, owner_id, 0)
            run_sum = lax.dynamic_update_index_in_dim(run_sum, old_sum * keep_scale[..., None] + added_weight[..., None] * group_out, owner_id, 0)
        return ((run_top, run_weight, run_sum), None)
    start_state = (jnp.full((REQUESTS, CH, H), LOWEST, jnp.float32), jnp.zeros((REQUESTS, CH, H), jnp.float32), jnp.zeros((REQUESTS, CH, H, HD), jnp.float32))
    blocks = (piece_keys.reshape(REQUESTS, P_DEV, PIECE, KVH * HD), piece_values.reshape(REQUESTS, P_DEV, PIECE, KVH * HD), piece_owner.reshape(REQUESTS, P_DEV), piece_len.reshape(REQUESTS, P_DEV))
    (far_top, far_weight, far_sum), unused = lax.scan(block_step, start_state, blocks)
    final_top = jnp.maximum(far_top, near_top)
    far_scale = jnp.exp(far_top - final_top)
    near_scale = jnp.exp(near_top - final_top)
    span_att = rounded((far_sum * far_scale[..., None] + near_sum * near_scale[..., None]) / (far_weight * far_scale + near_total * near_scale)[..., None])
    group_size = H // KVH
    decode_q = queries[:, CH:].reshape(DECODES, KVH, group_size, HD).astype(jnp.float32)
    decode_k = new_keys[:, CH:].reshape(DECODES, KVH, HD).astype(jnp.float32)
    decode_v = new_values[:, CH:].reshape(DECODES, KVH, HD).astype(jnp.float32)
    cache_key = cache_keys.reshape(DECODES, DCACHE, KVH, HD).astype(jnp.float32)
    cache_value = cache_values.reshape(DECODES, DCACHE, KVH, HD).astype(jnp.float32)
    cache_scores = jnp.einsum('tkgd,tjkd->tkgj', decode_q, cache_key, precision=highest_prec) * score_scale
    cache_valid = lax.broadcasted_iota(jnp.int32, (1, 1, 1, DCACHE), 3) < cache_len[:, None, None, None]
    cache_scores = jnp.where(cache_valid, cache_scores, LOWEST)
    own_scores = jnp.einsum('tkgd,tkd->tkg', decode_q, decode_k, precision=highest_prec) * score_scale
    decode_top = jnp.maximum(lax.optimization_barrier(jnp.max(cache_scores, axis=-1)), own_scores)
    cache_exp = jnp.exp(cache_scores - decode_top[..., None])
    own_exp = jnp.exp(own_scores - decode_top)
    decode_total = lax.optimization_barrier(jnp.sum(cache_exp, axis=-1)) + own_exp
    decode_sum = jnp.einsum('tkgj,tjkd->tkgd', rounded(cache_exp).astype(jnp.float32), cache_value, precision=highest_prec) + rounded(own_exp).astype(jnp.float32)[..., None] * decode_v[:, :, None, :]
    decode_att = rounded(decode_sum / decode_total[..., None])
    attended = jnp.concatenate([span_att.reshape(REQUESTS, CH, H * HD), decode_att.reshape(REQUESTS, DEC_DEV, H * HD)], axis=1).reshape(TOKENS, H * HD)
    proj_sum = jnp.dot(attended, o_weight, preferred_element_type=jnp.float32)
    return finish_rows(proj_sum, tok_float, tok_norm, layer_input, attn_gain, laurel_left, laurel_right, laurel_gain, layer_gate, layer_proj, layer_gain)
```

```python
import functools
import math

import jax
import jax.numpy as jnp
from jax import lax
from jax.experimental import pallas as pl
from jax.experimental.pallas import tpu as pltpu
from jax.sharding import PartitionSpec as P

H = 8
KVH = 2
HD = 256
CH = 512
DEC_DEV = 4
P_DEV = 8
PIECE = 1024
DCACHE = 512
ROWS = 516
STAT = 128


LOWEST = -1e30
SCORE_SCALE = 1.0 / math.sqrt(HD)


def passed_along(x, axis, by):
    length = lax.axis_size(axis)
    return lax.ppermute(x, axis, [(i, (i + by) % length) for i in range(length)])


def rounded(x):
    return lax.optimization_barrier(x.astype(jnp.bfloat16))


def normed(x, scale_gain):
    return x * lax.rsqrt(jnp.mean(x * x, axis=-1, keepdims=True) + 1e-06) * scale_gain


def head_partial(q, keys, values, valid):
    scores = (
        lax.dot_general(q, keys, (((1,), (1,)), ((), ())), preferred_element_type=jnp.float32)
        * SCORE_SCALE
    )
    scores = jnp.where(valid, scores, LOWEST)
    top = jnp.max(scores, axis=1, keepdims=True)
    weights = jnp.exp(scores - top)
    total = jnp.sum(weights, axis=1, keepdims=True)
    summed = jnp.dot(weights.astype(jnp.bfloat16), values, preferred_element_type=jnp.float32)
    return top, total, summed


def split3(x):
    hi = x.astype(jnp.bfloat16).astype(jnp.float32)
    rest = x - hi
    mid = rest.astype(jnp.bfloat16).astype(jnp.float32)
    lo = rest - mid
    return hi, mid, lo


def piece_kernel(tab_ref, *refs):
    q_refs = refs[:P_DEV]
    k_ref, v_ref, out_ref, qbuf, acc_m, acc_l, acc_n = refs[P_DEV:]
    step = pl.program_id(0)
    slot = tab_ref[P_DEV + step]
    length = tab_ref[2 * P_DEV + step]
    first = tab_ref[3 * P_DEV + step]
    last = tab_ref[4 * P_DEV + step]
    for k in range(P_DEV):

        @pl.when(slot == k)
        def _(k=k):
            qbuf[...] = q_refs[k][...]

    keys = k_ref[0]
    values = v_ref[0]
    rows = qbuf.shape[0]
    valid = lax.broadcasted_iota(jnp.int32, (rows, keys.shape[0]), 1) < length
    for h in range(2):
        top, total, summed = head_partial(qbuf[:, h * HD:(h + 1) * HD], keys, values, valid)

        @pl.when(first == 1)
        def _(h=h, top=top, total=total, summed=summed):
            acc_m[h] = top
            acc_l[h] = total
            acc_n[h] = summed

        @pl.when(first == 0)
        def _(h=h, top=top, total=total, summed=summed):
            old = acc_m[h]
            new = jnp.maximum(old, top)
            keep = jnp.exp(old - new)
            add = jnp.exp(top - new)
            acc_l[h] = acc_l[h] * keep + total * add
            acc_n[h] = acc_n[h] * keep + summed * add
            acc_m[h] = new

    @pl.when(last == 1)
    def _():
        lane = lax.broadcasted_iota(jnp.int32, (rows, STAT), 1)
        stat = jnp.zeros((rows, STAT), jnp.float32)
        for h in range(2):
            total = acc_l[h]
            out_ref[slot, :, h * HD:(h + 1) * HD] = (acc_n[h] / total).astype(jnp.bfloat16)
            for i, part in enumerate(split3(acc_m[h]) + split3(total)):
                stat = jnp.where(lane == 8 * h + i, part, stat)
        out_ref[slot, :, 2 * HD:] = stat.astype(jnp.bfloat16)


def piece_attention(table, windows, piece_keys, piece_values):
    rows = windows[0].shape[0]
    pieces = piece_keys.shape[0]
    q_spec = pl.BlockSpec((rows, 2 * HD), lambda s, t: (0, 0))
    kv_spec = pl.BlockSpec((1, PIECE, HD), lambda s, t: (t[s], 0, t[5 * P_DEV]))
    grid_spec = pltpu.PrefetchScalarGridSpec(
        num_scalar_prefetch=1,
        grid=(pieces,),
        in_specs=[q_spec] * P_DEV + [kv_spec, kv_spec],
        out_specs=pl.BlockSpec((P_DEV, rows, 2 * HD + STAT), lambda s, t: (0, 0, 0)),
        scratch_shapes=[
            pltpu.VMEM((rows, 2 * HD), jnp.bfloat16),
            pltpu.VMEM((2, rows, 1), jnp.float32),
            pltpu.VMEM((2, rows, 1), jnp.float32),
            pltpu.VMEM((2, rows, HD), jnp.float32),
        ],
    )
    flops = pieces * 2 * 2 * 2 * rows * PIECE * HD
    return pl.pallas_call(
        piece_kernel,
        grid_spec=grid_spec,
        out_shape=jax.ShapeDtypeStruct((P_DEV, rows, 2 * HD + STAT), jnp.bfloat16),
        compiler_params=pltpu.CompilerParams(
            dimension_semantics=("arbitrary",), vmem_limit_bytes=56 * 1024 * 1024
        ),
        cost_estimate=pl.CostEstimate(
            flops=flops,
            transcendentals=pieces * 2 * rows * PIECE,
            bytes_accessed=pieces * 2 * PIECE * HD * 2 + P_DEV * rows * 2 * HD * 2 * 2,
        ),
    )(table, *windows, piece_keys, piece_values)


def self_kernel(q_ref, k_ref, v_ref, n_ref, stat_ref):
    rows = q_ref.shape[0]
    valid = lax.broadcasted_iota(jnp.int32, (rows, rows), 1) <= lax.broadcasted_iota(
        jnp.int32, (rows, rows), 0
    )
    lane = lax.broadcasted_iota(jnp.int32, (rows, STAT), 1)
    stat = jnp.zeros((rows, STAT), jnp.float32)
    keys = k_ref[...]
    values = v_ref[...]
    for h in range(2):
        top, total, summed = head_partial(q_ref[:, h * HD:(h + 1) * HD], keys, values, valid)
        n_ref[:, h * HD:(h + 1) * HD] = summed
        stat = jnp.where(lane == 8 * h, top, stat)
        stat = jnp.where(lane == 8 * h + 3, total, stat)
    stat_ref[...] = stat


def self_attention(q, keys, values):
    rows = q.shape[0]
    return pl.pallas_call(
        self_kernel,
        out_shape=(
            jax.ShapeDtypeStruct((rows, 2 * HD), jnp.float32),
            jax.ShapeDtypeStruct((rows, STAT), jnp.float32),
        ),
        compiler_params=pltpu.CompilerParams(vmem_limit_bytes=48 * 1024 * 1024),
        cost_estimate=pl.CostEstimate(
            flops=2 * 2 * 2 * rows * rows * HD,
            transcendentals=2 * rows * rows,
            bytes_accessed=rows * 2 * HD * 2 + 2 * rows * HD * 2 + rows * (2 * HD + STAT) * 4,
        ),
    )(q, keys, values)


def finish_rows(
    proj_sum,
    tok_float,
    tok_norm,
    extra_input,
    attn_gain,
    laurel_left,
    laurel_right,
    laurel_gain,
    layer_gate,
    layer_proj,
    layer_gain,
):
    laurel_low = jnp.dot(tok_norm, laurel_left, preferred_element_type=jnp.float32).astype(
        jnp.bfloat16
    )
    laurel_out = tok_norm.astype(jnp.float32) + normed(
        jnp.dot(laurel_low, laurel_right, preferred_element_type=jnp.float32),
        laurel_gain.astype(jnp.float32),
    )
    mixture = (tok_float + normed(proj_sum, attn_gain.astype(jnp.float32)) + laurel_out) * (
        1.0 / math.sqrt(2.0)
    )
    gate_act = jnp.dot(mixture.astype(jnp.bfloat16), layer_gate, preferred_element_type=jnp.float32)
    gate_out = (jax.nn.gelu(gate_act, approximate=True) * extra_input.astype(jnp.float32)).astype(
        jnp.bfloat16
    )
    return (
        mixture
        + normed(
            jnp.dot(gate_out, layer_proj, preferred_element_type=jnp.float32),
            layer_gain.astype(jnp.float32),
        )
    ).astype(jnp.bfloat16)


def schedule_table(distances, lengths, kv_head):
    ids = jnp.arange(P_DEV, dtype=jnp.int32)
    before = (distances[None, :] < distances[:, None]) | (
        (distances[None, :] == distances[:, None]) & (ids[None, :] < ids[:, None])
    )
    rank = jnp.sum(before.astype(jnp.int32), axis=1)
    chosen = rank[:, None] == ids[None, :]
    order = jnp.sum(jnp.where(chosen, ids[:, None], 0), axis=0)
    slot = jnp.sum(jnp.where(chosen, distances[:, None], 0), axis=0)
    length = jnp.sum(jnp.where(chosen, lengths[:, None], 0), axis=0)
    minus = jnp.full((1,), -1, jnp.int32)
    first = (slot != jnp.concatenate([minus, slot[:-1]])).astype(jnp.int32)
    last = (slot != jnp.concatenate([slot[1:], minus])).astype(jnp.int32)
    kv_row = jnp.full((P_DEV,), kv_head, jnp.int32)
    return jnp.concatenate([order, slot, length, first, last, kv_row]).astype(jnp.int32)


def body(
    tokens,
    layer_input,
    input_gain,
    q_weight,
    k_weight,
    v_weight,
    q_gain,
    k_gain,
    o_weight,
    attn_gain,
    laurel_left,
    laurel_right,
    laurel_gain,
    layer_gate,
    layer_proj,
    layer_gain,
    piece_keys,
    piece_values,
    piece_owner,
    piece_len,
    cache_keys,
    cache_values,
    cache_len,
):
    req_count = lax.axis_size("req")
    tp_count = lax.axis_size("tp")
    req_index = lax.axis_index("req")
    tp_index = lax.axis_index("tp")
    local_heads = H // tp_count
    kv_head = tp_index * local_heads // (H // KVH)
    full_o_weight = lax.all_gather(o_weight, "tp", axis=0, tiled=True)
    tok_float = tokens.astype(jnp.float32)
    tok_norm = normed(tok_float, input_gain.astype(jnp.float32)).astype(jnp.bfloat16)
    queries = jnp.dot(tok_norm, q_weight, preferred_element_type=jnp.float32).reshape(
        ROWS, local_heads, HD
    )
    queries = (
        normed(queries, q_gain.astype(jnp.float32))
        .astype(jnp.bfloat16)
        .reshape(ROWS, local_heads * HD)
    )
    key_cols = lax.dynamic_slice_in_dim(k_weight, kv_head * HD, HD, 1)
    value_cols = lax.dynamic_slice_in_dim(v_weight, kv_head * HD, HD, 1)
    new_keys = normed(
        jnp.dot(tok_norm, key_cols, preferred_element_type=jnp.float32), k_gain.astype(jnp.float32)
    ).astype(jnp.bfloat16)
    new_values = normed(
        jnp.dot(tok_norm, value_cols, preferred_element_type=jnp.float32), 1.0
    ).astype(jnp.bfloat16)
    own_block = queries[:CH]
    windows = [own_block] + [passed_along(own_block, "req", d) for d in range(1, P_DEV)]
    self_sum, self_stat = self_attention(own_block, new_keys[:CH], new_values[:CH])

    owners = lax.dynamic_slice_in_dim(piece_owner, req_index * P_DEV, P_DEV)
    lengths = lax.dynamic_slice_in_dim(piece_len, req_index * P_DEV, P_DEV)
    distances = (req_index - owners + req_count) % req_count
    table = schedule_table(distances, lengths, kv_head)
    packed = piece_attention(table, windows, piece_keys, piece_values)
    slots = [packed[0]] + [passed_along(packed[d], "req", -d) for d in range(1, P_DEV)]

    block_ids = (req_index + jnp.arange(P_DEV, dtype=jnp.int32)) % req_count
    block_owners = jnp.take(piece_owner.reshape(req_count, P_DEV), block_ids, axis=0)
    has = jnp.any(block_owners == req_index, axis=1)
    tops, totals = [], []
    for got in slots:
        stat = got[:, 2 * HD:2 * HD + 16].astype(jnp.float32)
        tops.append(
            jnp.stack([stat[:, 8 * h] + stat[:, 8 * h + 1] + stat[:, 8 * h + 2] for h in range(2)], 1)
        )
        totals.append(
            jnp.stack([stat[:, 8 * h + 3] + stat[:, 8 * h + 4] + stat[:, 8 * h + 5] for h in range(2)], 1)
        )
    tops = jnp.stack(tops)
    totals = jnp.stack(totals)
    has3 = has[:, None, None]
    far_top = jnp.max(jnp.where(has3, tops, LOWEST), axis=0)
    weights = jnp.where(has3, totals * jnp.exp(tops - far_top[None]), 0.0)
    far_total = jnp.sum(weights, axis=0)
    far_sum = None
    for d, got in enumerate(slots):
        term = jnp.where(
            has[d],
            weights[d][:, :, None] * got[:, :2 * HD].reshape(CH, local_heads, HD).astype(jnp.float32),
            0.0,
        )
        far_sum = term if far_sum is None else far_sum + term
    near_top = jnp.stack([self_stat[:, 8 * h] for h in range(2)], 1)
    near_total = jnp.stack([self_stat[:, 8 * h + 3] for h in range(2)], 1)
    near_sum = self_sum.reshape(CH, local_heads, HD)
    final_top = jnp.maximum(far_top, near_top)
    far_scale = jnp.exp(far_top - final_top)
    near_scale = jnp.exp(near_top - final_top)
    span_att = (
        (
            (far_sum * far_scale[:, :, None] + near_sum * near_scale[:, :, None])
            / (far_total * far_scale + near_total * near_scale)[:, :, None]
        )
        .reshape(CH, local_heads * HD)
        .astype(jnp.bfloat16)
    )
    decode_q = queries[CH:].reshape(DEC_DEV, local_heads, HD)
    cache_key = lax.dynamic_slice_in_dim(cache_keys, kv_head * HD, HD, 2)
    cache_value = lax.dynamic_slice_in_dim(cache_values, kv_head * HD, HD, 2)
    cache_scores = (
        jnp.einsum("thd,tjd->thj", decode_q, cache_key, preferred_element_type=jnp.float32)
        * SCORE_SCALE
    )
    cache_valid = (
        lax.broadcasted_iota(jnp.int32, (DEC_DEV, 1, DCACHE), 2) < cache_len[:, None, None]
    )
    cache_scores = jnp.where(cache_valid, cache_scores, LOWEST)
    own_scores = (
        jnp.einsum("thd,td->th", decode_q, new_keys[CH:], preferred_element_type=jnp.float32)
        * SCORE_SCALE
    )
    decode_top = jnp.maximum(jnp.max(cache_scores, axis=-1), own_scores)
    cache_exp = jnp.exp(cache_scores - decode_top[:, :, None])
    own_exp = jnp.exp(own_scores - decode_top)
    decode_total = jnp.sum(cache_exp, axis=-1) + own_exp
    decode_sum = (
        jnp.einsum(
            "thj,tjd->thd",
            cache_exp.astype(jnp.bfloat16),
            cache_value,
            preferred_element_type=jnp.float32,
        )
        + rounded(own_exp).astype(jnp.float32)[:, :, None]
        * new_values[CH:].astype(jnp.float32)[:, None, :]
    )
    decode_att = (
        (decode_sum / decode_total[:, :, None])
        .reshape(DEC_DEV, local_heads * HD)
        .astype(jnp.bfloat16)
    )
    attended = jnp.concatenate([span_att, decode_att], axis=0)
    full_attended = lax.all_gather(attended, "tp", axis=1, tiled=True)
    proj_sum = jnp.dot(full_attended, full_o_weight, preferred_element_type=jnp.float32)
    return finish_rows(
        proj_sum,
        tok_float,
        tok_norm,
        layer_input,
        attn_gain,
        laurel_left,
        laurel_right,
        laurel_gain,
        layer_gate,
        layer_proj,
        layer_gain,
    )


def solution(mesh):
    placed = (
        P("req", None),
        P("req", None),
        P(),
        P(None, "tp"),
        P(),
        P(),
        P(),
        P(),
        P("tp", None),
        P(),
        P(),
        P(),
        P(),
        P(),
        P(),
        P(),
        P("req", None, None),
        P("req", None, None),
        P(),
        P(),
        P("req", None, None),
        P("req", None, None),
        P("req"),
    )
    return jax.shard_map(
        body, mesh=mesh, in_specs=placed, out_specs=P("req", None), check_vma=False
    )
```

```python
import functools
import math

import jax
import jax.numpy as jnp
from jax import lax
from jax.experimental import pallas as pl
from jax.experimental.pallas import tpu as pltpu
from jax.sharding import PartitionSpec as P

H = 8
KVH = 2
HD = 256
CH = 512
DEC_DEV = 4
P_DEV = 8
PIECE = 1024
DCACHE = 512
ROWS = 516
STAT = 128


LOWEST = -1e30
SCORE_SCALE = 1.0 / math.sqrt(HD)


def passed_along(x, axis, by):
    length = lax.axis_size(axis)
    return lax.ppermute(x, axis, [(i, (i + by) % length) for i in range(length)])


def rounded(x):
    return lax.optimization_barrier(x.astype(jnp.bfloat16))


def normed(x, scale_gain):
    return x * lax.rsqrt(jnp.mean(x * x, axis=-1, keepdims=True) + 1e-06) * scale_gain


def head_partial(q, keys, values, valid):
    scores = (
        lax.dot_general(q, keys, (((1,), (1,)), ((), ())), preferred_element_type=jnp.float32)
        * SCORE_SCALE
    )
    scores = jnp.where(valid, scores, LOWEST)
    top = jnp.max(scores, axis=1, keepdims=True)
    weights = jnp.exp(scores - top)
    total = jnp.sum(weights, axis=1, keepdims=True)
    summed = jnp.dot(weights.astype(jnp.bfloat16), values, preferred_element_type=jnp.float32)
    return top, total, summed


def split3(x):
    hi = x.astype(jnp.bfloat16).astype(jnp.float32)
    rest = x - hi
    mid = rest.astype(jnp.bfloat16).astype(jnp.float32)
    lo = rest - mid
    return hi, mid, lo


def piece_kernel(tab_ref, *refs):
    q_refs = refs[:P_DEV]
    k_ref, v_ref = refs[P_DEV:P_DEV + 2]
    out_refs = refs[P_DEV + 3:2 * P_DEV + 3]
    qbuf, fin, acc_m, acc_l, acc_n = refs[2 * P_DEV + 3:]
    step = pl.program_id(0)
    slot = tab_ref[P_DEV + step]
    length = tab_ref[2 * P_DEV + step]
    first = tab_ref[3 * P_DEV + step]
    last = tab_ref[4 * P_DEV + step]
    for k in range(P_DEV):

        @pl.when(slot == k)
        def _(k=k):
            qbuf[...] = q_refs[k][...]

    keys = k_ref[0]
    values = v_ref[0]
    rows = qbuf.shape[0]
    valid = lax.broadcasted_iota(jnp.int32, (rows, keys.shape[0]), 1) < length
    for h in range(2):
        top, total, summed = head_partial(qbuf[:, h * HD:(h + 1) * HD], keys, values, valid)

        @pl.when(first == 1)
        def _(h=h, top=top, total=total, summed=summed):
            acc_m[h] = top
            acc_l[h] = total
            acc_n[h] = summed

        @pl.when(first == 0)
        def _(h=h, top=top, total=total, summed=summed):
            old = acc_m[h]
            new = jnp.maximum(old, top)
            keep = jnp.exp(old - new)
            add = jnp.exp(top - new)
            acc_l[h] = acc_l[h] * keep + total * add
            acc_n[h] = acc_n[h] * keep + summed * add
            acc_m[h] = new

    @pl.when(last == 1)
    def _():
        lane = lax.broadcasted_iota(jnp.int32, (rows, STAT), 1)
        stat = jnp.zeros((rows, STAT), jnp.float32)
        for h in range(2):
            total = acc_l[h]
            fin[:, h * HD:(h + 1) * HD] = (acc_n[h] / total).astype(jnp.bfloat16)
            for i, part in enumerate(split3(acc_m[h]) + split3(total)):
                stat = jnp.where(lane == 8 * h + i, part, stat)
        fin[:, 2 * HD:] = stat.astype(jnp.bfloat16)
        for k in range(P_DEV):

            @pl.when(slot == k)
            def _(k=k):
                out_refs[k][...] = fin[...]


def piece_attention(table, windows, piece_keys, piece_values, after):
    rows = windows[0].shape[0]
    pieces = piece_keys.shape[0]
    q_spec = pl.BlockSpec((rows, 2 * HD), lambda s, t: (0, 0))
    kv_spec = pl.BlockSpec((1, PIECE, HD), lambda s, t: (t[s], 0, t[5 * P_DEV]))
    out_spec = pl.BlockSpec((rows, 2 * HD + STAT), lambda s, t: (0, 0))
    grid_spec = pltpu.PrefetchScalarGridSpec(
        num_scalar_prefetch=1,
        grid=(pieces,),
        in_specs=[q_spec] * P_DEV + [kv_spec, kv_spec, pl.BlockSpec(memory_space=pl.ANY)],
        out_specs=[out_spec] * P_DEV,
        scratch_shapes=[
            pltpu.VMEM((rows, 2 * HD), jnp.bfloat16),
            pltpu.VMEM((rows, 2 * HD + STAT), jnp.bfloat16),
            pltpu.VMEM((2, rows, 1), jnp.float32),
            pltpu.VMEM((2, rows, 1), jnp.float32),
            pltpu.VMEM((2, rows, HD), jnp.float32),
        ],
    )
    flops = pieces * 2 * 2 * 2 * rows * PIECE * HD
    return pl.pallas_call(
        piece_kernel,
        grid_spec=grid_spec,
        out_shape=[jax.ShapeDtypeStruct((rows, 2 * HD + STAT), jnp.bfloat16)] * P_DEV,
        compiler_params=pltpu.CompilerParams(
            dimension_semantics=("arbitrary",), vmem_limit_bytes=56 * 1024 * 1024
        ),
        cost_estimate=pl.CostEstimate(
            flops=flops,
            transcendentals=pieces * 2 * rows * PIECE,
            bytes_accessed=pieces * 2 * PIECE * HD * 2 + P_DEV * rows * 2 * HD * 2 * 2,
        ),
    )(table, *windows, piece_keys, piece_values, after)


def self_kernel(q_ref, k_ref, v_ref, n_ref, stat_ref):
    rows = q_ref.shape[0]
    valid = lax.broadcasted_iota(jnp.int32, (rows, rows), 1) <= lax.broadcasted_iota(
        jnp.int32, (rows, rows), 0
    )
    lane = lax.broadcasted_iota(jnp.int32, (rows, STAT), 1)
    stat = jnp.zeros((rows, STAT), jnp.float32)
    keys = k_ref[...]
    values = v_ref[...]
    for h in range(2):
        top, total, summed = head_partial(q_ref[:, h * HD:(h + 1) * HD], keys, values, valid)
        n_ref[:, h * HD:(h + 1) * HD] = summed
        stat = jnp.where(lane == 8 * h, top, stat)
        stat = jnp.where(lane == 8 * h + 3, total, stat)
    stat_ref[...] = stat


def self_attention(q, keys, values):
    rows = q.shape[0]
    return pl.pallas_call(
        self_kernel,
        out_shape=(
            jax.ShapeDtypeStruct((rows, 2 * HD), jnp.float32),
            jax.ShapeDtypeStruct((rows, STAT), jnp.float32),
        ),
        compiler_params=pltpu.CompilerParams(vmem_limit_bytes=48 * 1024 * 1024),
        cost_estimate=pl.CostEstimate(
            flops=2 * 2 * 2 * rows * rows * HD,
            transcendentals=2 * rows * rows,
            bytes_accessed=rows * 2 * HD * 2 + 2 * rows * HD * 2 + rows * (2 * HD + STAT) * 4,
        ),
    )(q, keys, values)


def combine_kernel(has_ref, *refs):
    slot_refs = refs[:P_DEV]
    sum_ref, stat_ref, out_ref = refs[P_DEV:]
    rows = out_ref.shape[0]
    lane = lax.broadcasted_iota(jnp.int32, (rows, STAT), 1)
    near_stat = stat_ref[...]
    stats = [slot_refs[d][:, 2 * HD:].astype(jnp.float32) for d in range(P_DEV)]

    def pick(stat, first, count):
        chosen = (lane >= first) & (lane < first + count)
        return jnp.sum(jnp.where(chosen, stat, 0.0), axis=1, keepdims=True)

    for h in range(2):
        tops = [pick(stats[d], 8 * h, 3) for d in range(P_DEV)]
        totals = [pick(stats[d], 8 * h + 3, 3) for d in range(P_DEV)]
        far_top = jnp.full((rows, 1), LOWEST, jnp.float32)
        for d in range(P_DEV):
            far_top = jnp.maximum(far_top, jnp.where(has_ref[d] == 1, tops[d], LOWEST))
        far_total = jnp.zeros((rows, 1), jnp.float32)
        far_sum = jnp.zeros((rows, HD), jnp.float32)
        for d in range(P_DEV):
            live = has_ref[d] == 1
            weight = jnp.where(live, totals[d] * jnp.exp(tops[d] - far_top), 0.0)
            far_total = far_total + weight
            block = slot_refs[d][:, h * HD:(h + 1) * HD].astype(jnp.float32)
            far_sum = far_sum + jnp.where(live, weight * block, 0.0)
        near_top = pick(near_stat, 8 * h, 1)
        near_total = pick(near_stat, 8 * h + 3, 1)
        final_top = jnp.maximum(far_top, near_top)
        far_scale = jnp.exp(far_top - final_top)
        near_scale = jnp.exp(near_top - final_top)
        near_sum = sum_ref[:, h * HD:(h + 1) * HD]
        out_ref[:, h * HD:(h + 1) * HD] = (
            (far_sum * far_scale + near_sum * near_scale)
            / (far_total * far_scale + near_total * near_scale)
        ).astype(out_ref.dtype)


def combine(has, slots, self_sum, self_stat):
    rows = slots[0].shape[0]
    tile = 128
    slot_spec = pl.BlockSpec((tile, 2 * HD + STAT), lambda i, t: (i, 0))
    grid_spec = pltpu.PrefetchScalarGridSpec(
        num_scalar_prefetch=1,
        grid=(rows // tile,),
        in_specs=[slot_spec] * P_DEV
        + [
            pl.BlockSpec((tile, 2 * HD), lambda i, t: (i, 0)),
            pl.BlockSpec((tile, STAT), lambda i, t: (i, 0)),
        ],
        out_specs=pl.BlockSpec((tile, 2 * HD), lambda i, t: (i, 0)),
    )
    return pl.pallas_call(
        combine_kernel,
        grid_spec=grid_spec,
        out_shape=jax.ShapeDtypeStruct((rows, 2 * HD), jnp.bfloat16),
        compiler_params=pltpu.CompilerParams(dimension_semantics=("arbitrary",)),
        cost_estimate=pl.CostEstimate(
            flops=rows * 2 * HD * 3 * P_DEV,
            transcendentals=rows * 2 * P_DEV,
            bytes_accessed=P_DEV * rows * (2 * HD + STAT) * 2 + rows * (2 * HD + STAT) * 4 + rows * 2 * HD * 2,
        ),
    )(has, *slots, self_sum, self_stat)


def finish_rows(
    proj_sum,
    tok_float,
    tok_norm,
    extra_input,
    attn_gain,
    laurel_left,
    laurel_right,
    laurel_gain,
    layer_gate,
    layer_proj,
    layer_gain,
):
    laurel_low = jnp.dot(tok_norm, laurel_left, preferred_element_type=jnp.float32).astype(
        jnp.bfloat16
    )
    laurel_out = tok_norm.astype(jnp.float32) + normed(
        jnp.dot(laurel_low, laurel_right, preferred_element_type=jnp.float32),
        laurel_gain.astype(jnp.float32),
    )
    mixture = (tok_float + normed(proj_sum, attn_gain.astype(jnp.float32)) + laurel_out) * (
        1.0 / math.sqrt(2.0)
    )
    gate_act = jnp.dot(mixture.astype(jnp.bfloat16), layer_gate, preferred_element_type=jnp.float32)
    gate_out = (jax.nn.gelu(gate_act, approximate=True) * extra_input.astype(jnp.float32)).astype(
        jnp.bfloat16
    )
    return (
        mixture
        + normed(
            jnp.dot(gate_out, layer_proj, preferred_element_type=jnp.float32),
            layer_gain.astype(jnp.float32),
        )
    ).astype(jnp.bfloat16)


def schedule_table(distances, lengths, kv_head):
    ids = jnp.arange(P_DEV, dtype=jnp.int32)
    before = (distances[None, :] < distances[:, None]) | (
        (distances[None, :] == distances[:, None]) & (ids[None, :] < ids[:, None])
    )
    rank = jnp.sum(before.astype(jnp.int32), axis=1)
    chosen = rank[:, None] == ids[None, :]
    order = jnp.sum(jnp.where(chosen, ids[:, None], 0), axis=0)
    slot = jnp.sum(jnp.where(chosen, distances[:, None], 0), axis=0)
    length = jnp.sum(jnp.where(chosen, lengths[:, None], 0), axis=0)
    minus = jnp.full((1,), -1, jnp.int32)
    first = (slot != jnp.concatenate([minus, slot[:-1]])).astype(jnp.int32)
    last = (slot != jnp.concatenate([slot[1:], minus])).astype(jnp.int32)
    kv_row = jnp.full((P_DEV,), kv_head, jnp.int32)
    return jnp.concatenate([order, slot, length, first, last, kv_row]).astype(jnp.int32)


def body(
    tokens,
    layer_input,
    input_gain,
    q_weight,
    k_weight,
    v_weight,
    q_gain,
    k_gain,
    o_weight,
    attn_gain,
    laurel_left,
    laurel_right,
    laurel_gain,
    layer_gate,
    layer_proj,
    layer_gain,
    piece_keys,
    piece_values,
    piece_owner,
    piece_len,
    cache_keys,
    cache_values,
    cache_len,
):
    req_count = lax.axis_size("req")
    tp_count = lax.axis_size("tp")
    req_index = lax.axis_index("req")
    tp_index = lax.axis_index("tp")
    local_heads = H // tp_count
    kv_head = tp_index * local_heads // (H // KVH)
    full_o_weight = lax.all_gather(o_weight, "tp", axis=0, tiled=True)
    tok_float = tokens.astype(jnp.float32)
    tok_norm = normed(tok_float, input_gain.astype(jnp.float32)).astype(jnp.bfloat16)
    queries = jnp.dot(tok_norm, q_weight, preferred_element_type=jnp.float32).reshape(
        ROWS, local_heads, HD
    )
    queries = (
        normed(queries, q_gain.astype(jnp.float32))
        .astype(jnp.bfloat16)
        .reshape(ROWS, local_heads * HD)
    )
    key_cols = lax.dynamic_slice_in_dim(k_weight, kv_head * HD, HD, 1)
    value_cols = lax.dynamic_slice_in_dim(v_weight, kv_head * HD, HD, 1)
    new_keys = normed(
        jnp.dot(tok_norm, key_cols, preferred_element_type=jnp.float32), k_gain.astype(jnp.float32)
    ).astype(jnp.bfloat16)
    new_values = normed(
        jnp.dot(tok_norm, value_cols, preferred_element_type=jnp.float32), 1.0
    ).astype(jnp.bfloat16)
    own_block = queries[:CH]
    windows = [own_block] + [passed_along(own_block, "req", d) for d in range(1, P_DEV)]
    self_sum, self_stat = self_attention(own_block, new_keys[:CH], new_values[:CH])

    owners = lax.dynamic_slice_in_dim(piece_owner, req_index * P_DEV, P_DEV)
    lengths = lax.dynamic_slice_in_dim(piece_len, req_index * P_DEV, P_DEV)
    distances = (req_index - owners + req_count) % req_count
    table = schedule_table(distances, lengths, kv_head)
    packed = piece_attention(table, windows, piece_keys, piece_values, self_stat)
    slots = [packed[0]] + [passed_along(packed[d], "req", -d) for d in range(1, P_DEV)]

    block_ids = (req_index + jnp.arange(P_DEV, dtype=jnp.int32)) % req_count
    block_owners = jnp.take(piece_owner.reshape(req_count, P_DEV), block_ids, axis=0)
    has = jnp.any(block_owners == req_index, axis=1).astype(jnp.int32)
    span_att = combine(has, slots, self_sum, self_stat)
    decode_q = queries[CH:].reshape(DEC_DEV, local_heads, HD)
    cache_key = lax.dynamic_slice_in_dim(cache_keys, kv_head * HD, HD, 2)
    cache_value = lax.dynamic_slice_in_dim(cache_values, kv_head * HD, HD, 2)
    cache_scores = (
        jnp.einsum("thd,tjd->thj", decode_q, cache_key, preferred_element_type=jnp.float32)
        * SCORE_SCALE
    )
    cache_valid = (
        lax.broadcasted_iota(jnp.int32, (DEC_DEV, 1, DCACHE), 2) < cache_len[:, None, None]
    )
    cache_scores = jnp.where(cache_valid, cache_scores, LOWEST)
    own_scores = (
        jnp.einsum("thd,td->th", decode_q, new_keys[CH:], preferred_element_type=jnp.float32)
        * SCORE_SCALE
    )
    decode_top = jnp.maximum(jnp.max(cache_scores, axis=-1), own_scores)
    cache_exp = jnp.exp(cache_scores - decode_top[:, :, None])
    own_exp = jnp.exp(own_scores - decode_top)
    decode_total = jnp.sum(cache_exp, axis=-1) + own_exp
    decode_sum = (
        jnp.einsum(
            "thj,tjd->thd",
            cache_exp.astype(jnp.bfloat16),
            cache_value,
            preferred_element_type=jnp.float32,
        )
        + rounded(own_exp).astype(jnp.float32)[:, :, None]
        * new_values[CH:].astype(jnp.float32)[:, None, :]
    )
    decode_att = (
        (decode_sum / decode_total[:, :, None])
        .reshape(DEC_DEV, local_heads * HD)
        .astype(jnp.bfloat16)
    )
    attended = jnp.concatenate([span_att, decode_att], axis=0)
    part = CH // tp_count

    def rows_of(x, owner):
        return jnp.concatenate(
            [lax.dynamic_slice_in_dim(x, owner * part, part, 0), x[CH:]], axis=0
        )

    proj_sum = jnp.dot(rows_of(attended, tp_index), o_weight, preferred_element_type=jnp.float32)
    for shift in range(1, tp_count):
        target = (tp_index + shift) % tp_count
        got_rows = passed_along(rows_of(attended, target), "tp", shift)
        got_weight = passed_along(o_weight, "tp", shift)
        proj_sum = proj_sum + jnp.dot(got_rows, got_weight, preferred_element_type=jnp.float32)
    mine = finish_rows(
        proj_sum,
        rows_of(tok_float, tp_index),
        rows_of(tok_norm, tp_index),
        rows_of(layer_input, tp_index),
        attn_gain,
        laurel_left,
        laurel_right,
        laurel_gain,
        layer_gate,
        layer_proj,
        layer_gain,
    )
    pieces = [(tp_index, mine)] + [
        ((tp_index - shift + tp_count) % tp_count, passed_along(mine, "tp", shift))
        for shift in range(1, tp_count)
    ]
    result = jnp.zeros((ROWS, mine.shape[1]), mine.dtype)
    decode_rows = jnp.zeros((ROWS - CH, mine.shape[1]), mine.dtype)
    for owner, got in pieces:
        result = lax.dynamic_update_slice_in_dim(result, got[:part], owner * part, 0)
        decode_rows = jnp.where(owner == 0, got[part:], decode_rows)
    return lax.dynamic_update_slice_in_dim(result, decode_rows, CH, 0)


def solution(mesh):
    placed = (
        P("req", None),
        P("req", None),
        P(),
        P(None, "tp"),
        P(),
        P(),
        P(),
        P(),
        P("tp", None),
        P(),
        P(),
        P(),
        P(),
        P(),
        P(),
        P(),
        P("req", None, None),
        P("req", None, None),
        P(),
        P(),
        P("req", None, None),
        P("req", None, None),
        P("req"),
    )
    return jax.shard_map(
        body, mesh=mesh, in_specs=placed, out_specs=P("req", None), check_vma=False
    )
```

```python
import functools
import math

import jax
import jax.numpy as jnp
from jax import lax
from jax.experimental import pallas as pl
from jax.experimental.pallas import tpu as pltpu
from jax.sharding import PartitionSpec as P

H = 8
KVH = 2
HD = 256
CH = 512
DEC_DEV = 4
P_DEV = 8
PIECE = 1024
DCACHE = 512
ROWS = 516
STAT = 128
CHUNK = 256


LOWEST = -1e30
SCORE_SCALE = 1.0 / math.sqrt(HD)


def passed_along(x, axis, by):
    length = lax.axis_size(axis)
    return lax.ppermute(x, axis, [(i, (i + by) % length) for i in range(length)])


def rounded(x):
    return lax.optimization_barrier(x.astype(jnp.bfloat16))


def normed(x, scale_gain):
    return x * lax.rsqrt(jnp.mean(x * x, axis=-1, keepdims=True) + 1e-06) * scale_gain


def head_partial(q, keys, values, valid):
    scores = lax.dot_general(q, keys, (((1,), (1,)), ((), ())), preferred_element_type=jnp.float32)
    scores = jnp.where(valid, scores, LOWEST)
    top = jnp.max(scores, axis=1, keepdims=True)
    weights = jnp.exp((scores - top) * SCORE_SCALE)
    total = jnp.sum(weights, axis=1, keepdims=True)
    summed = jnp.dot(weights.astype(jnp.bfloat16), values, preferred_element_type=jnp.float32)
    return top * SCORE_SCALE, total, summed


def split3(x):
    hi = x.astype(jnp.bfloat16).astype(jnp.float32)
    rest = x - hi
    mid = rest.astype(jnp.bfloat16).astype(jnp.float32)
    lo = rest - mid
    return hi, mid, lo


def piece_kernel(tab_ref, *refs):
    q_refs = refs[:P_DEV]
    k_ref, v_ref = refs[P_DEV:P_DEV + 2]
    out_refs = refs[P_DEV + 3:2 * P_DEV + 3]
    qbuf, fin, acc_m, acc_l, acc_n, sbuf, lbuf, nbuf = refs[2 * P_DEV + 3:]
    step = pl.program_id(0)
    slot = tab_ref[P_DEV + step]
    length = tab_ref[2 * P_DEV + step]
    first = tab_ref[3 * P_DEV + step]
    last = tab_ref[4 * P_DEV + step]
    for k in range(P_DEV):

        @pl.when(slot == k)
        def _(k=k):
            qbuf[...] = q_refs[k][...]

    rows = qbuf.shape[0]
    chunks = (length + CHUNK - 1) // CHUNK
    for h in range(2):
        q = qbuf[:, h * HD:(h + 1) * HD]

        def score_chunk(c, top, q=q):
            start = pl.multiple_of(c * CHUNK, CHUNK)
            scores = lax.dot_general(
                q, k_ref[0, pl.ds(start, CHUNK), :], (((1,), (1,)), ((), ())),
                preferred_element_type=jnp.float32,
            )
            valid = lax.broadcasted_iota(jnp.int32, (rows, CHUNK), 1) + start < length
            scores = jnp.where(valid, scores, LOWEST)
            sbuf[c] = scores
            return jnp.maximum(top, jnp.max(scores, axis=1, keepdims=True))

        top = lax.fori_loop(0, chunks, score_chunk, jnp.full((rows, 1), LOWEST, jnp.float32))
        lbuf[...] = jnp.zeros_like(lbuf)
        nbuf[...] = jnp.zeros_like(nbuf)

        @pl.loop(0, chunks)
        def _(c, top=top):
            start = pl.multiple_of(c * CHUNK, CHUNK)
            weights = jnp.exp((sbuf[c] - top) * SCORE_SCALE)
            lbuf[...] += jnp.sum(weights, axis=1, keepdims=True)
            nbuf[...] += jnp.dot(
                weights.astype(jnp.bfloat16), v_ref[0, pl.ds(start, CHUNK), :],
                preferred_element_type=jnp.float32,
            )

        top = top * SCORE_SCALE

        @pl.when(first == 1)
        def _(h=h, top=top):
            acc_m[h] = top
            acc_l[h] = lbuf[...]
            acc_n[h] = nbuf[...]

        @pl.when(first == 0)
        def _(h=h, top=top):
            old = acc_m[h]
            new = jnp.maximum(old, top)
            keep = jnp.exp(old - new)
            add = jnp.exp(top - new)
            acc_l[h] = acc_l[h] * keep + lbuf[...] * add
            acc_n[h] = acc_n[h] * keep + nbuf[...] * add
            acc_m[h] = new

    @pl.when(last == 1)
    def _():
        lane = lax.broadcasted_iota(jnp.int32, (rows, STAT), 1)
        stat = jnp.zeros((rows, STAT), jnp.float32)
        for h in range(2):
            total = acc_l[h]
            fin[:, h * HD:(h + 1) * HD] = (acc_n[h] / total).astype(jnp.bfloat16)
            for i, part in enumerate(split3(acc_m[h]) + split3(total)):
                stat = jnp.where(lane == 8 * h + i, part, stat)
        fin[:, 2 * HD:] = stat.astype(jnp.bfloat16)
        for k in range(P_DEV):

            @pl.when(slot == k)
            def _(k=k):
                out_refs[k][...] = fin[...]


def piece_attention(table, windows, piece_keys, piece_values, after):
    rows = windows[0].shape[0]
    pieces = piece_keys.shape[0]
    q_spec = pl.BlockSpec((rows, 2 * HD), lambda s, t: (0, 0))
    kv_spec = pl.BlockSpec((1, PIECE, HD), lambda s, t: (t[s], 0, t[5 * P_DEV]))
    out_spec = pl.BlockSpec((rows, 2 * HD + STAT), lambda s, t: (0, 0))
    grid_spec = pltpu.PrefetchScalarGridSpec(
        num_scalar_prefetch=1,
        grid=(pieces,),
        in_specs=[q_spec] * P_DEV + [kv_spec, kv_spec, pl.BlockSpec(memory_space=pl.ANY)],
        out_specs=[out_spec] * P_DEV,
        scratch_shapes=[
            pltpu.VMEM((rows, 2 * HD), jnp.bfloat16),
            pltpu.VMEM((rows, 2 * HD + STAT), jnp.bfloat16),
            pltpu.VMEM((2, rows, 1), jnp.float32),
            pltpu.VMEM((2, rows, 1), jnp.float32),
            pltpu.VMEM((2, rows, HD), jnp.float32),
            pltpu.VMEM((PIECE // CHUNK, rows, CHUNK), jnp.float32),
            pltpu.VMEM((rows, 1), jnp.float32),
            pltpu.VMEM((rows, HD), jnp.float32),
        ],
    )
    flops = pieces * 2 * 2 * 2 * rows * PIECE * HD
    return pl.pallas_call(
        piece_kernel,
        grid_spec=grid_spec,
        out_shape=[jax.ShapeDtypeStruct((rows, 2 * HD + STAT), jnp.bfloat16)] * P_DEV,
        compiler_params=pltpu.CompilerParams(
            dimension_semantics=("arbitrary",), vmem_limit_bytes=56 * 1024 * 1024
        ),
        cost_estimate=pl.CostEstimate(
            flops=flops,
            transcendentals=pieces * 2 * rows * PIECE,
            bytes_accessed=pieces * 2 * PIECE * HD * 2 + P_DEV * rows * 2 * HD * 2 * 2,
        ),
    )(table, *windows, piece_keys, piece_values, after)


def self_kernel(q_ref, k_ref, v_ref, n_ref, stat_ref):
    rows = q_ref.shape[0]
    valid = lax.broadcasted_iota(jnp.int32, (rows, rows), 1) <= lax.broadcasted_iota(
        jnp.int32, (rows, rows), 0
    )
    lane = lax.broadcasted_iota(jnp.int32, (rows, STAT), 1)
    stat = jnp.zeros((rows, STAT), jnp.float32)
    keys = k_ref[...]
    values = v_ref[...]
    for h in range(2):
        top, total, summed = head_partial(q_ref[:, h * HD:(h + 1) * HD], keys, values, valid)
        n_ref[:, h * HD:(h + 1) * HD] = summed
        stat = jnp.where(lane == 8 * h, top, stat)
        stat = jnp.where(lane == 8 * h + 3, total, stat)
    stat_ref[...] = stat


def self_attention(q, keys, values):
    rows = q.shape[0]
    return pl.pallas_call(
        self_kernel,
        out_shape=(
            jax.ShapeDtypeStruct((rows, 2 * HD), jnp.float32),
            jax.ShapeDtypeStruct((rows, STAT), jnp.float32),
        ),
        compiler_params=pltpu.CompilerParams(vmem_limit_bytes=48 * 1024 * 1024),
        cost_estimate=pl.CostEstimate(
            flops=2 * 2 * 2 * rows * rows * HD,
            transcendentals=2 * rows * rows,
            bytes_accessed=rows * 2 * HD * 2 + 2 * rows * HD * 2 + rows * (2 * HD + STAT) * 4,
        ),
    )(q, keys, values)


def combine_kernel(has_ref, *refs):
    slot_refs = refs[:P_DEV]
    sum_ref, stat_ref, out_ref = refs[P_DEV:]
    rows = out_ref.shape[0]
    lane = lax.broadcasted_iota(jnp.int32, (rows, STAT), 1)
    near_stat = stat_ref[...]
    stats = [slot_refs[d][:, 2 * HD:].astype(jnp.float32) for d in range(P_DEV)]

    def pick(stat, first, count):
        chosen = (lane >= first) & (lane < first + count)
        return jnp.sum(jnp.where(chosen, stat, 0.0), axis=1, keepdims=True)

    for h in range(2):
        tops = [pick(stats[d], 8 * h, 3) for d in range(P_DEV)]
        totals = [pick(stats[d], 8 * h + 3, 3) for d in range(P_DEV)]
        far_top = jnp.full((rows, 1), LOWEST, jnp.float32)
        for d in range(P_DEV):
            far_top = jnp.maximum(far_top, jnp.where(has_ref[d] == 1, tops[d], LOWEST))
        far_total = jnp.zeros((rows, 1), jnp.float32)
        far_sum = jnp.zeros((rows, HD), jnp.float32)
        for d in range(P_DEV):
            live = has_ref[d] == 1
            weight = jnp.where(live, totals[d] * jnp.exp(tops[d] - far_top), 0.0)
            far_total = far_total + weight
            block = slot_refs[d][:, h * HD:(h + 1) * HD].astype(jnp.float32)
            far_sum = far_sum + jnp.where(live, weight * block, 0.0)
        near_top = pick(near_stat, 8 * h, 1)
        near_total = pick(near_stat, 8 * h + 3, 1)
        final_top = jnp.maximum(far_top, near_top)
        far_scale = jnp.exp(far_top - final_top)
        near_scale = jnp.exp(near_top - final_top)
        near_sum = sum_ref[:, h * HD:(h + 1) * HD]
        out_ref[:, h * HD:(h + 1) * HD] = (
            (far_sum * far_scale + near_sum * near_scale)
            / (far_total * far_scale + near_total * near_scale)
        ).astype(out_ref.dtype)


def combine(has, slots, self_sum, self_stat):
    rows = slots[0].shape[0]
    tile = 128
    slot_spec = pl.BlockSpec((tile, 2 * HD + STAT), lambda i, t: (i, 0))
    grid_spec = pltpu.PrefetchScalarGridSpec(
        num_scalar_prefetch=1,
        grid=(rows // tile,),
        in_specs=[slot_spec] * P_DEV
        + [
            pl.BlockSpec((tile, 2 * HD), lambda i, t: (i, 0)),
            pl.BlockSpec((tile, STAT), lambda i, t: (i, 0)),
        ],
        out_specs=pl.BlockSpec((tile, 2 * HD), lambda i, t: (i, 0)),
    )
    return pl.pallas_call(
        combine_kernel,
        grid_spec=grid_spec,
        out_shape=jax.ShapeDtypeStruct((rows, 2 * HD), jnp.bfloat16),
        compiler_params=pltpu.CompilerParams(dimension_semantics=("arbitrary",)),
        cost_estimate=pl.CostEstimate(
            flops=rows * 2 * HD * 3 * P_DEV,
            transcendentals=rows * 2 * P_DEV,
            bytes_accessed=P_DEV * rows * (2 * HD + STAT) * 2 + rows * (2 * HD + STAT) * 4 + rows * 2 * HD * 2,
        ),
    )(has, *slots, self_sum, self_stat)


def finish_rows(
    proj_sum,
    tok_float,
    tok_norm,
    extra_input,
    attn_gain,
    laurel_left,
    laurel_right,
    laurel_gain,
    layer_gate,
    layer_proj,
    layer_gain,
):
    laurel_low = jnp.dot(tok_norm, laurel_left, preferred_element_type=jnp.float32).astype(
        jnp.bfloat16
    )
    laurel_out = tok_norm.astype(jnp.float32) + normed(
        jnp.dot(laurel_low, laurel_right, preferred_element_type=jnp.float32),
        laurel_gain.astype(jnp.float32),
    )
    mixture = (tok_float + normed(proj_sum, attn_gain.astype(jnp.float32)) + laurel_out) * (
        1.0 / math.sqrt(2.0)
    )
    gate_act = jnp.dot(mixture.astype(jnp.bfloat16), layer_gate, preferred_element_type=jnp.float32)
    gate_out = (jax.nn.gelu(gate_act, approximate=True) * extra_input.astype(jnp.float32)).astype(
        jnp.bfloat16
    )
    return (
        mixture
        + normed(
            jnp.dot(gate_out, layer_proj, preferred_element_type=jnp.float32),
            layer_gain.astype(jnp.float32),
        )
    ).astype(jnp.bfloat16)


def schedule_table(distances, lengths, kv_head):
    ids = jnp.arange(P_DEV, dtype=jnp.int32)
    before = (distances[None, :] < distances[:, None]) | (
        (distances[None, :] == distances[:, None]) & (ids[None, :] < ids[:, None])
    )
    rank = jnp.sum(before.astype(jnp.int32), axis=1)
    chosen = rank[:, None] == ids[None, :]
    order = jnp.sum(jnp.where(chosen, ids[:, None], 0), axis=0)
    slot = jnp.sum(jnp.where(chosen, distances[:, None], 0), axis=0)
    length = jnp.sum(jnp.where(chosen, lengths[:, None], 0), axis=0)
    minus = jnp.full((1,), -1, jnp.int32)
    first = (slot != jnp.concatenate([minus, slot[:-1]])).astype(jnp.int32)
    last = (slot != jnp.concatenate([slot[1:], minus])).astype(jnp.int32)
    kv_row = jnp.full((P_DEV,), kv_head, jnp.int32)
    return jnp.concatenate([order, slot, length, first, last, kv_row]).astype(jnp.int32)


def body(
    tokens,
    layer_input,
    input_gain,
    q_weight,
    k_weight,
    v_weight,
    q_gain,
    k_gain,
    o_weight,
    attn_gain,
    laurel_left,
    laurel_right,
    laurel_gain,
    layer_gate,
    layer_proj,
    layer_gain,
    piece_keys,
    piece_values,
    piece_owner,
    piece_len,
    cache_keys,
    cache_values,
    cache_len,
):
    req_count = lax.axis_size("req")
    tp_count = lax.axis_size("tp")
    req_index = lax.axis_index("req")
    tp_index = lax.axis_index("tp")
    local_heads = H // tp_count
    kv_head = tp_index * local_heads // (H // KVH)
    full_o_weight = lax.all_gather(o_weight, "tp", axis=0, tiled=True)
    tok_float = tokens.astype(jnp.float32)
    tok_norm = normed(tok_float, input_gain.astype(jnp.float32)).astype(jnp.bfloat16)
    queries = jnp.dot(tok_norm, q_weight, preferred_element_type=jnp.float32).reshape(
        ROWS, local_heads, HD
    )
    queries = (
        normed(queries, q_gain.astype(jnp.float32))
        .astype(jnp.bfloat16)
        .reshape(ROWS, local_heads * HD)
    )
    key_cols = lax.dynamic_slice_in_dim(k_weight, kv_head * HD, HD, 1)
    value_cols = lax.dynamic_slice_in_dim(v_weight, kv_head * HD, HD, 1)
    new_keys = normed(
        jnp.dot(tok_norm, key_cols, preferred_element_type=jnp.float32), k_gain.astype(jnp.float32)
    ).astype(jnp.bfloat16)
    new_values = normed(
        jnp.dot(tok_norm, value_cols, preferred_element_type=jnp.float32), 1.0
    ).astype(jnp.bfloat16)
    own_block = queries[:CH]
    windows = [own_block] + [passed_along(own_block, "req", d) for d in range(1, P_DEV)]
    self_sum, self_stat = self_attention(own_block, new_keys[:CH], new_values[:CH])

    owners = lax.dynamic_slice_in_dim(piece_owner, req_index * P_DEV, P_DEV)
    lengths = lax.dynamic_slice_in_dim(piece_len, req_index * P_DEV, P_DEV)
    distances = (req_index - owners + req_count) % req_count
    table = schedule_table(distances, lengths, kv_head)
    packed = piece_attention(table, windows, piece_keys, piece_values, self_stat)
    slots = [packed[0]] + [passed_along(packed[d], "req", -d) for d in range(1, P_DEV)]

    block_ids = (req_index + jnp.arange(P_DEV, dtype=jnp.int32)) % req_count
    block_owners = jnp.take(piece_owner.reshape(req_count, P_DEV), block_ids, axis=0)
    has = jnp.any(block_owners == req_index, axis=1).astype(jnp.int32)
    span_att = combine(has, slots, self_sum, self_stat)
    decode_q = queries[CH:].reshape(DEC_DEV, local_heads, HD)
    cache_key = lax.dynamic_slice_in_dim(cache_keys, kv_head * HD, HD, 2)
    cache_value = lax.dynamic_slice_in_dim(cache_values, kv_head * HD, HD, 2)
    cache_scores = (
        jnp.einsum("thd,tjd->thj", decode_q, cache_key, preferred_element_type=jnp.float32)
        * SCORE_SCALE
    )
    cache_valid = (
        lax.broadcasted_iota(jnp.int32, (DEC_DEV, 1, DCACHE), 2) < cache_len[:, None, None]
    )
    cache_scores = jnp.where(cache_valid, cache_scores, LOWEST)
    own_scores = (
        jnp.einsum("thd,td->th", decode_q, new_keys[CH:], preferred_element_type=jnp.float32)
        * SCORE_SCALE
    )
    decode_top = jnp.maximum(jnp.max(cache_scores, axis=-1), own_scores)
    cache_exp = jnp.exp(cache_scores - decode_top[:, :, None])
    own_exp = jnp.exp(own_scores - decode_top)
    decode_total = jnp.sum(cache_exp, axis=-1) + own_exp
    decode_sum = (
        jnp.einsum(
            "thj,tjd->thd",
            cache_exp.astype(jnp.bfloat16),
            cache_value,
            preferred_element_type=jnp.float32,
        )
        + rounded(own_exp).astype(jnp.float32)[:, :, None]
        * new_values[CH:].astype(jnp.float32)[:, None, :]
    )
    decode_att = (
        (decode_sum / decode_total[:, :, None])
        .reshape(DEC_DEV, local_heads * HD)
        .astype(jnp.bfloat16)
    )
    attended = jnp.concatenate([span_att, decode_att], axis=0)
    part = CH // tp_count

    def rows_of(x, owner):
        return jnp.concatenate(
            [lax.dynamic_slice_in_dim(x, owner * part, part, 0), x[CH:]], axis=0
        )

    proj_sum = jnp.dot(rows_of(attended, tp_index), o_weight, preferred_element_type=jnp.float32)
    for shift in range(1, tp_count):
        target = (tp_index + shift) % tp_count
        got_rows = passed_along(rows_of(attended, target), "tp", shift)
        got_weight = passed_along(o_weight, "tp", shift)
        proj_sum = proj_sum + jnp.dot(got_rows, got_weight, preferred_element_type=jnp.float32)
    mine = finish_rows(
        proj_sum,
        rows_of(tok_float, tp_index),
        rows_of(tok_norm, tp_index),
        rows_of(layer_input, tp_index),
        attn_gain,
        laurel_left,
        laurel_right,
        laurel_gain,
        layer_gate,
        layer_proj,
        layer_gain,
    )
    gathered = [mine] + [passed_along(mine, "tp", shift) for shift in range(1, tp_count)]

    def assemble(me):
        def build(*got):
            blocks = [got[(me - owner) % tp_count][:part] for owner in range(tp_count)]
            return jnp.concatenate(blocks + [got[me][part:]], axis=0)

        return build

    return lax.switch(tp_index, [assemble(me) for me in range(tp_count)], *gathered)


def solution(mesh):
    placed = (
        P("req", None),
        P("req", None),
        P(),
        P(None, "tp"),
        P(),
        P(),
        P(),
        P(),
        P("tp", None),
        P(),
        P(),
        P(),
        P(),
        P(),
        P(),
        P(),
        P("req", None, None),
        P("req", None, None),
        P(),
        P(),
        P("req", None, None),
        P("req", None, None),
        P("req"),
    )
    return jax.shard_map(
        body, mesh=mesh, in_specs=placed, out_specs=P("req", None), check_vma=False
    )
```

```python
import functools
import math

import jax
import jax.numpy as jnp
from jax import lax
from jax.experimental import pallas as pl
from jax.experimental.pallas import tpu as pltpu
from jax.sharding import PartitionSpec as P

H = 8
KVH = 2
HD = 256
CH = 512
DEC_DEV = 4
P_DEV = 8
PIECE = 1024
DCACHE = 512
ROWS = 516
STAT = 128
CHUNK = 256


LOWEST = -1e30
SCORE_SCALE = 1.0 / math.sqrt(HD)


def passed_along(x, axis, by):
    length = lax.axis_size(axis)
    return lax.ppermute(x, axis, [(i, (i + by) % length) for i in range(length)])


def rounded(x):
    return lax.optimization_barrier(x.astype(jnp.bfloat16))


def normed(x, scale_gain):
    return x * lax.rsqrt(jnp.mean(x * x, axis=-1, keepdims=True) + 1e-06) * scale_gain


def head_partial(q, keys, values, valid):
    scores = lax.dot_general(q, keys, (((1,), (1,)), ((), ())), preferred_element_type=jnp.float32)
    scores = jnp.where(valid, scores, LOWEST)
    top = jnp.max(scores, axis=1, keepdims=True)
    weights = jnp.exp((scores - top) * SCORE_SCALE)
    total = jnp.sum(weights, axis=1, keepdims=True)
    summed = jnp.dot(weights.astype(jnp.bfloat16), values, preferred_element_type=jnp.float32)
    return top * SCORE_SCALE, total, summed


def split3(x):
    hi = x.astype(jnp.bfloat16).astype(jnp.float32)
    rest = x - hi
    mid = rest.astype(jnp.bfloat16).astype(jnp.float32)
    lo = rest - mid
    return hi, mid, lo


def piece_kernel(slots, tab_ref, *refs):
    q_refs = refs[:slots]
    k_ref, v_ref = refs[slots:slots + 2]
    out_refs = refs[slots + 3:2 * slots + 3]
    scratch = refs[2 * slots + 3:]
    step = pl.program_id(0)

    @pl.when(tab_ref[5 * P_DEV + step] == 1)
    def _():
        piece_step(step, tab_ref, q_refs, k_ref, v_ref, out_refs, *scratch)


def piece_step(step, tab_ref, q_refs, k_ref, v_ref, out_refs, qbuf, fin, acc_m, acc_l, acc_n, sbuf, lbuf, nbuf):
    slots = len(q_refs)
    slot = tab_ref[P_DEV + step]
    length = tab_ref[2 * P_DEV + step]
    first = tab_ref[3 * P_DEV + step]
    last = tab_ref[4 * P_DEV + step]
    for k in range(slots):

        @pl.when(slot == k)
        def _(k=k):
            qbuf[...] = q_refs[k][...]

    rows = qbuf.shape[0]
    chunks = (length + CHUNK - 1) // CHUNK
    for h in range(2):
        q = qbuf[:, h * HD:(h + 1) * HD]

        def score_chunk(c, top, q=q):
            start = pl.multiple_of(c * CHUNK, CHUNK)
            scores = lax.dot_general(
                q, k_ref[0, pl.ds(start, CHUNK), :], (((1,), (1,)), ((), ())),
                preferred_element_type=jnp.float32,
            )
            valid = lax.broadcasted_iota(jnp.int32, (rows, CHUNK), 1) + start < length
            scores = jnp.where(valid, scores, LOWEST)
            sbuf[c] = scores
            return jnp.maximum(top, jnp.max(scores, axis=1, keepdims=True))

        top = lax.fori_loop(0, chunks, score_chunk, jnp.full((rows, 1), LOWEST, jnp.float32))
        lbuf[...] = jnp.zeros_like(lbuf)
        nbuf[...] = jnp.zeros_like(nbuf)

        @pl.loop(0, chunks)
        def _(c, top=top):
            start = pl.multiple_of(c * CHUNK, CHUNK)
            weights = jnp.exp((sbuf[c] - top) * SCORE_SCALE)
            lbuf[...] += jnp.sum(weights, axis=1, keepdims=True)
            nbuf[...] += jnp.dot(
                weights.astype(jnp.bfloat16), v_ref[0, pl.ds(start, CHUNK), :],
                preferred_element_type=jnp.float32,
            )

        top = top * SCORE_SCALE

        @pl.when(first == 1)
        def _(h=h, top=top):
            acc_m[h] = top
            acc_l[h] = lbuf[...]
            acc_n[h] = nbuf[...]

        @pl.when(first == 0)
        def _(h=h, top=top):
            old = acc_m[h]
            new = jnp.maximum(old, top)
            keep = jnp.exp(old - new)
            add = jnp.exp(top - new)
            acc_l[h] = acc_l[h] * keep + lbuf[...] * add
            acc_n[h] = acc_n[h] * keep + nbuf[...] * add
            acc_m[h] = new

    @pl.when(last == 1)
    def _():
        lane = lax.broadcasted_iota(jnp.int32, (rows, STAT), 1)
        stat = jnp.zeros((rows, STAT), jnp.float32)
        for h in range(2):
            total = acc_l[h]
            fin[:, h * HD:(h + 1) * HD] = (acc_n[h] / total).astype(jnp.bfloat16)
            for i, part in enumerate(split3(acc_m[h]) + split3(total)):
                stat = jnp.where(lane == 8 * h + i, part, stat)
        fin[:, 2 * HD:] = stat.astype(jnp.bfloat16)
        for k in range(slots):

            @pl.when(slot == k)
            def _(k=k):
                out_refs[k][...] = fin[...]


def piece_attention(table, windows, piece_keys, piece_values, after):
    rows = windows[0].shape[0]
    slots = len(windows)
    q_spec = pl.BlockSpec((rows, 2 * HD), lambda s, t: (0, 0))
    kv_spec = pl.BlockSpec((1, PIECE, HD), lambda s, t: (t[s], 0, t[6 * P_DEV]))
    out_spec = pl.BlockSpec((rows, 2 * HD + STAT), lambda s, t: (0, 0))
    grid_spec = pltpu.PrefetchScalarGridSpec(
        num_scalar_prefetch=1,
        grid=(P_DEV,),
        in_specs=[q_spec] * slots + [kv_spec, kv_spec, pl.BlockSpec(memory_space=pl.ANY)],
        out_specs=[out_spec] * slots,
        scratch_shapes=[
            pltpu.VMEM((rows, 2 * HD), jnp.bfloat16),
            pltpu.VMEM((rows, 2 * HD + STAT), jnp.bfloat16),
            pltpu.VMEM((2, rows, 1), jnp.float32),
            pltpu.VMEM((2, rows, 1), jnp.float32),
            pltpu.VMEM((2, rows, HD), jnp.float32),
            pltpu.VMEM((PIECE // CHUNK, rows, CHUNK), jnp.float32),
            pltpu.VMEM((rows, 1), jnp.float32),
            pltpu.VMEM((rows, HD), jnp.float32),
        ],
    )
    pieces = P_DEV // 2
    flops = pieces * 2 * 2 * 2 * rows * PIECE * HD
    return pl.pallas_call(
        functools.partial(piece_kernel, slots),
        grid_spec=grid_spec,
        out_shape=[jax.ShapeDtypeStruct((rows, 2 * HD + STAT), jnp.bfloat16)] * slots,
        compiler_params=pltpu.CompilerParams(
            dimension_semantics=("arbitrary",), vmem_limit_bytes=48 * 1024 * 1024
        ),
        cost_estimate=pl.CostEstimate(
            flops=flops,
            transcendentals=pieces * 2 * rows * PIECE,
            bytes_accessed=pieces * 2 * PIECE * HD * 2 + slots * rows * 2 * HD * 2 * 2,
        ),
    )(table, *windows, piece_keys, piece_values, after)


def self_kernel(q_ref, k_ref, v_ref, n_ref, stat_ref):
    rows = q_ref.shape[0]
    valid = lax.broadcasted_iota(jnp.int32, (rows, rows), 1) <= lax.broadcasted_iota(
        jnp.int32, (rows, rows), 0
    )
    lane = lax.broadcasted_iota(jnp.int32, (rows, STAT), 1)
    stat = jnp.zeros((rows, STAT), jnp.float32)
    keys = k_ref[...]
    values = v_ref[...]
    for h in range(2):
        top, total, summed = head_partial(q_ref[:, h * HD:(h + 1) * HD], keys, values, valid)
        n_ref[:, h * HD:(h + 1) * HD] = summed
        stat = jnp.where(lane == 8 * h, top, stat)
        stat = jnp.where(lane == 8 * h + 3, total, stat)
    stat_ref[...] = stat


def self_attention(q, keys, values):
    rows = q.shape[0]
    return pl.pallas_call(
        self_kernel,
        out_shape=(
            jax.ShapeDtypeStruct((rows, 2 * HD), jnp.float32),
            jax.ShapeDtypeStruct((rows, STAT), jnp.float32),
        ),
        compiler_params=pltpu.CompilerParams(vmem_limit_bytes=48 * 1024 * 1024),
        cost_estimate=pl.CostEstimate(
            flops=2 * 2 * 2 * rows * rows * HD,
            transcendentals=2 * rows * rows,
            bytes_accessed=rows * 2 * HD * 2 + 2 * rows * HD * 2 + rows * (2 * HD + STAT) * 4,
        ),
    )(q, keys, values)


def combine_kernel(has_ref, *refs):
    slot_refs = refs[:P_DEV]
    sum_ref, stat_ref, out_ref = refs[P_DEV:]
    rows = out_ref.shape[0]
    lane = lax.broadcasted_iota(jnp.int32, (rows, STAT), 1)
    near_stat = stat_ref[...]
    stats = [slot_refs[d][:, 2 * HD:].astype(jnp.float32) for d in range(P_DEV)]

    def pick(stat, first, count):
        chosen = (lane >= first) & (lane < first + count)
        return jnp.sum(jnp.where(chosen, stat, 0.0), axis=1, keepdims=True)

    for h in range(2):
        tops = [pick(stats[d], 8 * h, 3) for d in range(P_DEV)]
        totals = [pick(stats[d], 8 * h + 3, 3) for d in range(P_DEV)]
        far_top = jnp.full((rows, 1), LOWEST, jnp.float32)
        for d in range(P_DEV):
            far_top = jnp.maximum(far_top, jnp.where(has_ref[d] == 1, tops[d], LOWEST))
        far_total = jnp.zeros((rows, 1), jnp.float32)
        far_sum = jnp.zeros((rows, HD), jnp.float32)
        for d in range(P_DEV):
            live = has_ref[d] == 1
            weight = jnp.where(live, totals[d] * jnp.exp(tops[d] - far_top), 0.0)
            far_total = far_total + weight
            block = slot_refs[d][:, h * HD:(h + 1) * HD].astype(jnp.float32)
            far_sum = far_sum + jnp.where(live, weight * block, 0.0)
        near_top = pick(near_stat, 8 * h, 1)
        near_total = pick(near_stat, 8 * h + 3, 1)
        final_top = jnp.maximum(far_top, near_top)
        far_scale = jnp.exp(far_top - final_top)
        near_scale = jnp.exp(near_top - final_top)
        near_sum = sum_ref[:, h * HD:(h + 1) * HD]
        out_ref[:, h * HD:(h + 1) * HD] = (
            (far_sum * far_scale + near_sum * near_scale)
            / (far_total * far_scale + near_total * near_scale)
        ).astype(out_ref.dtype)


def combine(has, slots, self_sum, self_stat):
    rows = slots[0].shape[0]
    tile = 128
    slot_spec = pl.BlockSpec((tile, 2 * HD + STAT), lambda i, t: (i, 0))
    grid_spec = pltpu.PrefetchScalarGridSpec(
        num_scalar_prefetch=1,
        grid=(rows // tile,),
        in_specs=[slot_spec] * P_DEV
        + [
            pl.BlockSpec((tile, 2 * HD), lambda i, t: (i, 0)),
            pl.BlockSpec((tile, STAT), lambda i, t: (i, 0)),
        ],
        out_specs=pl.BlockSpec((tile, 2 * HD), lambda i, t: (i, 0)),
    )
    return pl.pallas_call(
        combine_kernel,
        grid_spec=grid_spec,
        out_shape=jax.ShapeDtypeStruct((rows, 2 * HD), jnp.bfloat16),
        compiler_params=pltpu.CompilerParams(dimension_semantics=("arbitrary",)),
        cost_estimate=pl.CostEstimate(
            flops=rows * 2 * HD * 3 * P_DEV,
            transcendentals=rows * 2 * P_DEV,
            bytes_accessed=P_DEV * rows * (2 * HD + STAT) * 2 + rows * (2 * HD + STAT) * 4 + rows * 2 * HD * 2,
        ),
    )(has, *slots, self_sum, self_stat)


def finish_rows(
    proj_sum,
    tok_float,
    tok_norm,
    extra_input,
    attn_gain,
    laurel_left,
    laurel_right,
    laurel_gain,
    layer_gate,
    layer_proj,
    layer_gain,
):
    laurel_low = jnp.dot(tok_norm, laurel_left, preferred_element_type=jnp.float32).astype(
        jnp.bfloat16
    )
    laurel_out = tok_norm.astype(jnp.float32) + normed(
        jnp.dot(laurel_low, laurel_right, preferred_element_type=jnp.float32),
        laurel_gain.astype(jnp.float32),
    )
    mixture = (tok_float + normed(proj_sum, attn_gain.astype(jnp.float32)) + laurel_out) * (
        1.0 / math.sqrt(2.0)
    )
    gate_act = jnp.dot(mixture.astype(jnp.bfloat16), layer_gate, preferred_element_type=jnp.float32)
    gate_out = (jax.nn.gelu(gate_act, approximate=True) * extra_input.astype(jnp.float32)).astype(
        jnp.bfloat16
    )
    return (
        mixture
        + normed(
            jnp.dot(gate_out, layer_proj, preferred_element_type=jnp.float32),
            layer_gain.astype(jnp.float32),
        )
    ).astype(jnp.bfloat16)


def schedule_table(distances, lengths):
    ids = jnp.arange(P_DEV, dtype=jnp.int32)
    before = (distances[None, :] < distances[:, None]) | (
        (distances[None, :] == distances[:, None]) & (ids[None, :] < ids[:, None])
    )
    rank = jnp.sum(before.astype(jnp.int32), axis=1)
    chosen = rank[:, None] == ids[None, :]
    order = jnp.sum(jnp.where(chosen, ids[:, None], 0), axis=0)
    slot = jnp.sum(jnp.where(chosen, distances[:, None], 0), axis=0)
    length = jnp.sum(jnp.where(chosen, lengths[:, None], 0), axis=0)
    minus = jnp.full((1,), -1, jnp.int32)
    first = (slot != jnp.concatenate([minus, slot[:-1]])).astype(jnp.int32)
    last = (slot != jnp.concatenate([slot[1:], minus])).astype(jnp.int32)
    return order, slot, length, first, last


def stage_table(sorted_rows, kv_head, low, high):
    order, slot, length, first, last = sorted_rows
    ids = jnp.arange(P_DEV, dtype=jnp.int32)
    start = jnp.sum((slot < low).astype(jnp.int32))
    count = jnp.sum(((slot >= low) & (slot <= high)).astype(jnp.int32))
    active = (ids < count).astype(jnp.int32)
    where = jnp.clip(start + jnp.minimum(ids, jnp.maximum(count, 1) - 1), 0, P_DEV - 1)
    rows = [jnp.take(x, where) for x in (order, slot - low, length, first, last)]
    kv_row = jnp.full((P_DEV,), kv_head, jnp.int32)
    return jnp.concatenate(rows + [active, kv_row]).astype(jnp.int32)


def body(
    tokens,
    layer_input,
    input_gain,
    q_weight,
    k_weight,
    v_weight,
    q_gain,
    k_gain,
    o_weight,
    attn_gain,
    laurel_left,
    laurel_right,
    laurel_gain,
    layer_gate,
    layer_proj,
    layer_gain,
    piece_keys,
    piece_values,
    piece_owner,
    piece_len,
    cache_keys,
    cache_values,
    cache_len,
):
    req_count = lax.axis_size("req")
    tp_count = lax.axis_size("tp")
    req_index = lax.axis_index("req")
    tp_index = lax.axis_index("tp")
    local_heads = H // tp_count
    kv_head = tp_index * local_heads // (H // KVH)
    full_o_weight = lax.all_gather(o_weight, "tp", axis=0, tiled=True)
    tok_float = tokens.astype(jnp.float32)
    tok_norm = normed(tok_float, input_gain.astype(jnp.float32)).astype(jnp.bfloat16)
    queries = jnp.dot(tok_norm, q_weight, preferred_element_type=jnp.float32).reshape(
        ROWS, local_heads, HD
    )
    queries = (
        normed(queries, q_gain.astype(jnp.float32))
        .astype(jnp.bfloat16)
        .reshape(ROWS, local_heads * HD)
    )
    key_cols = lax.dynamic_slice_in_dim(k_weight, kv_head * HD, HD, 1)
    value_cols = lax.dynamic_slice_in_dim(v_weight, kv_head * HD, HD, 1)
    new_keys = normed(
        jnp.dot(tok_norm, key_cols, preferred_element_type=jnp.float32), k_gain.astype(jnp.float32)
    ).astype(jnp.bfloat16)
    new_values = normed(
        jnp.dot(tok_norm, value_cols, preferred_element_type=jnp.float32), 1.0
    ).astype(jnp.bfloat16)
    own_block = queries[:CH]
    half = P_DEV // 2
    early = [passed_along(own_block, "req", d) for d in range(1, half)]
    held = lax.optimization_barrier((own_block, *early))[0]
    late = [passed_along(held, "req", d) for d in range(half, P_DEV)]
    self_sum, self_stat = self_attention(own_block, new_keys[:CH], new_values[:CH])

    owners = lax.dynamic_slice_in_dim(piece_owner, req_index * P_DEV, P_DEV)
    lengths = lax.dynamic_slice_in_dim(piece_len, req_index * P_DEV, P_DEV)
    distances = (req_index - owners + req_count) % req_count
    sorted_rows = schedule_table(distances, lengths)
    near = piece_attention(
        stage_table(sorted_rows, kv_head, 0, half - 1), [own_block] + early,
        piece_keys, piece_values, self_stat,
    )
    far = piece_attention(
        stage_table(sorted_rows, kv_head, half, P_DEV - 1), late,
        piece_keys, piece_values, near[0],
    )
    packed = list(near) + list(far)
    slots = [packed[0]] + [passed_along(packed[d], "req", -d) for d in range(1, P_DEV)]

    block_ids = (req_index + jnp.arange(P_DEV, dtype=jnp.int32)) % req_count
    block_owners = jnp.take(piece_owner.reshape(req_count, P_DEV), block_ids, axis=0)
    has = jnp.any(block_owners == req_index, axis=1).astype(jnp.int32)
    span_att = combine(has, slots, self_sum, self_stat)
    decode_q = queries[CH:].reshape(DEC_DEV, local_heads, HD)
    cache_key = lax.dynamic_slice_in_dim(cache_keys, kv_head * HD, HD, 2)
    cache_value = lax.dynamic_slice_in_dim(cache_values, kv_head * HD, HD, 2)
    cache_scores = (
        jnp.einsum("thd,tjd->thj", decode_q, cache_key, preferred_element_type=jnp.float32)
        * SCORE_SCALE
    )
    cache_valid = (
        lax.broadcasted_iota(jnp.int32, (DEC_DEV, 1, DCACHE), 2) < cache_len[:, None, None]
    )
    cache_scores = jnp.where(cache_valid, cache_scores, LOWEST)
    own_scores = (
        jnp.einsum("thd,td->th", decode_q, new_keys[CH:], preferred_element_type=jnp.float32)
        * SCORE_SCALE
    )
    decode_top = jnp.maximum(jnp.max(cache_scores, axis=-1), own_scores)
    cache_exp = jnp.exp(cache_scores - decode_top[:, :, None])
    own_exp = jnp.exp(own_scores - decode_top)
    decode_total = jnp.sum(cache_exp, axis=-1) + own_exp
    decode_sum = (
        jnp.einsum(
            "thj,tjd->thd",
            cache_exp.astype(jnp.bfloat16),
            cache_value,
            preferred_element_type=jnp.float32,
        )
        + rounded(own_exp).astype(jnp.float32)[:, :, None]
        * new_values[CH:].astype(jnp.float32)[:, None, :]
    )
    decode_att = (
        (decode_sum / decode_total[:, :, None])
        .reshape(DEC_DEV, local_heads * HD)
        .astype(jnp.bfloat16)
    )
    attended = jnp.concatenate([span_att, decode_att], axis=0)
    part = CH // tp_count

    def rows_of(x, owner):
        return jnp.concatenate(
            [lax.dynamic_slice_in_dim(x, owner * part, part, 0), x[CH:]], axis=0
        )

    proj_sum = jnp.dot(rows_of(attended, tp_index), o_weight, preferred_element_type=jnp.float32)
    for shift in range(1, tp_count):
        target = (tp_index + shift) % tp_count
        got_rows = passed_along(rows_of(attended, target), "tp", shift)
        got_weight = passed_along(o_weight, "tp", shift)
        proj_sum = proj_sum + jnp.dot(got_rows, got_weight, preferred_element_type=jnp.float32)
    mine = finish_rows(
        proj_sum,
        rows_of(tok_float, tp_index),
        rows_of(tok_norm, tp_index),
        rows_of(layer_input, tp_index),
        attn_gain,
        laurel_left,
        laurel_right,
        laurel_gain,
        layer_gate,
        layer_proj,
        layer_gain,
    )
    gathered = [mine] + [passed_along(mine, "tp", shift) for shift in range(1, tp_count)]

    def assemble(me):
        def build(*got):
            blocks = [got[(me - owner) % tp_count][:part] for owner in range(tp_count)]
            return jnp.concatenate(blocks + [got[me][part:]], axis=0)

        return build

    return lax.switch(tp_index, [assemble(me) for me in range(tp_count)], *gathered)


def solution(mesh):
    placed = (
        P("req", None),
        P("req", None),
        P(),
        P(None, "tp"),
        P(),
        P(),
        P(),
        P(),
        P("tp", None),
        P(),
        P(),
        P(),
        P(),
        P(),
        P(),
        P(),
        P("req", None, None),
        P("req", None, None),
        P(),
        P(),
        P("req", None, None),
        P("req", None, None),
        P("req"),
    )
    return jax.shard_map(
        body, mesh=mesh, in_specs=placed, out_specs=P("req", None), check_vma=False
    )
```

```python
import functools
import math

import jax
import jax.numpy as jnp
from jax import lax
from jax.experimental import pallas as pl
from jax.experimental.pallas import tpu as pltpu
from jax.sharding import PartitionSpec as P

H = 8
KVH = 2
HD = 256
CH = 512
DEC_DEV = 4
P_DEV = 8
PIECE = 1024
DCACHE = 512
ROWS = 516
STAT = 128
CHUNK = 256


LOWEST = -1e30
SCORE_SCALE = 1.0 / math.sqrt(HD)


def passed_along(x, axis, by):
    length = lax.axis_size(axis)
    return lax.ppermute(x, axis, [(i, (i + by) % length) for i in range(length)])


def rounded(x):
    return lax.optimization_barrier(x.astype(jnp.bfloat16))


def normed(x, scale_gain):
    return x * lax.rsqrt(jnp.mean(x * x, axis=-1, keepdims=True) + 1e-06) * scale_gain


def head_partial(q, keys, values, valid):
    scores = lax.dot_general(q, keys, (((1,), (1,)), ((), ())), preferred_element_type=jnp.float32)
    scores = jnp.where(valid, scores, LOWEST)
    top = jnp.max(scores, axis=1, keepdims=True)
    weights = jnp.exp((scores - top) * SCORE_SCALE)
    total = jnp.sum(weights, axis=1, keepdims=True)
    summed = jnp.dot(weights.astype(jnp.bfloat16), values, preferred_element_type=jnp.float32)
    return top * SCORE_SCALE, total, summed


def split3(x):
    hi = x.astype(jnp.bfloat16).astype(jnp.float32)
    rest = x - hi
    mid = rest.astype(jnp.bfloat16).astype(jnp.float32)
    lo = rest - mid
    return hi, mid, lo


def piece_kernel(slots, tab_ref, *refs):
    q_refs = refs[:slots]
    k_ref, v_ref = refs[slots:slots + 2]
    out_refs = refs[slots + 3:2 * slots + 3]
    scratch = refs[2 * slots + 3:]
    step = pl.program_id(0)

    @pl.when(tab_ref[5 * P_DEV + step] == 1)
    def _():
        piece_step(step, tab_ref, q_refs, k_ref, v_ref, out_refs, *scratch)


def piece_step(step, tab_ref, q_refs, k_ref, v_ref, out_refs, qbuf, fin, acc_m, acc_l, acc_n, sbuf, lbuf, nbuf):
    slots = len(q_refs)
    slot = tab_ref[P_DEV + step]
    length = tab_ref[2 * P_DEV + step]
    first = tab_ref[3 * P_DEV + step]
    last = tab_ref[4 * P_DEV + step]
    for k in range(slots):

        @pl.when(slot == k)
        def _(k=k):
            qbuf[...] = q_refs[k][...]

    rows = qbuf.shape[0]
    chunks = (length + CHUNK - 1) // CHUNK
    for h in range(2):
        q = qbuf[:, h * HD:(h + 1) * HD]

        def score_chunk(c, top, q=q):
            start = pl.multiple_of(c * CHUNK, CHUNK)
            scores = lax.dot_general(
                q, k_ref[0, pl.ds(start, CHUNK), :], (((1,), (1,)), ((), ())),
                preferred_element_type=jnp.float32,
            )
            valid = lax.broadcasted_iota(jnp.int32, (rows, CHUNK), 1) + start < length
            scores = jnp.where(valid, scores, LOWEST)
            sbuf[c] = scores
            return jnp.maximum(top, jnp.max(scores, axis=1, keepdims=True))

        top = lax.fori_loop(0, chunks, score_chunk, jnp.full((rows, 1), LOWEST, jnp.float32))
        lbuf[...] = jnp.zeros_like(lbuf)
        nbuf[...] = jnp.zeros_like(nbuf)

        @pl.loop(0, chunks)
        def _(c, top=top):
            start = pl.multiple_of(c * CHUNK, CHUNK)
            weights = jnp.exp((sbuf[c] - top) * SCORE_SCALE)
            lbuf[...] += jnp.sum(weights, axis=1, keepdims=True)
            nbuf[...] += jnp.dot(
                weights.astype(jnp.bfloat16), v_ref[0, pl.ds(start, CHUNK), :],
                preferred_element_type=jnp.float32,
            )

        top = top * SCORE_SCALE

        @pl.when(first == 1)
        def _(h=h, top=top):
            acc_m[h] = top
            acc_l[h] = lbuf[...]
            acc_n[h] = nbuf[...]

        @pl.when(first == 0)
        def _(h=h, top=top):
            old = acc_m[h]
            new = jnp.maximum(old, top)
            keep = jnp.exp(old - new)
            add = jnp.exp(top - new)
            acc_l[h] = acc_l[h] * keep + lbuf[...] * add
            acc_n[h] = acc_n[h] * keep + nbuf[...] * add
            acc_m[h] = new

    @pl.when(last == 1)
    def _():
        lane = lax.broadcasted_iota(jnp.int32, (rows, STAT), 1)
        stat = jnp.zeros((rows, STAT), jnp.float32)
        for h in range(2):
            total = acc_l[h]
            fin[:, h * HD:(h + 1) * HD] = (acc_n[h] / total).astype(jnp.bfloat16)
            for i, part in enumerate(split3(acc_m[h]) + split3(total)):
                stat = jnp.where(lane == 8 * h + i, part, stat)
        fin[:, 2 * HD:] = stat.astype(jnp.bfloat16)
        for k in range(slots):

            @pl.when(slot == k)
            def _(k=k):
                out_refs[k][...] = fin[...]


def piece_attention(table, windows, piece_keys, piece_values, after):
    rows = windows[0].shape[0]
    slots = len(windows)
    q_spec = pl.BlockSpec((rows, 2 * HD), lambda s, t: (0, 0))
    kv_spec = pl.BlockSpec((1, PIECE, HD), lambda s, t: (t[s], 0, t[6 * P_DEV]))
    out_spec = pl.BlockSpec((rows, 2 * HD + STAT), lambda s, t: (0, 0))
    grid_spec = pltpu.PrefetchScalarGridSpec(
        num_scalar_prefetch=1,
        grid=(P_DEV,),
        in_specs=[q_spec] * slots + [kv_spec, kv_spec, pl.BlockSpec(memory_space=pl.ANY)],
        out_specs=[out_spec] * slots,
        scratch_shapes=[
            pltpu.VMEM((rows, 2 * HD), jnp.bfloat16),
            pltpu.VMEM((rows, 2 * HD + STAT), jnp.bfloat16),
            pltpu.VMEM((2, rows, 1), jnp.float32),
            pltpu.VMEM((2, rows, 1), jnp.float32),
            pltpu.VMEM((2, rows, HD), jnp.float32),
            pltpu.VMEM((PIECE // CHUNK, rows, CHUNK), jnp.float32),
            pltpu.VMEM((rows, 1), jnp.float32),
            pltpu.VMEM((rows, HD), jnp.float32),
        ],
    )
    pieces = P_DEV // 2
    flops = pieces * 2 * 2 * 2 * rows * PIECE * HD
    return pl.pallas_call(
        functools.partial(piece_kernel, slots),
        grid_spec=grid_spec,
        out_shape=[jax.ShapeDtypeStruct((rows, 2 * HD + STAT), jnp.bfloat16)] * slots,
        compiler_params=pltpu.CompilerParams(
            dimension_semantics=("arbitrary",), vmem_limit_bytes=48 * 1024 * 1024
        ),
        cost_estimate=pl.CostEstimate(
            flops=flops,
            transcendentals=pieces * 2 * rows * PIECE,
            bytes_accessed=pieces * 2 * PIECE * HD * 2 + slots * rows * 2 * HD * 2 * 2,
        ),
    )(table, *windows, piece_keys, piece_values, after)


def self_kernel(q_ref, k_ref, v_ref, n_ref, stat_ref):
    rows = q_ref.shape[0]
    valid = lax.broadcasted_iota(jnp.int32, (rows, rows), 1) <= lax.broadcasted_iota(
        jnp.int32, (rows, rows), 0
    )
    lane = lax.broadcasted_iota(jnp.int32, (rows, STAT), 1)
    stat = jnp.zeros((rows, STAT), jnp.float32)
    keys = k_ref[...]
    values = v_ref[...]
    for h in range(2):
        top, total, summed = head_partial(q_ref[:, h * HD:(h + 1) * HD], keys, values, valid)
        n_ref[:, h * HD:(h + 1) * HD] = summed
        stat = jnp.where(lane == 8 * h, top, stat)
        stat = jnp.where(lane == 8 * h + 3, total, stat)
    stat_ref[...] = stat


def self_attention(q, keys, values):
    rows = q.shape[0]
    return pl.pallas_call(
        self_kernel,
        out_shape=(
            jax.ShapeDtypeStruct((rows, 2 * HD), jnp.float32),
            jax.ShapeDtypeStruct((rows, STAT), jnp.float32),
        ),
        compiler_params=pltpu.CompilerParams(vmem_limit_bytes=48 * 1024 * 1024),
        cost_estimate=pl.CostEstimate(
            flops=2 * 2 * 2 * rows * rows * HD,
            transcendentals=2 * rows * rows,
            bytes_accessed=rows * 2 * HD * 2 + 2 * rows * HD * 2 + rows * (2 * HD + STAT) * 4,
        ),
    )(q, keys, values)


def combine_kernel(has_ref, *refs):
    slot_refs = refs[:P_DEV]
    sum_ref, stat_ref, out_ref = refs[P_DEV:]
    rows = out_ref.shape[0]
    lane = lax.broadcasted_iota(jnp.int32, (rows, STAT), 1)
    near_stat = stat_ref[...]
    stats = [slot_refs[d][:, 2 * HD:].astype(jnp.float32) for d in range(P_DEV)]

    def pick(stat, first, count):
        chosen = (lane >= first) & (lane < first + count)
        return jnp.sum(jnp.where(chosen, stat, 0.0), axis=1, keepdims=True)

    for h in range(2):
        tops = [pick(stats[d], 8 * h, 3) for d in range(P_DEV)]
        totals = [pick(stats[d], 8 * h + 3, 3) for d in range(P_DEV)]
        far_top = jnp.full((rows, 1), LOWEST, jnp.float32)
        for d in range(P_DEV):
            far_top = jnp.maximum(far_top, jnp.where(has_ref[d] == 1, tops[d], LOWEST))
        far_total = jnp.zeros((rows, 1), jnp.float32)
        far_sum = jnp.zeros((rows, HD), jnp.float32)
        for d in range(P_DEV):
            live = has_ref[d] == 1
            weight = jnp.where(live, totals[d] * jnp.exp(tops[d] - far_top), 0.0)
            far_total = far_total + weight
            block = slot_refs[d][:, h * HD:(h + 1) * HD].astype(jnp.float32)
            far_sum = far_sum + jnp.where(live, weight * block, 0.0)
        near_top = pick(near_stat, 8 * h, 1)
        near_total = pick(near_stat, 8 * h + 3, 1)
        final_top = jnp.maximum(far_top, near_top)
        far_scale = jnp.exp(far_top - final_top)
        near_scale = jnp.exp(near_top - final_top)
        near_sum = sum_ref[:, h * HD:(h + 1) * HD]
        out_ref[:, h * HD:(h + 1) * HD] = (
            (far_sum * far_scale + near_sum * near_scale)
            / (far_total * far_scale + near_total * near_scale)
        ).astype(out_ref.dtype)


def combine(has, slots, self_sum, self_stat):
    rows = slots[0].shape[0]
    tile = 128
    slot_spec = pl.BlockSpec((tile, 2 * HD + STAT), lambda i, t: (i, 0))
    grid_spec = pltpu.PrefetchScalarGridSpec(
        num_scalar_prefetch=1,
        grid=(rows // tile,),
        in_specs=[slot_spec] * P_DEV
        + [
            pl.BlockSpec((tile, 2 * HD), lambda i, t: (i, 0)),
            pl.BlockSpec((tile, STAT), lambda i, t: (i, 0)),
        ],
        out_specs=pl.BlockSpec((tile, 2 * HD), lambda i, t: (i, 0)),
    )
    return pl.pallas_call(
        combine_kernel,
        grid_spec=grid_spec,
        out_shape=jax.ShapeDtypeStruct((rows, 2 * HD), jnp.bfloat16),
        compiler_params=pltpu.CompilerParams(dimension_semantics=("arbitrary",)),
        cost_estimate=pl.CostEstimate(
            flops=rows * 2 * HD * 3 * P_DEV,
            transcendentals=rows * 2 * P_DEV,
            bytes_accessed=P_DEV * rows * (2 * HD + STAT) * 2 + rows * (2 * HD + STAT) * 4 + rows * 2 * HD * 2,
        ),
    )(has, *slots, self_sum, self_stat)


def finish_rows(
    proj_sum,
    tok_float,
    tok_norm,
    extra_input,
    attn_gain,
    laurel_left,
    laurel_right,
    laurel_gain,
    layer_gate,
    layer_proj,
    layer_gain,
):
    laurel_low = jnp.dot(tok_norm, laurel_left, preferred_element_type=jnp.float32).astype(
        jnp.bfloat16
    )
    laurel_out = tok_norm.astype(jnp.float32) + normed(
        jnp.dot(laurel_low, laurel_right, preferred_element_type=jnp.float32),
        laurel_gain.astype(jnp.float32),
    )
    mixture = (tok_float + normed(proj_sum, attn_gain.astype(jnp.float32)) + laurel_out) * (
        1.0 / math.sqrt(2.0)
    )
    gate_act = jnp.dot(mixture.astype(jnp.bfloat16), layer_gate, preferred_element_type=jnp.float32)
    gate_out = (jax.nn.gelu(gate_act, approximate=True) * extra_input.astype(jnp.float32)).astype(
        jnp.bfloat16
    )
    return (
        mixture
        + normed(
            jnp.dot(gate_out, layer_proj, preferred_element_type=jnp.float32),
            layer_gain.astype(jnp.float32),
        )
    ).astype(jnp.bfloat16)


def schedule_table(distances, lengths):
    ids = jnp.arange(P_DEV, dtype=jnp.int32)
    before = (distances[None, :] < distances[:, None]) | (
        (distances[None, :] == distances[:, None]) & (ids[None, :] < ids[:, None])
    )
    rank = jnp.sum(before.astype(jnp.int32), axis=1)
    chosen = rank[:, None] == ids[None, :]
    order = jnp.sum(jnp.where(chosen, ids[:, None], 0), axis=0)
    slot = jnp.sum(jnp.where(chosen, distances[:, None], 0), axis=0)
    length = jnp.sum(jnp.where(chosen, lengths[:, None], 0), axis=0)
    minus = jnp.full((1,), -1, jnp.int32)
    first = (slot != jnp.concatenate([minus, slot[:-1]])).astype(jnp.int32)
    last = (slot != jnp.concatenate([slot[1:], minus])).astype(jnp.int32)
    return order, slot, length, first, last


def stage_table(sorted_rows, kv_head, low, high):
    order, slot, length, first, last = sorted_rows
    ids = jnp.arange(P_DEV, dtype=jnp.int32)
    start = jnp.sum((slot < low).astype(jnp.int32))
    count = jnp.sum(((slot >= low) & (slot <= high)).astype(jnp.int32))
    active = (ids < count).astype(jnp.int32)
    where = jnp.clip(start + jnp.minimum(ids, jnp.maximum(count, 1) - 1), 0, P_DEV - 1)
    rows = [jnp.take(x, where) for x in (order, slot - low, length, first, last)]
    kv_row = jnp.full((P_DEV,), kv_head, jnp.int32)
    return jnp.concatenate(rows + [active, kv_row]).astype(jnp.int32)


def body(
    tokens,
    layer_input,
    input_gain,
    q_weight,
    k_weight,
    v_weight,
    q_gain,
    k_gain,
    o_weight,
    attn_gain,
    laurel_left,
    laurel_right,
    laurel_gain,
    layer_gate,
    layer_proj,
    layer_gain,
    piece_keys,
    piece_values,
    piece_owner,
    piece_len,
    cache_keys,
    cache_values,
    cache_len,
):
    req_count = lax.axis_size("req")
    tp_count = lax.axis_size("tp")
    req_index = lax.axis_index("req")
    tp_index = lax.axis_index("tp")
    local_heads = H // tp_count
    kv_head = tp_index * local_heads // (H // KVH)
    full_o_weight = lax.all_gather(o_weight, "tp", axis=0, tiled=True)
    tok_float = tokens.astype(jnp.float32)
    tok_norm = normed(tok_float, input_gain.astype(jnp.float32)).astype(jnp.bfloat16)
    queries = jnp.dot(tok_norm, q_weight, preferred_element_type=jnp.float32).reshape(
        ROWS, local_heads, HD
    )
    queries = (
        normed(queries, q_gain.astype(jnp.float32))
        .astype(jnp.bfloat16)
        .reshape(ROWS, local_heads * HD)
    )
    key_cols = lax.dynamic_slice_in_dim(k_weight, kv_head * HD, HD, 1)
    value_cols = lax.dynamic_slice_in_dim(v_weight, kv_head * HD, HD, 1)
    new_keys = normed(
        jnp.dot(tok_norm, key_cols, preferred_element_type=jnp.float32), k_gain.astype(jnp.float32)
    ).astype(jnp.bfloat16)
    new_values = normed(
        jnp.dot(tok_norm, value_cols, preferred_element_type=jnp.float32), 1.0
    ).astype(jnp.bfloat16)
    own_block = queries[:CH]
    half = P_DEV // 2
    far_windows = [passed_along(own_block, "req", d) for d in range(half, P_DEV)]
    held = lax.optimization_barrier((own_block, *far_windows))[0]
    near_windows = [passed_along(held, "req", d) for d in range(1, half)]
    self_sum, self_stat = self_attention(own_block, new_keys[:CH], new_values[:CH])

    owners = lax.dynamic_slice_in_dim(piece_owner, req_index * P_DEV, P_DEV)
    lengths = lax.dynamic_slice_in_dim(piece_len, req_index * P_DEV, P_DEV)
    distances = (req_index - owners + req_count) % req_count
    sorted_rows = schedule_table(distances, lengths)
    own = piece_attention(
        stage_table(sorted_rows, kv_head, 0, 0), [own_block], piece_keys, piece_values, self_stat
    )
    far = piece_attention(
        stage_table(sorted_rows, kv_head, half, P_DEV - 1), far_windows,
        piece_keys, piece_values, own[0],
    )
    far_back = [passed_along(far[d - half], "req", -d) for d in range(half, P_DEV)]
    near = piece_attention(
        stage_table(sorted_rows, kv_head, 1, half - 1), near_windows,
        piece_keys, piece_values, far[0],
    )
    near_back = [passed_along(near[d - 1], "req", -d) for d in range(1, half)]
    slots = [own[0]] + near_back + far_back

    block_ids = (req_index + jnp.arange(P_DEV, dtype=jnp.int32)) % req_count
    block_owners = jnp.take(piece_owner.reshape(req_count, P_DEV), block_ids, axis=0)
    has = jnp.any(block_owners == req_index, axis=1).astype(jnp.int32)
    span_att = combine(has, slots, self_sum, self_stat)
    decode_q = queries[CH:].reshape(DEC_DEV, local_heads, HD)
    cache_key = lax.dynamic_slice_in_dim(cache_keys, kv_head * HD, HD, 2)
    cache_value = lax.dynamic_slice_in_dim(cache_values, kv_head * HD, HD, 2)
    cache_scores = (
        jnp.einsum("thd,tjd->thj", decode_q, cache_key, preferred_element_type=jnp.float32)
        * SCORE_SCALE
    )
    cache_valid = (
        lax.broadcasted_iota(jnp.int32, (DEC_DEV, 1, DCACHE), 2) < cache_len[:, None, None]
    )
    cache_scores = jnp.where(cache_valid, cache_scores, LOWEST)
    own_scores = (
        jnp.einsum("thd,td->th", decode_q, new_keys[CH:], preferred_element_type=jnp.float32)
        * SCORE_SCALE
    )
    decode_top = jnp.maximum(jnp.max(cache_scores, axis=-1), own_scores)
    cache_exp = jnp.exp(cache_scores - decode_top[:, :, None])
    own_exp = jnp.exp(own_scores - decode_top)
    decode_total = jnp.sum(cache_exp, axis=-1) + own_exp
    decode_sum = (
        jnp.einsum(
            "thj,tjd->thd",
            cache_exp.astype(jnp.bfloat16),
            cache_value,
            preferred_element_type=jnp.float32,
        )
        + rounded(own_exp).astype(jnp.float32)[:, :, None]
        * new_values[CH:].astype(jnp.float32)[:, None, :]
    )
    decode_att = (
        (decode_sum / decode_total[:, :, None])
        .reshape(DEC_DEV, local_heads * HD)
        .astype(jnp.bfloat16)
    )
    attended = jnp.concatenate([span_att, decode_att], axis=0)
    part = CH // tp_count

    def rows_of(x, owner):
        return jnp.concatenate(
            [lax.dynamic_slice_in_dim(x, owner * part, part, 0), x[CH:]], axis=0
        )

    proj_sum = jnp.dot(rows_of(attended, tp_index), o_weight, preferred_element_type=jnp.float32)
    for shift in range(1, tp_count):
        target = (tp_index + shift) % tp_count
        got_rows = passed_along(rows_of(attended, target), "tp", shift)
        got_weight = passed_along(o_weight, "tp", shift)
        proj_sum = proj_sum + jnp.dot(got_rows, got_weight, preferred_element_type=jnp.float32)
    mine = finish_rows(
        proj_sum,
        rows_of(tok_float, tp_index),
        rows_of(tok_norm, tp_index),
        rows_of(layer_input, tp_index),
        attn_gain,
        laurel_left,
        laurel_right,
        laurel_gain,
        layer_gate,
        layer_proj,
        layer_gain,
    )
    gathered = [mine] + [passed_along(mine, "tp", shift) for shift in range(1, tp_count)]

    def assemble(me):
        def build(*got):
            blocks = [got[(me - owner) % tp_count][:part] for owner in range(tp_count)]
            return jnp.concatenate(blocks + [got[me][part:]], axis=0)

        return build

    return lax.switch(tp_index, [assemble(me) for me in range(tp_count)], *gathered)


def solution(mesh):
    placed = (
        P("req", None),
        P("req", None),
        P(),
        P(None, "tp"),
        P(),
        P(),
        P(),
        P(),
        P("tp", None),
        P(),
        P(),
        P(),
        P(),
        P(),
        P(),
        P(),
        P("req", None, None),
        P("req", None, None),
        P(),
        P(),
        P("req", None, None),
        P("req", None, None),
        P("req"),
    )
    return jax.shard_map(
        body, mesh=mesh, in_specs=placed, out_specs=P("req", None), check_vma=False
    )
```

```python
import functools
import math

import jax
import jax.numpy as jnp
from jax import lax
from jax.experimental import pallas as pl
from jax.experimental.pallas import tpu as pltpu
from jax.sharding import PartitionSpec as P

H = 8
KVH = 2
HD = 256
CH = 512
DEC_DEV = 4
P_DEV = 8
PIECE = 1024
DCACHE = 512
ROWS = 516
STAT = 128
STAT_ROWS = 16
CHUNK = 256


LOWEST = -1e30
SCORE_SCALE = 1.0 / math.sqrt(HD)


def passed_along(x, axis, by):
    length = lax.axis_size(axis)
    return lax.ppermute(x, axis, [(i, (i + by) % length) for i in range(length)])


def rounded(x):
    return lax.optimization_barrier(x.astype(jnp.bfloat16))


def normed(x, scale_gain):
    return x * lax.rsqrt(jnp.mean(x * x, axis=-1, keepdims=True) + 1e-06) * scale_gain


def head_partial(q, keys, values, valid):
    scores = lax.dot_general(q, keys, (((1,), (1,)), ((), ())), preferred_element_type=jnp.float32)
    scores = jnp.where(valid, scores, LOWEST)
    top = jnp.max(scores, axis=1, keepdims=True)
    weights = jnp.exp((scores - top) * SCORE_SCALE)
    total = jnp.sum(weights, axis=1, keepdims=True)
    summed = jnp.dot(weights.astype(jnp.bfloat16), values, preferred_element_type=jnp.float32)
    return top * SCORE_SCALE, total, summed


def split3(x):
    hi = x.astype(jnp.bfloat16).astype(jnp.float32)
    rest = x - hi
    mid = rest.astype(jnp.bfloat16).astype(jnp.float32)
    lo = rest - mid
    return hi, mid, lo


def piece_kernel(slots, tab_ref, *refs):
    q_refs = refs[:slots]
    k_ref, v_ref = refs[slots:slots + 2]
    out_refs = refs[slots + 3:2 * slots + 3]
    scratch = refs[2 * slots + 3:]
    step = pl.program_id(0)

    @pl.when(tab_ref[5 * P_DEV + step] == 1)
    def _():
        piece_step(step, tab_ref, q_refs, k_ref, v_ref, out_refs, *scratch)


def piece_step(step, tab_ref, q_refs, k_ref, v_ref, out_refs, qbuf, fin, acc_m, acc_l, acc_n, sbuf, lbuf, nbuf):
    slots = len(q_refs)
    slot = tab_ref[P_DEV + step]
    length = tab_ref[2 * P_DEV + step]
    first = tab_ref[3 * P_DEV + step]
    last = tab_ref[4 * P_DEV + step]
    for k in range(slots):

        @pl.when(slot == k)
        def _(k=k):
            qbuf[...] = q_refs[k][...]

    rows = qbuf.shape[0]
    chunks = (length + CHUNK - 1) // CHUNK
    for h in range(2):
        q = qbuf[:, h * HD:(h + 1) * HD]

        def score_chunk(c, top, q=q):
            start = pl.multiple_of(c * CHUNK, CHUNK)
            scores = lax.dot_general(
                q, k_ref[0, pl.ds(start, CHUNK), :], (((1,), (1,)), ((), ())),
                preferred_element_type=jnp.float32,
            )
            valid = lax.broadcasted_iota(jnp.int32, (rows, CHUNK), 1) + start < length
            scores = jnp.where(valid, scores, LOWEST)
            sbuf[c] = scores
            return jnp.maximum(top, jnp.max(scores, axis=1, keepdims=True))

        top = lax.fori_loop(0, chunks, score_chunk, jnp.full((rows, 1), LOWEST, jnp.float32))
        lbuf[...] = jnp.zeros_like(lbuf)
        nbuf[...] = jnp.zeros_like(nbuf)

        @pl.loop(0, chunks)
        def _(c, top=top):
            start = pl.multiple_of(c * CHUNK, CHUNK)
            weights = jnp.exp((sbuf[c] - top) * SCORE_SCALE)
            lbuf[...] += jnp.sum(weights, axis=1, keepdims=True)
            nbuf[...] += jnp.dot(
                weights.astype(jnp.bfloat16), v_ref[0, pl.ds(start, CHUNK), :],
                preferred_element_type=jnp.float32,
            )

        top = top * SCORE_SCALE

        @pl.when(first == 1)
        def _(h=h, top=top):
            acc_m[h] = top
            acc_l[h] = lbuf[...]
            acc_n[h] = nbuf[...]

        @pl.when(first == 0)
        def _(h=h, top=top):
            old = acc_m[h]
            new = jnp.maximum(old, top)
            keep = jnp.exp(old - new)
            add = jnp.exp(top - new)
            acc_l[h] = acc_l[h] * keep + lbuf[...] * add
            acc_n[h] = acc_n[h] * keep + nbuf[...] * add
            acc_m[h] = new

    @pl.when(last == 1)
    def _():
        lane = lax.broadcasted_iota(jnp.int32, (rows, STAT), 1)
        stat = jnp.zeros((rows, STAT), jnp.float32)
        for h in range(2):
            total = acc_l[h]
            fin[:rows, h * HD:(h + 1) * HD] = (acc_n[h] / total).astype(jnp.bfloat16)
            for i, part in enumerate(split3(acc_m[h]) + split3(total)):
                stat = jnp.where(lane == 8 * h + i, part, stat)
        fin[rows:, :] = jnp.transpose(stat)[:STAT_ROWS].astype(jnp.bfloat16)
        for k in range(slots):

            @pl.when(slot == k)
            def _(k=k):
                out_refs[k][...] = fin[...]


def piece_attention(table, windows, piece_keys, piece_values, after):
    rows = windows[0].shape[0]
    slots = len(windows)
    q_spec = pl.BlockSpec((rows, 2 * HD), lambda s, t: (0, 0))
    kv_spec = pl.BlockSpec((1, PIECE, HD), lambda s, t: (t[s], 0, t[6 * P_DEV]))
    out_spec = pl.BlockSpec((rows + STAT_ROWS, 2 * HD), lambda s, t: (0, 0))
    grid_spec = pltpu.PrefetchScalarGridSpec(
        num_scalar_prefetch=1,
        grid=(P_DEV,),
        in_specs=[q_spec] * slots + [kv_spec, kv_spec, pl.BlockSpec(memory_space=pl.ANY)],
        out_specs=[out_spec] * slots,
        scratch_shapes=[
            pltpu.VMEM((rows, 2 * HD), jnp.bfloat16),
            pltpu.VMEM((rows + STAT_ROWS, 2 * HD), jnp.bfloat16),
            pltpu.VMEM((2, rows, 1), jnp.float32),
            pltpu.VMEM((2, rows, 1), jnp.float32),
            pltpu.VMEM((2, rows, HD), jnp.float32),
            pltpu.VMEM((PIECE // CHUNK, rows, CHUNK), jnp.float32),
            pltpu.VMEM((rows, 1), jnp.float32),
            pltpu.VMEM((rows, HD), jnp.float32),
        ],
    )
    pieces = P_DEV // 2
    flops = pieces * 2 * 2 * 2 * rows * PIECE * HD
    return pl.pallas_call(
        functools.partial(piece_kernel, slots),
        grid_spec=grid_spec,
        out_shape=[jax.ShapeDtypeStruct((rows + STAT_ROWS, 2 * HD), jnp.bfloat16)] * slots,
        compiler_params=pltpu.CompilerParams(
            dimension_semantics=("arbitrary",), vmem_limit_bytes=48 * 1024 * 1024
        ),
        cost_estimate=pl.CostEstimate(
            flops=flops,
            transcendentals=pieces * 2 * rows * PIECE,
            bytes_accessed=pieces * 2 * PIECE * HD * 2 + slots * rows * 2 * HD * 2 * 2,
        ),
    )(table, *windows, piece_keys, piece_values, after)


def self_kernel(q_ref, k_ref, v_ref, n_ref, stat_ref):
    rows = q_ref.shape[0]
    valid = lax.broadcasted_iota(jnp.int32, (rows, rows), 1) <= lax.broadcasted_iota(
        jnp.int32, (rows, rows), 0
    )
    lane = lax.broadcasted_iota(jnp.int32, (rows, STAT), 1)
    stat = jnp.zeros((rows, STAT), jnp.float32)
    keys = k_ref[...]
    values = v_ref[...]
    for h in range(2):
        top, total, summed = head_partial(q_ref[:, h * HD:(h + 1) * HD], keys, values, valid)
        n_ref[:, h * HD:(h + 1) * HD] = summed
        stat = jnp.where(lane == 8 * h, top, stat)
        stat = jnp.where(lane == 8 * h + 3, total, stat)
    stat_ref[...] = stat


def self_attention(q, keys, values):
    rows = q.shape[0]
    return pl.pallas_call(
        self_kernel,
        out_shape=(
            jax.ShapeDtypeStruct((rows, 2 * HD), jnp.float32),
            jax.ShapeDtypeStruct((rows, STAT), jnp.float32),
        ),
        compiler_params=pltpu.CompilerParams(vmem_limit_bytes=48 * 1024 * 1024),
        cost_estimate=pl.CostEstimate(
            flops=2 * 2 * 2 * rows * rows * HD,
            transcendentals=2 * rows * rows,
            bytes_accessed=rows * 2 * HD * 2 + 2 * rows * HD * 2 + rows * (2 * HD + STAT) * 4,
        ),
    )(q, keys, values)


def combine_kernel(has_ref, *refs):
    slot_refs = refs[:P_DEV]
    row_refs = refs[P_DEV:2 * P_DEV]
    sum_ref, stat_ref, out_ref = refs[2 * P_DEV:]
    rows = out_ref.shape[0]
    lane = lax.broadcasted_iota(jnp.int32, (rows, STAT), 1)
    near_stat = stat_ref[...]
    pad = jnp.zeros((STAT - STAT_ROWS, rows), jnp.float32)
    stats = [
        jnp.transpose(jnp.concatenate([row_refs[d][...].astype(jnp.float32), pad], axis=0))
        for d in range(P_DEV)
    ]

    def pick(stat, first, count):
        chosen = (lane >= first) & (lane < first + count)
        return jnp.sum(jnp.where(chosen, stat, 0.0), axis=1, keepdims=True)

    for h in range(2):
        tops = [pick(stats[d], 8 * h, 3) for d in range(P_DEV)]
        totals = [pick(stats[d], 8 * h + 3, 3) for d in range(P_DEV)]
        far_top = jnp.full((rows, 1), LOWEST, jnp.float32)
        for d in range(P_DEV):
            far_top = jnp.maximum(far_top, jnp.where(has_ref[d] == 1, tops[d], LOWEST))
        far_total = jnp.zeros((rows, 1), jnp.float32)
        far_sum = jnp.zeros((rows, HD), jnp.float32)
        for d in range(P_DEV):
            live = has_ref[d] == 1
            weight = jnp.where(live, totals[d] * jnp.exp(tops[d] - far_top), 0.0)
            far_total = far_total + weight
            block = slot_refs[d][:, h * HD:(h + 1) * HD].astype(jnp.float32)
            far_sum = far_sum + jnp.where(live, weight * block, 0.0)
        near_top = pick(near_stat, 8 * h, 1)
        near_total = pick(near_stat, 8 * h + 3, 1)
        final_top = jnp.maximum(far_top, near_top)
        far_scale = jnp.exp(far_top - final_top)
        near_scale = jnp.exp(near_top - final_top)
        near_sum = sum_ref[:, h * HD:(h + 1) * HD]
        out_ref[:, h * HD:(h + 1) * HD] = (
            (far_sum * far_scale + near_sum * near_scale)
            / (far_total * far_scale + near_total * near_scale)
        ).astype(out_ref.dtype)


def combine(has, slots, self_sum, self_stat):
    rows = self_sum.shape[0]
    tile = 128
    slot_spec = pl.BlockSpec((tile, 2 * HD), lambda i, t: (i, 0))
    row_spec = pl.BlockSpec((STAT_ROWS, tile), lambda i, t: (rows // STAT_ROWS, i))
    grid_spec = pltpu.PrefetchScalarGridSpec(
        num_scalar_prefetch=1,
        grid=(rows // tile,),
        in_specs=[slot_spec] * P_DEV
        + [row_spec] * P_DEV
        + [
            pl.BlockSpec((tile, 2 * HD), lambda i, t: (i, 0)),
            pl.BlockSpec((tile, STAT), lambda i, t: (i, 0)),
        ],
        out_specs=pl.BlockSpec((tile, 2 * HD), lambda i, t: (i, 0)),
    )
    return pl.pallas_call(
        combine_kernel,
        grid_spec=grid_spec,
        out_shape=jax.ShapeDtypeStruct((rows, 2 * HD), jnp.bfloat16),
        compiler_params=pltpu.CompilerParams(dimension_semantics=("arbitrary",)),
        cost_estimate=pl.CostEstimate(
            flops=rows * 2 * HD * 3 * P_DEV,
            transcendentals=rows * 2 * P_DEV,
            bytes_accessed=P_DEV * (rows + STAT_ROWS) * 2 * HD * 2 + rows * (2 * HD + STAT) * 4 + rows * 2 * HD * 2,
        ),
    )(has, *slots, *slots, self_sum, self_stat)


def finish_rows(
    proj_sum,
    tok_float,
    tok_norm,
    extra_input,
    attn_gain,
    laurel_left,
    laurel_right,
    laurel_gain,
    layer_gate,
    layer_proj,
    layer_gain,
):
    laurel_low = jnp.dot(tok_norm, laurel_left, preferred_element_type=jnp.float32).astype(
        jnp.bfloat16
    )
    laurel_out = tok_norm.astype(jnp.float32) + normed(
        jnp.dot(laurel_low, laurel_right, preferred_element_type=jnp.float32),
        laurel_gain.astype(jnp.float32),
    )
    mixture = (tok_float + normed(proj_sum, attn_gain.astype(jnp.float32)) + laurel_out) * (
        1.0 / math.sqrt(2.0)
    )
    gate_act = jnp.dot(mixture.astype(jnp.bfloat16), layer_gate, preferred_element_type=jnp.float32)
    gate_out = (jax.nn.gelu(gate_act, approximate=True) * extra_input.astype(jnp.float32)).astype(
        jnp.bfloat16
    )
    return (
        mixture
        + normed(
            jnp.dot(gate_out, layer_proj, preferred_element_type=jnp.float32),
            layer_gain.astype(jnp.float32),
        )
    ).astype(jnp.bfloat16)


def schedule_table(distances, lengths):
    ids = jnp.arange(P_DEV, dtype=jnp.int32)
    before = (distances[None, :] < distances[:, None]) | (
        (distances[None, :] == distances[:, None]) & (ids[None, :] < ids[:, None])
    )
    rank = jnp.sum(before.astype(jnp.int32), axis=1)
    chosen = rank[:, None] == ids[None, :]
    order = jnp.sum(jnp.where(chosen, ids[:, None], 0), axis=0)
    slot = jnp.sum(jnp.where(chosen, distances[:, None], 0), axis=0)
    length = jnp.sum(jnp.where(chosen, lengths[:, None], 0), axis=0)
    minus = jnp.full((1,), -1, jnp.int32)
    first = (slot != jnp.concatenate([minus, slot[:-1]])).astype(jnp.int32)
    last = (slot != jnp.concatenate([slot[1:], minus])).astype(jnp.int32)
    return order, slot, length, first, last


def stage_table(sorted_rows, kv_head, low, high):
    order, slot, length, first, last = sorted_rows
    ids = jnp.arange(P_DEV, dtype=jnp.int32)
    start = jnp.sum((slot < low).astype(jnp.int32))
    count = jnp.sum(((slot >= low) & (slot <= high)).astype(jnp.int32))
    active = (ids < count).astype(jnp.int32)
    where = jnp.clip(start + jnp.minimum(ids, jnp.maximum(count, 1) - 1), 0, P_DEV - 1)
    rows = [jnp.take(x, where) for x in (order, slot - low, length, first, last)]
    kv_row = jnp.full((P_DEV,), kv_head, jnp.int32)
    return jnp.concatenate(rows + [active, kv_row]).astype(jnp.int32)


def body(
    tokens,
    layer_input,
    input_gain,
    q_weight,
    k_weight,
    v_weight,
    q_gain,
    k_gain,
    o_weight,
    attn_gain,
    laurel_left,
    laurel_right,
    laurel_gain,
    layer_gate,
    layer_proj,
    layer_gain,
    piece_keys,
    piece_values,
    piece_owner,
    piece_len,
    cache_keys,
    cache_values,
    cache_len,
):
    req_count = lax.axis_size("req")
    tp_count = lax.axis_size("tp")
    req_index = lax.axis_index("req")
    tp_index = lax.axis_index("tp")
    local_heads = H // tp_count
    kv_head = tp_index * local_heads // (H // KVH)
    full_o_weight = lax.all_gather(o_weight, "tp", axis=0, tiled=True)
    tok_float = tokens.astype(jnp.float32)
    tok_norm = normed(tok_float, input_gain.astype(jnp.float32)).astype(jnp.bfloat16)
    queries = jnp.dot(tok_norm, q_weight, preferred_element_type=jnp.float32).reshape(
        ROWS, local_heads, HD
    )
    queries = (
        normed(queries, q_gain.astype(jnp.float32))
        .astype(jnp.bfloat16)
        .reshape(ROWS, local_heads * HD)
    )
    key_cols = lax.dynamic_slice_in_dim(k_weight, kv_head * HD, HD, 1)
    value_cols = lax.dynamic_slice_in_dim(v_weight, kv_head * HD, HD, 1)
    new_keys = normed(
        jnp.dot(tok_norm, key_cols, preferred_element_type=jnp.float32), k_gain.astype(jnp.float32)
    ).astype(jnp.bfloat16)
    new_values = normed(
        jnp.dot(tok_norm, value_cols, preferred_element_type=jnp.float32), 1.0
    ).astype(jnp.bfloat16)
    own_block = queries[:CH]
    half = P_DEV // 2
    far_windows = [passed_along(own_block, "req", d) for d in range(half, P_DEV)]
    held = lax.optimization_barrier((own_block, *far_windows))[0]
    near_windows = [passed_along(held, "req", d) for d in range(1, half)]
    self_sum, self_stat = self_attention(own_block, new_keys[:CH], new_values[:CH])

    owners = lax.dynamic_slice_in_dim(piece_owner, req_index * P_DEV, P_DEV)
    lengths = lax.dynamic_slice_in_dim(piece_len, req_index * P_DEV, P_DEV)
    distances = (req_index - owners + req_count) % req_count
    sorted_rows = schedule_table(distances, lengths)
    own = piece_attention(
        stage_table(sorted_rows, kv_head, 0, 0), [own_block], piece_keys, piece_values, self_stat
    )
    far = piece_attention(
        stage_table(sorted_rows, kv_head, half, P_DEV - 1), far_windows,
        piece_keys, piece_values, own[0],
    )
    far_back = [passed_along(far[d - half], "req", -d) for d in range(half, P_DEV)]
    near = piece_attention(
        stage_table(sorted_rows, kv_head, 1, half - 1), near_windows,
        piece_keys, piece_values, far[0],
    )
    near_back = [passed_along(near[d - 1], "req", -d) for d in range(1, half)]
    slots = [own[0]] + near_back + far_back

    block_ids = (req_index + jnp.arange(P_DEV, dtype=jnp.int32)) % req_count
    block_owners = jnp.take(piece_owner.reshape(req_count, P_DEV), block_ids, axis=0)
    has = jnp.any(block_owners == req_index, axis=1).astype(jnp.int32)
    span_att = combine(has, slots, self_sum, self_stat)
    decode_q = queries[CH:].reshape(DEC_DEV, local_heads, HD)
    cache_key = lax.dynamic_slice_in_dim(cache_keys, kv_head * HD, HD, 2)
    cache_value = lax.dynamic_slice_in_dim(cache_values, kv_head * HD, HD, 2)
    cache_scores = (
        jnp.einsum("thd,tjd->thj", decode_q, cache_key, preferred_element_type=jnp.float32)
        * SCORE_SCALE
    )
    cache_valid = (
        lax.broadcasted_iota(jnp.int32, (DEC_DEV, 1, DCACHE), 2) < cache_len[:, None, None]
    )
    cache_scores = jnp.where(cache_valid, cache_scores, LOWEST)
    own_scores = (
        jnp.einsum("thd,td->th", decode_q, new_keys[CH:], preferred_element_type=jnp.float32)
        * SCORE_SCALE
    )
    decode_top = jnp.maximum(jnp.max(cache_scores, axis=-1), own_scores)
    cache_exp = jnp.exp(cache_scores - decode_top[:, :, None])
    own_exp = jnp.exp(own_scores - decode_top)
    decode_total = jnp.sum(cache_exp, axis=-1) + own_exp
    decode_sum = (
        jnp.einsum(
            "thj,tjd->thd",
            cache_exp.astype(jnp.bfloat16),
            cache_value,
            preferred_element_type=jnp.float32,
        )
        + rounded(own_exp).astype(jnp.float32)[:, :, None]
        * new_values[CH:].astype(jnp.float32)[:, None, :]
    )
    decode_att = (
        (decode_sum / decode_total[:, :, None])
        .reshape(DEC_DEV, local_heads * HD)
        .astype(jnp.bfloat16)
    )
    attended = jnp.concatenate([span_att, decode_att], axis=0)
    part = CH // tp_count

    def rows_of(x, owner):
        return jnp.concatenate(
            [lax.dynamic_slice_in_dim(x, owner * part, part, 0), x[CH:]], axis=0
        )

    proj_sum = jnp.dot(rows_of(attended, tp_index), o_weight, preferred_element_type=jnp.float32)
    for shift in range(1, tp_count):
        target = (tp_index + shift) % tp_count
        got_rows = passed_along(rows_of(attended, target), "tp", shift)
        got_weight = passed_along(o_weight, "tp", shift)
        proj_sum = proj_sum + jnp.dot(got_rows, got_weight, preferred_element_type=jnp.float32)
    mine = finish_rows(
        proj_sum,
        rows_of(tok_float, tp_index),
        rows_of(tok_norm, tp_index),
        rows_of(layer_input, tp_index),
        attn_gain,
        laurel_left,
        laurel_right,
        laurel_gain,
        layer_gate,
        layer_proj,
        layer_gain,
    )
    gathered = [mine] + [passed_along(mine, "tp", shift) for shift in range(1, tp_count)]

    def assemble(me):
        def build(*got):
            blocks = [got[(me - owner) % tp_count][:part] for owner in range(tp_count)]
            return jnp.concatenate(blocks + [got[me][part:]], axis=0)

        return build

    return lax.switch(tp_index, [assemble(me) for me in range(tp_count)], *gathered)


def solution(mesh):
    placed = (
        P("req", None),
        P("req", None),
        P(),
        P(None, "tp"),
        P(),
        P(),
        P(),
        P(),
        P("tp", None),
        P(),
        P(),
        P(),
        P(),
        P(),
        P(),
        P(),
        P("req", None, None),
        P("req", None, None),
        P(),
        P(),
        P("req", None, None),
        P("req", None, None),
        P("req"),
    )
    return jax.shard_map(
        body, mesh=mesh, in_specs=placed, out_specs=P("req", None), check_vma=False
    )
```

```python
import functools
import math

import jax
import jax.numpy as jnp
from jax import lax
from jax.experimental import pallas as pl
from jax.experimental.pallas import tpu as pltpu
from jax.sharding import PartitionSpec as P

H = 8
KVH = 2
HD = 256
CH = 512
DEC_DEV = 4
P_DEV = 8
PIECE = 1024
DCACHE = 512
ROWS = 516
STAT = 128
STAT_ROWS = 16
CHUNK = 256


LOWEST = -1e30
SCORE_SCALE = 1.0 / math.sqrt(HD)


def passed_along(x, axis, by):
    length = lax.axis_size(axis)
    return lax.ppermute(x, axis, [(i, (i + by) % length) for i in range(length)])


def rounded(x):
    return lax.optimization_barrier(x.astype(jnp.bfloat16))


def normed(x, scale_gain):
    return x * lax.rsqrt(jnp.mean(x * x, axis=-1, keepdims=True) + 1e-06) * scale_gain


def head_partial(q, keys, values, valid):
    scores = lax.dot_general(q, keys, (((1,), (1,)), ((), ())), preferred_element_type=jnp.float32)
    scores = jnp.where(valid, scores, LOWEST)
    top = jnp.max(scores, axis=1, keepdims=True)
    weights = jnp.exp((scores - top) * SCORE_SCALE)
    total = jnp.sum(weights, axis=1, keepdims=True)
    summed = jnp.dot(weights.astype(jnp.bfloat16), values, preferred_element_type=jnp.float32)
    return top * SCORE_SCALE, total, summed


def split3(x):
    hi = x.astype(jnp.bfloat16).astype(jnp.float32)
    rest = x - hi
    mid = rest.astype(jnp.bfloat16).astype(jnp.float32)
    lo = rest - mid
    return hi, mid, lo


def piece_kernel(slots, tab_ref, *refs):
    q_refs = refs[:slots]
    k_ref, v_ref = refs[slots:slots + 2]
    out_refs = refs[slots + 3:2 * slots + 3]
    scratch = refs[2 * slots + 3:]
    step = pl.program_id(0)

    @pl.when(tab_ref[5 * P_DEV + step] == 1)
    def _():
        piece_step(step, tab_ref, q_refs, k_ref, v_ref, out_refs, *scratch)


def piece_step(step, tab_ref, q_refs, k_ref, v_ref, out_refs, qbuf, fin, acc_m, acc_l, acc_n, sbuf, lbuf, nbuf):
    slots = len(q_refs)
    slot = tab_ref[P_DEV + step]
    length = tab_ref[2 * P_DEV + step]
    first = tab_ref[3 * P_DEV + step]
    last = tab_ref[4 * P_DEV + step]
    for k in range(slots):

        @pl.when(slot == k)
        def _(k=k):
            qbuf[...] = q_refs[k][...]

    rows = qbuf.shape[0]
    chunks = (length + CHUNK - 1) // CHUNK
    for h in range(2):
        q = qbuf[:, h * HD:(h + 1) * HD]

        def score_chunk(c, top, q=q):
            start = pl.multiple_of(c * CHUNK, CHUNK)
            scores = lax.dot_general(
                q, k_ref[0, pl.ds(start, CHUNK), :], (((1,), (1,)), ((), ())),
                preferred_element_type=jnp.float32,
            )
            valid = lax.broadcasted_iota(jnp.int32, (rows, CHUNK), 1) + start < length
            scores = jnp.where(valid, scores, LOWEST)
            sbuf[c] = scores
            return jnp.maximum(top, jnp.max(scores, axis=1, keepdims=True))

        top = lax.fori_loop(0, chunks, score_chunk, jnp.full((rows, 1), LOWEST, jnp.float32))
        lbuf[...] = jnp.zeros_like(lbuf)
        nbuf[...] = jnp.zeros_like(nbuf)

        @pl.loop(0, chunks)
        def _(c, top=top):
            start = pl.multiple_of(c * CHUNK, CHUNK)
            weights = jnp.exp((sbuf[c] - top) * SCORE_SCALE)
            lbuf[...] += jnp.sum(weights, axis=1, keepdims=True)
            nbuf[...] += jnp.dot(
                weights.astype(jnp.bfloat16), v_ref[0, pl.ds(start, CHUNK), :],
                preferred_element_type=jnp.float32,
            )

        top = top * SCORE_SCALE

        @pl.when(first == 1)
        def _(h=h, top=top):
            acc_m[h] = top
            acc_l[h] = lbuf[...]
            acc_n[h] = nbuf[...]

        @pl.when(first == 0)
        def _(h=h, top=top):
            old = acc_m[h]
            new = jnp.maximum(old, top)
            keep = jnp.exp(old - new)
            add = jnp.exp(top - new)
            acc_l[h] = acc_l[h] * keep + lbuf[...] * add
            acc_n[h] = acc_n[h] * keep + nbuf[...] * add
            acc_m[h] = new

    @pl.when(last == 1)
    def _():
        lane = lax.broadcasted_iota(jnp.int32, (rows, STAT), 1)
        stat = jnp.zeros((rows, STAT), jnp.float32)
        for h in range(2):
            total = acc_l[h]
            fin[:rows, h * HD:(h + 1) * HD] = (acc_n[h] / total).astype(jnp.bfloat16)
            for i, part in enumerate(split3(acc_m[h]) + split3(total)):
                stat = jnp.where(lane == 8 * h + i, part, stat)
        fin[rows:, :] = jnp.transpose(stat)[:STAT_ROWS].astype(jnp.bfloat16)
        for k in range(slots):

            @pl.when(slot == k)
            def _(k=k):
                out_refs[k][...] = fin[...]


def piece_attention(table, windows, piece_keys, piece_values, after):
    rows = windows[0].shape[0]
    slots = len(windows)
    q_spec = pl.BlockSpec((rows, 2 * HD), lambda s, t: (0, 0))
    kv_spec = pl.BlockSpec((1, PIECE, HD), lambda s, t: (t[s], 0, t[6 * P_DEV]))
    out_spec = pl.BlockSpec((rows + STAT_ROWS, 2 * HD), lambda s, t: (0, 0))
    grid_spec = pltpu.PrefetchScalarGridSpec(
        num_scalar_prefetch=1,
        grid=(P_DEV,),
        in_specs=[q_spec] * slots + [kv_spec, kv_spec, pl.BlockSpec(memory_space=pl.ANY)],
        out_specs=[out_spec] * slots,
        scratch_shapes=[
            pltpu.VMEM((rows, 2 * HD), jnp.bfloat16),
            pltpu.VMEM((rows + STAT_ROWS, 2 * HD), jnp.bfloat16),
            pltpu.VMEM((2, rows, 1), jnp.float32),
            pltpu.VMEM((2, rows, 1), jnp.float32),
            pltpu.VMEM((2, rows, HD), jnp.float32),
            pltpu.VMEM((PIECE // CHUNK, rows, CHUNK), jnp.float32),
            pltpu.VMEM((rows, 1), jnp.float32),
            pltpu.VMEM((rows, HD), jnp.float32),
        ],
    )
    pieces = P_DEV // 2
    flops = pieces * 2 * 2 * 2 * rows * PIECE * HD
    return pl.pallas_call(
        functools.partial(piece_kernel, slots),
        grid_spec=grid_spec,
        out_shape=[jax.ShapeDtypeStruct((rows + STAT_ROWS, 2 * HD), jnp.bfloat16)] * slots,
        compiler_params=pltpu.CompilerParams(
            dimension_semantics=("arbitrary",), vmem_limit_bytes=48 * 1024 * 1024
        ),
        cost_estimate=pl.CostEstimate(
            flops=flops,
            transcendentals=pieces * 2 * rows * PIECE,
            bytes_accessed=pieces * 2 * PIECE * HD * 2 + slots * rows * 2 * HD * 2 * 2,
        ),
    )(table, *windows, piece_keys, piece_values, after)


def self_kernel(q_ref, k_ref, v_ref, n_ref, stat_ref):
    rows = q_ref.shape[0]
    valid = lax.broadcasted_iota(jnp.int32, (rows, rows), 1) <= lax.broadcasted_iota(
        jnp.int32, (rows, rows), 0
    )
    lane = lax.broadcasted_iota(jnp.int32, (rows, STAT), 1)
    stat = jnp.zeros((rows, STAT), jnp.float32)
    keys = k_ref[...]
    values = v_ref[...]
    for h in range(2):
        top, total, summed = head_partial(q_ref[:, h * HD:(h + 1) * HD], keys, values, valid)
        n_ref[:, h * HD:(h + 1) * HD] = summed
        stat = jnp.where(lane == 8 * h, top, stat)
        stat = jnp.where(lane == 8 * h + 3, total, stat)
    stat_ref[...] = stat


def self_attention(q, keys, values):
    rows = q.shape[0]
    return pl.pallas_call(
        self_kernel,
        out_shape=(
            jax.ShapeDtypeStruct((rows, 2 * HD), jnp.float32),
            jax.ShapeDtypeStruct((rows, STAT), jnp.float32),
        ),
        compiler_params=pltpu.CompilerParams(vmem_limit_bytes=48 * 1024 * 1024),
        cost_estimate=pl.CostEstimate(
            flops=2 * 2 * 2 * rows * rows * HD,
            transcendentals=2 * rows * rows,
            bytes_accessed=rows * 2 * HD * 2 + 2 * rows * HD * 2 + rows * (2 * HD + STAT) * 4,
        ),
    )(q, keys, values)


def combine_kernel(has_ref, *refs):
    slot_refs = refs[:P_DEV]
    row_refs = refs[P_DEV:2 * P_DEV]
    sum_ref, stat_ref, out_ref = refs[2 * P_DEV:]
    rows = out_ref.shape[0]
    lane = lax.broadcasted_iota(jnp.int32, (rows, STAT), 1)
    near_stat = stat_ref[...]
    pad = jnp.zeros((STAT - STAT_ROWS, rows), jnp.float32)
    stats = [
        jnp.transpose(jnp.concatenate([row_refs[d][...].astype(jnp.float32), pad], axis=0))
        for d in range(P_DEV)
    ]

    def pick(stat, first, count):
        chosen = (lane >= first) & (lane < first + count)
        return jnp.sum(jnp.where(chosen, stat, 0.0), axis=1, keepdims=True)

    for h in range(2):
        tops = [pick(stats[d], 8 * h, 3) for d in range(P_DEV)]
        totals = [pick(stats[d], 8 * h + 3, 3) for d in range(P_DEV)]
        far_top = jnp.full((rows, 1), LOWEST, jnp.float32)
        for d in range(P_DEV):
            far_top = jnp.maximum(far_top, jnp.where(has_ref[d] == 1, tops[d], LOWEST))
        far_total = jnp.zeros((rows, 1), jnp.float32)
        far_sum = jnp.zeros((rows, HD), jnp.float32)
        for d in range(P_DEV):
            live = has_ref[d] == 1
            weight = jnp.where(live, totals[d] * jnp.exp(tops[d] - far_top), 0.0)
            far_total = far_total + weight
            block = slot_refs[d][:, h * HD:(h + 1) * HD].astype(jnp.float32)
            far_sum = far_sum + jnp.where(live, weight * block, 0.0)
        near_top = pick(near_stat, 8 * h, 1)
        near_total = pick(near_stat, 8 * h + 3, 1)
        final_top = jnp.maximum(far_top, near_top)
        far_scale = jnp.exp(far_top - final_top)
        near_scale = jnp.exp(near_top - final_top)
        near_sum = sum_ref[:, h * HD:(h + 1) * HD]
        out_ref[:, h * HD:(h + 1) * HD] = (
            (far_sum * far_scale + near_sum * near_scale)
            / (far_total * far_scale + near_total * near_scale)
        ).astype(out_ref.dtype)


def combine(has, slots, self_sum, self_stat):
    rows = self_sum.shape[0]
    tile = 128
    slot_spec = pl.BlockSpec((tile, 2 * HD), lambda i, t: (i, 0))
    row_spec = pl.BlockSpec((STAT_ROWS, tile), lambda i, t: (rows // STAT_ROWS, i))
    grid_spec = pltpu.PrefetchScalarGridSpec(
        num_scalar_prefetch=1,
        grid=(rows // tile,),
        in_specs=[slot_spec] * P_DEV
        + [row_spec] * P_DEV
        + [
            pl.BlockSpec((tile, 2 * HD), lambda i, t: (i, 0)),
            pl.BlockSpec((tile, STAT), lambda i, t: (i, 0)),
        ],
        out_specs=pl.BlockSpec((tile, 2 * HD), lambda i, t: (i, 0)),
    )
    return pl.pallas_call(
        combine_kernel,
        grid_spec=grid_spec,
        out_shape=jax.ShapeDtypeStruct((rows, 2 * HD), jnp.bfloat16),
        compiler_params=pltpu.CompilerParams(dimension_semantics=("arbitrary",)),
        cost_estimate=pl.CostEstimate(
            flops=rows * 2 * HD * 3 * P_DEV,
            transcendentals=rows * 2 * P_DEV,
            bytes_accessed=P_DEV * (rows + STAT_ROWS) * 2 * HD * 2 + rows * (2 * HD + STAT) * 4 + rows * 2 * HD * 2,
        ),
    )(has, *slots, *slots, self_sum, self_stat)


def finish_rows(
    proj_sum,
    tok_float,
    tok_norm,
    extra_input,
    attn_gain,
    laurel_left,
    laurel_right,
    laurel_gain,
    layer_gate,
    layer_proj,
    layer_gain,
):
    laurel_low = jnp.dot(tok_norm, laurel_left, preferred_element_type=jnp.float32).astype(
        jnp.bfloat16
    )
    laurel_out = tok_norm.astype(jnp.float32) + normed(
        jnp.dot(laurel_low, laurel_right, preferred_element_type=jnp.float32),
        laurel_gain.astype(jnp.float32),
    )
    mixture = (tok_float + normed(proj_sum, attn_gain.astype(jnp.float32)) + laurel_out) * (
        1.0 / math.sqrt(2.0)
    )
    gate_act = jnp.dot(mixture.astype(jnp.bfloat16), layer_gate, preferred_element_type=jnp.float32)
    gate_out = (jax.nn.gelu(gate_act, approximate=True) * extra_input.astype(jnp.float32)).astype(
        jnp.bfloat16
    )
    return (
        mixture
        + normed(
            jnp.dot(gate_out, layer_proj, preferred_element_type=jnp.float32),
            layer_gain.astype(jnp.float32),
        )
    ).astype(jnp.bfloat16)


def schedule_table(distances, lengths):
    ids = jnp.arange(P_DEV, dtype=jnp.int32)
    before = (distances[None, :] < distances[:, None]) | (
        (distances[None, :] == distances[:, None]) & (ids[None, :] < ids[:, None])
    )
    rank = jnp.sum(before.astype(jnp.int32), axis=1)
    chosen = rank[:, None] == ids[None, :]
    order = jnp.sum(jnp.where(chosen, ids[:, None], 0), axis=0)
    slot = jnp.sum(jnp.where(chosen, distances[:, None], 0), axis=0)
    length = jnp.sum(jnp.where(chosen, lengths[:, None], 0), axis=0)
    minus = jnp.full((1,), -1, jnp.int32)
    first = (slot != jnp.concatenate([minus, slot[:-1]])).astype(jnp.int32)
    last = (slot != jnp.concatenate([slot[1:], minus])).astype(jnp.int32)
    return order, slot, length, first, last


def stage_table(sorted_rows, kv_head, low, high):
    order, slot, length, first, last = sorted_rows
    ids = jnp.arange(P_DEV, dtype=jnp.int32)
    start = jnp.sum((slot < low).astype(jnp.int32))
    count = jnp.sum(((slot >= low) & (slot <= high)).astype(jnp.int32))
    active = (ids < count).astype(jnp.int32)
    where = jnp.clip(start + jnp.minimum(ids, jnp.maximum(count, 1) - 1), 0, P_DEV - 1)
    rows = [jnp.take(x, where) for x in (order, slot - low, length, first, last)]
    kv_row = jnp.full((P_DEV,), kv_head, jnp.int32)
    return jnp.concatenate(rows + [active, kv_row]).astype(jnp.int32)


def body(
    tokens,
    layer_input,
    input_gain,
    q_weight,
    k_weight,
    v_weight,
    q_gain,
    k_gain,
    o_weight,
    attn_gain,
    laurel_left,
    laurel_right,
    laurel_gain,
    layer_gate,
    layer_proj,
    layer_gain,
    piece_keys,
    piece_values,
    piece_owner,
    piece_len,
    cache_keys,
    cache_values,
    cache_len,
):
    req_count = lax.axis_size("req")
    tp_count = lax.axis_size("tp")
    req_index = lax.axis_index("req")
    tp_index = lax.axis_index("tp")
    local_heads = H // tp_count
    kv_head = tp_index * local_heads // (H // KVH)
    full_o_weight = lax.all_gather(o_weight, "tp", axis=0, tiled=True)
    tok_float = tokens.astype(jnp.float32)
    tok_norm = normed(tok_float, input_gain.astype(jnp.float32)).astype(jnp.bfloat16)
    queries = jnp.dot(tok_norm, q_weight, preferred_element_type=jnp.float32).reshape(
        ROWS, local_heads, HD
    )
    queries = (
        normed(queries, q_gain.astype(jnp.float32))
        .astype(jnp.bfloat16)
        .reshape(ROWS, local_heads * HD)
    )
    key_cols = lax.dynamic_slice_in_dim(k_weight, kv_head * HD, HD, 1)
    value_cols = lax.dynamic_slice_in_dim(v_weight, kv_head * HD, HD, 1)
    new_keys = normed(
        jnp.dot(tok_norm, key_cols, preferred_element_type=jnp.float32), k_gain.astype(jnp.float32)
    ).astype(jnp.bfloat16)
    new_values = normed(
        jnp.dot(tok_norm, value_cols, preferred_element_type=jnp.float32), 1.0
    ).astype(jnp.bfloat16)
    own_block = queries[:CH]
    half = P_DEV // 2
    far_windows = [passed_along(own_block, "req", d) for d in range(half, P_DEV)]
    held, late_weight = lax.optimization_barrier((own_block, o_weight, *far_windows))[:2]
    near_windows = [passed_along(held, "req", d) for d in range(1, half)]
    self_sum, self_stat = self_attention(own_block, new_keys[:CH], new_values[:CH])

    owners = lax.dynamic_slice_in_dim(piece_owner, req_index * P_DEV, P_DEV)
    lengths = lax.dynamic_slice_in_dim(piece_len, req_index * P_DEV, P_DEV)
    distances = (req_index - owners + req_count) % req_count
    sorted_rows = schedule_table(distances, lengths)
    own = piece_attention(
        stage_table(sorted_rows, kv_head, 0, 0), [own_block], piece_keys, piece_values, self_stat
    )
    far = piece_attention(
        stage_table(sorted_rows, kv_head, half, P_DEV - 1), far_windows,
        piece_keys, piece_values, own[0],
    )
    far_back = [passed_along(far[d - half], "req", -d) for d in range(half, P_DEV)]
    near = piece_attention(
        stage_table(sorted_rows, kv_head, 1, half - 1), near_windows,
        piece_keys, piece_values, far[0],
    )
    near_back = [passed_along(near[d - 1], "req", -d) for d in range(1, half)]
    slots = [own[0]] + near_back + far_back

    block_ids = (req_index + jnp.arange(P_DEV, dtype=jnp.int32)) % req_count
    block_owners = jnp.take(piece_owner.reshape(req_count, P_DEV), block_ids, axis=0)
    has = jnp.any(block_owners == req_index, axis=1).astype(jnp.int32)
    span_att = combine(has, slots, self_sum, self_stat)
    decode_q = queries[CH:].reshape(DEC_DEV, local_heads, HD)
    cache_key = lax.dynamic_slice_in_dim(cache_keys, kv_head * HD, HD, 2)
    cache_value = lax.dynamic_slice_in_dim(cache_values, kv_head * HD, HD, 2)
    cache_scores = (
        jnp.einsum("thd,tjd->thj", decode_q, cache_key, preferred_element_type=jnp.float32)
        * SCORE_SCALE
    )
    cache_valid = (
        lax.broadcasted_iota(jnp.int32, (DEC_DEV, 1, DCACHE), 2) < cache_len[:, None, None]
    )
    cache_scores = jnp.where(cache_valid, cache_scores, LOWEST)
    own_scores = (
        jnp.einsum("thd,td->th", decode_q, new_keys[CH:], preferred_element_type=jnp.float32)
        * SCORE_SCALE
    )
    decode_top = jnp.maximum(jnp.max(cache_scores, axis=-1), own_scores)
    cache_exp = jnp.exp(cache_scores - decode_top[:, :, None])
    own_exp = jnp.exp(own_scores - decode_top)
    decode_total = jnp.sum(cache_exp, axis=-1) + own_exp
    decode_sum = (
        jnp.einsum(
            "thj,tjd->thd",
            cache_exp.astype(jnp.bfloat16),
            cache_value,
            preferred_element_type=jnp.float32,
        )
        + rounded(own_exp).astype(jnp.float32)[:, :, None]
        * new_values[CH:].astype(jnp.float32)[:, None, :]
    )
    decode_att = (
        (decode_sum / decode_total[:, :, None])
        .reshape(DEC_DEV, local_heads * HD)
        .astype(jnp.bfloat16)
    )
    attended = jnp.concatenate([span_att, decode_att], axis=0)
    part = CH // tp_count

    def rows_of(x, owner):
        return jnp.concatenate(
            [lax.dynamic_slice_in_dim(x, owner * part, part, 0), x[CH:]], axis=0
        )

    proj_sum = jnp.dot(rows_of(attended, tp_index), o_weight, preferred_element_type=jnp.float32)
    for shift in range(1, tp_count):
        target = (tp_index + shift) % tp_count
        got_rows = passed_along(rows_of(attended, target), "tp", shift)
        got_weight = passed_along(late_weight, "tp", shift)
        proj_sum = proj_sum + jnp.dot(got_rows, got_weight, preferred_element_type=jnp.float32)
    mine = finish_rows(
        proj_sum,
        rows_of(tok_float, tp_index),
        rows_of(tok_norm, tp_index),
        rows_of(layer_input, tp_index),
        attn_gain,
        laurel_left,
        laurel_right,
        laurel_gain,
        layer_gate,
        layer_proj,
        layer_gain,
    )
    gathered = [mine] + [passed_along(mine, "tp", shift) for shift in range(1, tp_count)]

    def assemble(me):
        def build(*got):
            blocks = [got[(me - owner) % tp_count][:part] for owner in range(tp_count)]
            return jnp.concatenate(blocks + [got[me][part:]], axis=0)

        return build

    return lax.switch(tp_index, [assemble(me) for me in range(tp_count)], *gathered)


def solution(mesh):
    placed = (
        P("req", None),
        P("req", None),
        P(),
        P(None, "tp"),
        P(),
        P(),
        P(),
        P(),
        P("tp", None),
        P(),
        P(),
        P(),
        P(),
        P(),
        P(),
        P(),
        P("req", None, None),
        P("req", None, None),
        P(),
        P(),
        P("req", None, None),
        P("req", None, None),
        P("req"),
    )
    return jax.shard_map(
        body, mesh=mesh, in_specs=placed, out_specs=P("req", None), check_vma=False
    )
```

```python
import functools
import math

import jax
import jax.numpy as jnp
from jax import lax
from jax.experimental import pallas as pl
from jax.experimental.pallas import tpu as pltpu
from jax.sharding import PartitionSpec as P


H = 8
KVH = 2
HD = 256
CH = 512
DEC_DEV = 4
P_DEV = 8
PIECE = 1024
DCACHE = 512
ROWS = 516
STAT = 128
STAT_ROWS = 16
CHUNK = 256


LOWEST = -1e30
SCORE_SCALE = 1.0 / math.sqrt(HD)


def passed_along(x, axis, by):
    length = lax.axis_size(axis)
    return lax.ppermute(x, axis, [(i, (i + by) % length) for i in range(length)])


def rounded(x):
    return lax.optimization_barrier(x.astype(jnp.bfloat16))


def normed(x, scale_gain):
    return x * lax.rsqrt(jnp.mean(x * x, axis=-1, keepdims=True) + 1e-06) * scale_gain


def head_partial(q, keys, values, valid):
    scores = lax.dot_general(q, keys, (((1,), (1,)), ((), ())), preferred_element_type=jnp.float32)
    scores = jnp.where(valid, scores, LOWEST)
    top = jnp.max(scores, axis=1, keepdims=True)
    weights = jnp.exp((scores - top) * SCORE_SCALE)
    total = jnp.sum(weights, axis=1, keepdims=True)
    summed = jnp.dot(weights.astype(jnp.bfloat16), values, preferred_element_type=jnp.float32)
    return top * SCORE_SCALE, total, summed


def split3(x):
    hi = x.astype(jnp.bfloat16).astype(jnp.float32)
    rest = x - hi
    mid = rest.astype(jnp.bfloat16).astype(jnp.float32)
    lo = rest - mid
    return hi, mid, lo


def piece_kernel(slots, tab_ref, *refs):
    q_refs = refs[:slots]
    k_ref, v_ref = refs[slots:slots + 2]
    out_refs = refs[slots + 3:2 * slots + 3]
    scratch = refs[2 * slots + 3:]
    step = pl.program_id(0)

    @pl.when(tab_ref[5 * P_DEV + step] == 1)
    def _():
        piece_step(step, tab_ref, q_refs, k_ref, v_ref, out_refs, *scratch)


def piece_step(step, tab_ref, q_refs, k_ref, v_ref, out_refs, qbuf, fin, acc_m, acc_l, acc_n, sbuf, lbuf, nbuf):
    slots = len(q_refs)
    slot = tab_ref[P_DEV + step]
    length = tab_ref[2 * P_DEV + step]
    first = tab_ref[3 * P_DEV + step]
    last = tab_ref[4 * P_DEV + step]
    for k in range(slots):

        @pl.when(slot == k)
        def _(k=k):
            qbuf[...] = q_refs[k][...]

    rows = qbuf.shape[0]
    chunks = (length + CHUNK - 1) // CHUNK
    for h in range(2):
        q = qbuf[:, h * HD:(h + 1) * HD]

        def score_chunk(c, top, q=q):
            start = pl.multiple_of(c * CHUNK, CHUNK)
            scores = lax.dot_general(
                q, k_ref[0, pl.ds(start, CHUNK), :], (((1,), (1,)), ((), ())),
                preferred_element_type=jnp.float32,
            )
            valid = lax.broadcasted_iota(jnp.int32, (rows, CHUNK), 1) + start < length
            scores = jnp.where(valid, scores, LOWEST)
            sbuf[c] = scores
            return jnp.maximum(top, jnp.max(scores, axis=1, keepdims=True))

        top = lax.fori_loop(0, chunks, score_chunk, jnp.full((rows, 1), LOWEST, jnp.float32))
        lbuf[...] = jnp.zeros_like(lbuf)
        nbuf[...] = jnp.zeros_like(nbuf)

        @pl.loop(0, chunks)
        def _(c, top=top):
            start = pl.multiple_of(c * CHUNK, CHUNK)
            weights = jnp.exp((sbuf[c] - top) * SCORE_SCALE)
            lbuf[...] += jnp.sum(weights, axis=1, keepdims=True)
            nbuf[...] += jnp.dot(
                weights.astype(jnp.bfloat16), v_ref[0, pl.ds(start, CHUNK), :],
                preferred_element_type=jnp.float32,
            )

        top = top * SCORE_SCALE

        @pl.when(first == 1)
        def _(h=h, top=top):
            acc_m[h] = top
            acc_l[h] = lbuf[...]
            acc_n[h] = nbuf[...]

        @pl.when(first == 0)
        def _(h=h, top=top):
            old = acc_m[h]
            new = jnp.maximum(old, top)
            keep = jnp.exp(old - new)
            add = jnp.exp(top - new)
            acc_l[h] = acc_l[h] * keep + lbuf[...] * add
            acc_n[h] = acc_n[h] * keep + nbuf[...] * add
            acc_m[h] = new

    @pl.when(last == 1)
    def _():
        lane = lax.broadcasted_iota(jnp.int32, (rows, STAT), 1)
        stat = jnp.zeros((rows, STAT), jnp.float32)
        for h in range(2):
            total = acc_l[h]
            fin[:rows, h * HD:(h + 1) * HD] = (acc_n[h] / total).astype(jnp.bfloat16)
            for i, part in enumerate(split3(acc_m[h]) + split3(total)):
                stat = jnp.where(lane == 8 * h + i, part, stat)
        fin[rows:, :] = jnp.transpose(stat)[:STAT_ROWS].astype(jnp.bfloat16)
        for k in range(slots):

            @pl.when(slot == k)
            def _(k=k):
                out_refs[k][...] = fin[...]


def piece_attention(table, windows, piece_keys, piece_values, after):
    rows = windows[0].shape[0]
    slots = len(windows)
    q_spec = pl.BlockSpec((rows, 2 * HD), lambda s, t: (0, 0))
    kv_spec = pl.BlockSpec((1, PIECE, HD), lambda s, t: (t[s], 0, t[6 * P_DEV]))
    out_spec = pl.BlockSpec((rows + STAT_ROWS, 2 * HD), lambda s, t: (0, 0))
    grid_spec = pltpu.PrefetchScalarGridSpec(
        num_scalar_prefetch=1,
        grid=(P_DEV,),
        in_specs=[q_spec] * slots + [kv_spec, kv_spec, pl.BlockSpec(memory_space=pl.ANY)],
        out_specs=[out_spec] * slots,
        scratch_shapes=[
            pltpu.VMEM((rows, 2 * HD), jnp.bfloat16),
            pltpu.VMEM((rows + STAT_ROWS, 2 * HD), jnp.bfloat16),
            pltpu.VMEM((2, rows, 1), jnp.float32),
            pltpu.VMEM((2, rows, 1), jnp.float32),
            pltpu.VMEM((2, rows, HD), jnp.float32),
            pltpu.VMEM((PIECE // CHUNK, rows, CHUNK), jnp.float32),
            pltpu.VMEM((rows, 1), jnp.float32),
            pltpu.VMEM((rows, HD), jnp.float32),
        ],
    )
    pieces = P_DEV // 2
    flops = pieces * 2 * 2 * 2 * rows * PIECE * HD
    return pl.pallas_call(
        functools.partial(piece_kernel, slots),
        grid_spec=grid_spec,
        out_shape=[jax.ShapeDtypeStruct((rows + STAT_ROWS, 2 * HD), jnp.bfloat16)] * slots,
        compiler_params=pltpu.CompilerParams(
            dimension_semantics=("arbitrary",), vmem_limit_bytes=48 * 1024 * 1024
        ),
        cost_estimate=pl.CostEstimate(
            flops=flops,
            transcendentals=pieces * 2 * rows * PIECE,
            bytes_accessed=pieces * 2 * PIECE * HD * 2 + slots * rows * 2 * HD * 2 * 2,
        ),
    )(table, *windows, piece_keys, piece_values, after)


def self_kernel(q_ref, k_ref, v_ref, n_ref, stat_ref):
    rows = q_ref.shape[0]
    valid = lax.broadcasted_iota(jnp.int32, (rows, rows), 1) <= lax.broadcasted_iota(
        jnp.int32, (rows, rows), 0
    )
    lane = lax.broadcasted_iota(jnp.int32, (rows, STAT), 1)
    stat = jnp.zeros((rows, STAT), jnp.float32)
    keys = k_ref[...]
    values = v_ref[...]
    for h in range(2):
        top, total, summed = head_partial(q_ref[:, h * HD:(h + 1) * HD], keys, values, valid)
        n_ref[:, h * HD:(h + 1) * HD] = summed
        stat = jnp.where(lane == 8 * h, top, stat)
        stat = jnp.where(lane == 8 * h + 3, total, stat)
    stat_ref[...] = stat


def self_attention(q, keys, values):
    rows = q.shape[0]
    return pl.pallas_call(
        self_kernel,
        out_shape=(
            jax.ShapeDtypeStruct((rows, 2 * HD), jnp.float32),
            jax.ShapeDtypeStruct((rows, STAT), jnp.float32),
        ),
        compiler_params=pltpu.CompilerParams(vmem_limit_bytes=48 * 1024 * 1024),
        cost_estimate=pl.CostEstimate(
            flops=2 * 2 * 2 * rows * rows * HD,
            transcendentals=2 * rows * rows,
            bytes_accessed=rows * 2 * HD * 2 + 2 * rows * HD * 2 + rows * (2 * HD + STAT) * 4,
        ),
    )(q, keys, values)


def combine_kernel(has_ref, *refs):
    slot_refs = refs[:P_DEV]
    row_refs = refs[P_DEV:2 * P_DEV]
    sum_ref, stat_ref, out_ref = refs[2 * P_DEV:]
    rows = out_ref.shape[0]
    lane = lax.broadcasted_iota(jnp.int32, (rows, STAT), 1)
    near_stat = stat_ref[...]
    pad = jnp.zeros((STAT - STAT_ROWS, rows), jnp.float32)
    stats = [
        jnp.transpose(jnp.concatenate([row_refs[d][...].astype(jnp.float32), pad], axis=0))
        for d in range(P_DEV)
    ]

    def pick(stat, first, count):
        chosen = (lane >= first) & (lane < first + count)
        return jnp.sum(jnp.where(chosen, stat, 0.0), axis=1, keepdims=True)

    for h in range(2):
        tops = [pick(stats[d], 8 * h, 3) for d in range(P_DEV)]
        totals = [pick(stats[d], 8 * h + 3, 3) for d in range(P_DEV)]
        far_top = jnp.full((rows, 1), LOWEST, jnp.float32)
        for d in range(P_DEV):
            far_top = jnp.maximum(far_top, jnp.where(has_ref[d] == 1, tops[d], LOWEST))
        far_total = jnp.zeros((rows, 1), jnp.float32)
        far_sum = jnp.zeros((rows, HD), jnp.float32)
        for d in range(P_DEV):
            live = has_ref[d] == 1
            weight = jnp.where(live, totals[d] * jnp.exp(tops[d] - far_top), 0.0)
            far_total = far_total + weight
            block = slot_refs[d][:, h * HD:(h + 1) * HD].astype(jnp.float32)
            far_sum = far_sum + jnp.where(live, weight * block, 0.0)
        near_top = pick(near_stat, 8 * h, 1)
        near_total = pick(near_stat, 8 * h + 3, 1)
        final_top = jnp.maximum(far_top, near_top)
        far_scale = jnp.exp(far_top - final_top)
        near_scale = jnp.exp(near_top - final_top)
        near_sum = sum_ref[:, h * HD:(h + 1) * HD]
        out_ref[:, h * HD:(h + 1) * HD] = (
            (far_sum * far_scale + near_sum * near_scale)
            / (far_total * far_scale + near_total * near_scale)
        ).astype(out_ref.dtype)


def combine(has, slots, self_sum, self_stat):
    rows = self_sum.shape[0]
    tile = 128
    slot_spec = pl.BlockSpec((tile, 2 * HD), lambda i, t: (i, 0))
    row_spec = pl.BlockSpec((STAT_ROWS, tile), lambda i, t: (rows // STAT_ROWS, i))
    grid_spec = pltpu.PrefetchScalarGridSpec(
        num_scalar_prefetch=1,
        grid=(rows // tile,),
        in_specs=[slot_spec] * P_DEV
        + [row_spec] * P_DEV
        + [
            pl.BlockSpec((tile, 2 * HD), lambda i, t: (i, 0)),
            pl.BlockSpec((tile, STAT), lambda i, t: (i, 0)),
        ],
        out_specs=pl.BlockSpec((tile, 2 * HD), lambda i, t: (i, 0)),
    )
    return pl.pallas_call(
        combine_kernel,
        grid_spec=grid_spec,
        out_shape=jax.ShapeDtypeStruct((rows, 2 * HD), jnp.bfloat16),
        compiler_params=pltpu.CompilerParams(dimension_semantics=("arbitrary",)),
        cost_estimate=pl.CostEstimate(
            flops=rows * 2 * HD * 3 * P_DEV,
            transcendentals=rows * 2 * P_DEV,
            bytes_accessed=P_DEV * (rows + STAT_ROWS) * 2 * HD * 2 + rows * (2 * HD + STAT) * 4 + rows * 2 * HD * 2,
        ),
    )(has, *slots, *slots, self_sum, self_stat)


def finish_rows(
    proj_sum,
    tok_float,
    tok_norm,
    extra_input,
    attn_gain,
    laurel_left,
    laurel_right,
    laurel_gain,
    layer_gate,
    layer_proj,
    layer_gain,
):
    laurel_low = jnp.dot(tok_norm, laurel_left, preferred_element_type=jnp.float32).astype(
        jnp.bfloat16
    )
    laurel_out = tok_norm.astype(jnp.float32) + normed(
        jnp.dot(laurel_low, laurel_right, preferred_element_type=jnp.float32),
        laurel_gain.astype(jnp.float32),
    )
    mixture = (tok_float + normed(proj_sum, attn_gain.astype(jnp.float32)) + laurel_out) * (
        1.0 / math.sqrt(2.0)
    )
    gate_act = jnp.dot(mixture.astype(jnp.bfloat16), layer_gate, preferred_element_type=jnp.float32)
    gate_out = (jax.nn.gelu(gate_act, approximate=True) * extra_input.astype(jnp.float32)).astype(
        jnp.bfloat16
    )
    return (
        mixture
        + normed(
            jnp.dot(gate_out, layer_proj, preferred_element_type=jnp.float32),
            layer_gain.astype(jnp.float32),
        )
    ).astype(jnp.bfloat16)


def schedule_table(distances, lengths):
    ids = jnp.arange(P_DEV, dtype=jnp.int32)
    before = (distances[None, :] < distances[:, None]) | (
        (distances[None, :] == distances[:, None]) & (ids[None, :] < ids[:, None])
    )
    rank = jnp.sum(before.astype(jnp.int32), axis=1)
    chosen = rank[:, None] == ids[None, :]
    order = jnp.sum(jnp.where(chosen, ids[:, None], 0), axis=0)
    slot = jnp.sum(jnp.where(chosen, distances[:, None], 0), axis=0)
    length = jnp.sum(jnp.where(chosen, lengths[:, None], 0), axis=0)
    minus = jnp.full((1,), -1, jnp.int32)
    first = (slot != jnp.concatenate([minus, slot[:-1]])).astype(jnp.int32)
    last = (slot != jnp.concatenate([slot[1:], minus])).astype(jnp.int32)
    return order, slot, length, first, last


def stage_table(sorted_rows, kv_head, low, high):
    order, slot, length, first, last = sorted_rows
    ids = jnp.arange(P_DEV, dtype=jnp.int32)
    start = jnp.sum((slot < low).astype(jnp.int32))
    count = jnp.sum(((slot >= low) & (slot <= high)).astype(jnp.int32))
    active = (ids < count).astype(jnp.int32)
    where = jnp.clip(start + jnp.minimum(ids, jnp.maximum(count, 1) - 1), 0, P_DEV - 1)
    rows = [jnp.take(x, where) for x in (order, slot - low, length, first, last)]
    kv_row = jnp.full((P_DEV,), kv_head, jnp.int32)
    return jnp.concatenate(rows + [active, kv_row]).astype(jnp.int32)


def layer(
    tokens,
    layer_input,
    input_gain,
    q_weight,
    k_weight,
    v_weight,
    q_gain,
    k_gain,
    o_weight,
    attn_gain,
    laurel_left,
    laurel_right,
    laurel_gain,
    layer_gate,
    layer_proj,
    layer_gain,
    piece_keys,
    piece_values,
    piece_owner,
    piece_len,
    cache_keys,
    cache_values,
    cache_len,
):
    req_count = lax.axis_size("req")
    tp_count = lax.axis_size("tp")
    req_index = lax.axis_index("req")
    tp_index = lax.axis_index("tp")
    local_heads = H // tp_count
    kv_head = tp_index * local_heads // (H // KVH)
    full_o_weight = lax.all_gather(o_weight, "tp", axis=0, tiled=True)
    tok_float = tokens.astype(jnp.float32)
    tok_norm = normed(tok_float, input_gain.astype(jnp.float32)).astype(jnp.bfloat16)
    queries = jnp.dot(tok_norm, q_weight, preferred_element_type=jnp.float32).reshape(
        ROWS, local_heads, HD
    )
    queries = (
        normed(queries, q_gain.astype(jnp.float32))
        .astype(jnp.bfloat16)
        .reshape(ROWS, local_heads * HD)
    )
    key_cols = lax.dynamic_slice_in_dim(k_weight, kv_head * HD, HD, 1)
    value_cols = lax.dynamic_slice_in_dim(v_weight, kv_head * HD, HD, 1)
    new_keys = normed(
        jnp.dot(tok_norm, key_cols, preferred_element_type=jnp.float32), k_gain.astype(jnp.float32)
    ).astype(jnp.bfloat16)
    new_values = normed(
        jnp.dot(tok_norm, value_cols, preferred_element_type=jnp.float32), 1.0
    ).astype(jnp.bfloat16)
    own_block = queries[:CH]
    self_sum, self_stat = self_attention(own_block, new_keys[:CH], new_values[:CH])
    owners = lax.dynamic_slice_in_dim(piece_owner, req_index * P_DEV, P_DEV)
    lengths = lax.dynamic_slice_in_dim(piece_len, req_index * P_DEV, P_DEV)
    distances = (req_index - owners + req_count) % req_count
    sorted_rows = schedule_table(distances, lengths)
    own = piece_attention(
        stage_table(sorted_rows, kv_head, 0, 0), [own_block], piece_keys, piece_values, self_stat
    )
    slots = [own[0]] + [None] * (P_DEV - 1)
    weight_hold = o_weight
    after = own[0]
    for low, high in STAGES:
        windows = [passed_along(own_block, "req", d) for d in range(low, high + 1)]
        stage = piece_attention(
            stage_table(sorted_rows, kv_head, low, high), windows, piece_keys, piece_values, after
        )
        after = stage[0]
        for d in range(low, high + 1):
            slots[d] = passed_along(stage[d - low], "req", -d)
    late_weight = weight_hold

    block_ids = (req_index + jnp.arange(P_DEV, dtype=jnp.int32)) % req_count
    block_owners = jnp.take(piece_owner.reshape(req_count, P_DEV), block_ids, axis=0)
    has = jnp.any(block_owners == req_index, axis=1).astype(jnp.int32)
    span_att = combine(has, slots, self_sum, self_stat)
    decode_q = queries[CH:].reshape(DEC_DEV, local_heads, HD)
    cache_key = lax.dynamic_slice_in_dim(cache_keys, kv_head * HD, HD, 2)
    cache_value = lax.dynamic_slice_in_dim(cache_values, kv_head * HD, HD, 2)
    cache_scores = (
        jnp.einsum("thd,tjd->thj", decode_q, cache_key, preferred_element_type=jnp.float32)
        * SCORE_SCALE
    )
    cache_valid = (
        lax.broadcasted_iota(jnp.int32, (DEC_DEV, 1, DCACHE), 2) < cache_len[:, None, None]
    )
    cache_scores = jnp.where(cache_valid, cache_scores, LOWEST)
    own_scores = (
        jnp.einsum("thd,td->th", decode_q, new_keys[CH:], preferred_element_type=jnp.float32)
        * SCORE_SCALE
    )
    decode_top = jnp.maximum(jnp.max(cache_scores, axis=-1), own_scores)
    cache_exp = jnp.exp(cache_scores - decode_top[:, :, None])
    own_exp = jnp.exp(own_scores - decode_top)
    decode_total = jnp.sum(cache_exp, axis=-1) + own_exp
    decode_sum = (
        jnp.einsum(
            "thj,tjd->thd",
            cache_exp.astype(jnp.bfloat16),
            cache_value,
            preferred_element_type=jnp.float32,
        )
        + rounded(own_exp).astype(jnp.float32)[:, :, None]
        * new_values[CH:].astype(jnp.float32)[:, None, :]
    )
    decode_att = (
        (decode_sum / decode_total[:, :, None])
        .reshape(DEC_DEV, local_heads * HD)
        .astype(jnp.bfloat16)
    )
    attended = jnp.concatenate([span_att, decode_att], axis=0)
    part = CH // tp_count

    def rows_of(x, owner):
        return jnp.concatenate(
            [lax.dynamic_slice_in_dim(x, owner * part, part, 0), x[CH:]], axis=0
        )

    proj_sum = jnp.dot(rows_of(attended, tp_index), o_weight, preferred_element_type=jnp.float32)
    for shift in range(1, tp_count):
        target = (tp_index + shift) % tp_count
        got_rows = passed_along(rows_of(attended, target), "tp", shift)
        got_weight = passed_along(late_weight, "tp", shift)
        proj_sum = proj_sum + jnp.dot(got_rows, got_weight, preferred_element_type=jnp.float32)
    mine = finish_rows(
        proj_sum,
        rows_of(tok_float, tp_index),
        rows_of(tok_norm, tp_index),
        rows_of(layer_input, tp_index),
        attn_gain,
        laurel_left,
        laurel_right,
        laurel_gain,
        layer_gate,
        layer_proj,
        layer_gain,
    )
    gathered = [mine] + [passed_along(mine, "tp", shift) for shift in range(1, tp_count)]

    def assemble(me):
        def build(*got):
            blocks = [got[(me - owner) % tp_count][:part] for owner in range(tp_count)]
            return jnp.concatenate(blocks + [got[me][part:]], axis=0)

        return build

    return lax.switch(tp_index, [assemble(me) for me in range(tp_count)], *gathered)


STAGES = ((6, 7), (4, 5), (1, 3))


def solution(mesh):
    placed = (
        P("req", None),
        P("req", None),
        P(),
        P(None, "tp"),
        P(),
        P(),
        P(),
        P(),
        P("tp", None),
        P(),
        P(),
        P(),
        P(),
        P(),
        P(),
        P(),
        P("req", None, None),
        P("req", None, None),
        P(),
        P(),
        P("req", None, None),
        P("req", None, None),
        P("req"),
    )
    return jax.shard_map(
        layer, mesh=mesh, in_specs=placed, out_specs=P("req", None), check_vma=False
    )
```

```python
import functools
import math

import jax
import jax.numpy as jnp
from jax import lax
from jax.experimental import pallas as pl
from jax.experimental.pallas import tpu as pltpu
from jax.sharding import PartitionSpec as P

H = 8
KVH = 2
HD = 256
CH = 512
DEC_DEV = 4
P_DEV = 8
PIECE = 1024
DCACHE = 512
ROWS = 516
STAT = 128
CHUNK = 256


LOWEST = -1e30
SCORE_SCALE = 1.0 / math.sqrt(HD)


def passed_along(x, axis, by):
    length = lax.axis_size(axis)
    return lax.ppermute(x, axis, [(i, (i + by) % length) for i in range(length)])


def rounded(x):
    return lax.optimization_barrier(x.astype(jnp.bfloat16))


def normed(x, scale_gain):
    return x * lax.rsqrt(jnp.mean(x * x, axis=-1, keepdims=True) + 1e-06) * scale_gain


def head_partial(q, keys, values, valid):
    scores = lax.dot_general(q, keys, (((1,), (1,)), ((), ())), preferred_element_type=jnp.float32)
    scores = jnp.where(valid, scores, LOWEST)
    top = jnp.max(scores, axis=1, keepdims=True)
    weights = jnp.exp((scores - top) * SCORE_SCALE)
    total = jnp.sum(weights, axis=1, keepdims=True)
    summed = jnp.dot(weights.astype(jnp.bfloat16), values, preferred_element_type=jnp.float32)
    return top * SCORE_SCALE, total, summed


def split3(x):
    hi = x.astype(jnp.bfloat16).astype(jnp.float32)
    rest = x - hi
    mid = rest.astype(jnp.bfloat16).astype(jnp.float32)
    lo = rest - mid
    return hi, mid, lo


def piece_kernel(slots, tab_ref, *refs):
    q_refs = refs[:slots]
    k_ref, v_ref = refs[slots:slots + 2]
    out_refs = refs[slots + 3:2 * slots + 3]
    scratch = refs[2 * slots + 3:]
    step = pl.program_id(0)

    @pl.when(tab_ref[5 * P_DEV + step] == 1)
    def _():
        piece_step(step, tab_ref, q_refs, k_ref, v_ref, out_refs, *scratch)


def piece_step(step, tab_ref, q_refs, k_ref, v_ref, out_refs, qbuf, fin, acc_m, acc_l, acc_n, sbuf, lbuf, nbuf):
    slots = len(q_refs)
    slot = tab_ref[P_DEV + step]
    length = tab_ref[2 * P_DEV + step]
    first = tab_ref[3 * P_DEV + step]
    last = tab_ref[4 * P_DEV + step]
    for k in range(slots):

        @pl.when(slot == k)
        def _(k=k):
            qbuf[...] = q_refs[k][...]

    rows = qbuf.shape[0]
    chunks = (length + CHUNK - 1) // CHUNK
    for h in range(2):
        q = qbuf[:, h * HD:(h + 1) * HD]

        def score_chunk(c, top, q=q):
            start = pl.multiple_of(c * CHUNK, CHUNK)
            scores = lax.dot_general(
                q, k_ref[0, pl.ds(start, CHUNK), :], (((1,), (1,)), ((), ())),
                preferred_element_type=jnp.float32,
            )
            valid = lax.broadcasted_iota(jnp.int32, (rows, CHUNK), 1) + start < length
            scores = jnp.where(valid, scores, LOWEST)
            sbuf[c] = scores
            return jnp.maximum(top, jnp.max(scores, axis=1, keepdims=True))

        top = lax.fori_loop(0, chunks, score_chunk, jnp.full((rows, 1), LOWEST, jnp.float32))
        lbuf[...] = jnp.zeros_like(lbuf)
        nbuf[...] = jnp.zeros_like(nbuf)

        @pl.loop(0, chunks)
        def _(c, top=top):
            start = pl.multiple_of(c * CHUNK, CHUNK)
            weights = jnp.exp((sbuf[c] - top) * SCORE_SCALE)
            lbuf[...] += jnp.sum(weights, axis=1, keepdims=True)
            nbuf[...] += jnp.dot(
                weights.astype(jnp.bfloat16), v_ref[0, pl.ds(start, CHUNK), :],
                preferred_element_type=jnp.float32,
            )

        top = top * SCORE_SCALE

        @pl.when(first == 1)
        def _(h=h, top=top):
            acc_m[h] = top
            acc_l[h] = lbuf[...]
            acc_n[h] = nbuf[...]

        @pl.when(first == 0)
        def _(h=h, top=top):
            old = acc_m[h]
            new = jnp.maximum(old, top)
            keep = jnp.exp(old - new)
            add = jnp.exp(top - new)
            acc_l[h] = acc_l[h] * keep + lbuf[...] * add
            acc_n[h] = acc_n[h] * keep + nbuf[...] * add
            acc_m[h] = new

    @pl.when(last == 1)
    def _():
        lane = lax.broadcasted_iota(jnp.int32, (rows, STAT), 1)
        stat = jnp.zeros((rows, STAT), jnp.float32)
        for h in range(2):
            total = acc_l[h]
            fin[:, h * HD:(h + 1) * HD] = (acc_n[h] / total).astype(jnp.bfloat16)
            for i, part in enumerate(split3(acc_m[h]) + split3(total)):
                stat = jnp.where(lane == 8 * h + i, part, stat)
        fin[:, 2 * HD:] = stat.astype(jnp.bfloat16)
        for k in range(slots):

            @pl.when(slot == k)
            def _(k=k):
                out_refs[k][...] = fin[...]


def piece_attention(table, windows, piece_keys, piece_values, after):
    rows = windows[0].shape[0]
    slots = len(windows)
    q_spec = pl.BlockSpec((rows, 2 * HD), lambda s, t: (0, 0))
    kv_spec = pl.BlockSpec((1, PIECE, HD), lambda s, t: (t[s], 0, t[6 * P_DEV]))
    out_spec = pl.BlockSpec((rows, 2 * HD + STAT), lambda s, t: (0, 0))
    grid_spec = pltpu.PrefetchScalarGridSpec(
        num_scalar_prefetch=1,
        grid=(P_DEV,),
        in_specs=[q_spec] * slots + [kv_spec, kv_spec, pl.BlockSpec(memory_space=pl.ANY)],
        out_specs=[out_spec] * slots,
        scratch_shapes=[
            pltpu.VMEM((rows, 2 * HD), jnp.bfloat16),
            pltpu.VMEM((rows, 2 * HD + STAT), jnp.bfloat16),
            pltpu.VMEM((2, rows, 1), jnp.float32),
            pltpu.VMEM((2, rows, 1), jnp.float32),
            pltpu.VMEM((2, rows, HD), jnp.float32),
            pltpu.VMEM((PIECE // CHUNK, rows, CHUNK), jnp.float32),
            pltpu.VMEM((rows, 1), jnp.float32),
            pltpu.VMEM((rows, HD), jnp.float32),
        ],
    )
    pieces = P_DEV // 2
    flops = pieces * 2 * 2 * 2 * rows * PIECE * HD
    return pl.pallas_call(
        functools.partial(piece_kernel, slots),
        grid_spec=grid_spec,
        out_shape=[jax.ShapeDtypeStruct((rows, 2 * HD + STAT), jnp.bfloat16)] * slots,
        compiler_params=pltpu.CompilerParams(
            dimension_semantics=("arbitrary",), vmem_limit_bytes=48 * 1024 * 1024
        ),
        cost_estimate=pl.CostEstimate(
            flops=flops,
            transcendentals=pieces * 2 * rows * PIECE,
            bytes_accessed=pieces * 2 * PIECE * HD * 2 + slots * rows * 2 * HD * 2 * 2,
        ),
    )(table, *windows, piece_keys, piece_values, after)


def self_kernel(q_ref, k_ref, v_ref, n_ref, stat_ref):
    rows = q_ref.shape[0]
    valid = lax.broadcasted_iota(jnp.int32, (rows, rows), 1) <= lax.broadcasted_iota(
        jnp.int32, (rows, rows), 0
    )
    lane = lax.broadcasted_iota(jnp.int32, (rows, STAT), 1)
    stat = jnp.zeros((rows, STAT), jnp.float32)
    keys = k_ref[...]
    values = v_ref[...]
    for h in range(2):
        top, total, summed = head_partial(q_ref[:, h * HD:(h + 1) * HD], keys, values, valid)
        n_ref[:, h * HD:(h + 1) * HD] = summed
        stat = jnp.where(lane == 8 * h, top, stat)
        stat = jnp.where(lane == 8 * h + 3, total, stat)
    stat_ref[...] = stat


def self_attention(q, keys, values):
    rows = q.shape[0]
    return pl.pallas_call(
        self_kernel,
        out_shape=(
            jax.ShapeDtypeStruct((rows, 2 * HD), jnp.float32),
            jax.ShapeDtypeStruct((rows, STAT), jnp.float32),
        ),
        compiler_params=pltpu.CompilerParams(vmem_limit_bytes=48 * 1024 * 1024),
        cost_estimate=pl.CostEstimate(
            flops=2 * 2 * 2 * rows * rows * HD,
            transcendentals=2 * rows * rows,
            bytes_accessed=rows * 2 * HD * 2 + 2 * rows * HD * 2 + rows * (2 * HD + STAT) * 4,
        ),
    )(q, keys, values)


def combine_kernel(has_ref, *refs):
    slot_refs = refs[:P_DEV]
    sum_ref, stat_ref, out_ref = refs[P_DEV:]
    rows = out_ref.shape[0]
    lane = lax.broadcasted_iota(jnp.int32, (rows, STAT), 1)
    near_stat = stat_ref[...]
    stats = [slot_refs[d][:, 2 * HD:].astype(jnp.float32) for d in range(P_DEV)]

    def pick(stat, first, count):
        chosen = (lane >= first) & (lane < first + count)
        return jnp.sum(jnp.where(chosen, stat, 0.0), axis=1, keepdims=True)

    for h in range(2):
        tops = [pick(stats[d], 8 * h, 3) for d in range(P_DEV)]
        totals = [pick(stats[d], 8 * h + 3, 3) for d in range(P_DEV)]
        far_top = jnp.full((rows, 1), LOWEST, jnp.float32)
        for d in range(P_DEV):
            far_top = jnp.maximum(far_top, jnp.where(has_ref[d] == 1, tops[d], LOWEST))
        far_total = jnp.zeros((rows, 1), jnp.float32)
        far_sum = jnp.zeros((rows, HD), jnp.float32)
        for d in range(P_DEV):
            live = has_ref[d] == 1
            weight = jnp.where(live, totals[d] * jnp.exp(tops[d] - far_top), 0.0)
            far_total = far_total + weight
            block = slot_refs[d][:, h * HD:(h + 1) * HD].astype(jnp.float32)
            far_sum = far_sum + jnp.where(live, weight * block, 0.0)
        near_top = pick(near_stat, 8 * h, 1)
        near_total = pick(near_stat, 8 * h + 3, 1)
        final_top = jnp.maximum(far_top, near_top)
        far_scale = jnp.exp(far_top - final_top)
        near_scale = jnp.exp(near_top - final_top)
        near_sum = sum_ref[:, h * HD:(h + 1) * HD]
        out_ref[:, h * HD:(h + 1) * HD] = (
            (far_sum * far_scale + near_sum * near_scale)
            / (far_total * far_scale + near_total * near_scale)
        ).astype(out_ref.dtype)


def combine(has, slots, self_sum, self_stat):
    rows = slots[0].shape[0]
    tile = 128
    slot_spec = pl.BlockSpec((tile, 2 * HD + STAT), lambda i, t: (i, 0))
    grid_spec = pltpu.PrefetchScalarGridSpec(
        num_scalar_prefetch=1,
        grid=(rows // tile,),
        in_specs=[slot_spec] * P_DEV
        + [
            pl.BlockSpec((tile, 2 * HD), lambda i, t: (i, 0)),
            pl.BlockSpec((tile, STAT), lambda i, t: (i, 0)),
        ],
        out_specs=pl.BlockSpec((tile, 2 * HD), lambda i, t: (i, 0)),
    )
    return pl.pallas_call(
        combine_kernel,
        grid_spec=grid_spec,
        out_shape=jax.ShapeDtypeStruct((rows, 2 * HD), jnp.bfloat16),
        compiler_params=pltpu.CompilerParams(dimension_semantics=("arbitrary",)),
        cost_estimate=pl.CostEstimate(
            flops=rows * 2 * HD * 3 * P_DEV,
            transcendentals=rows * 2 * P_DEV,
            bytes_accessed=P_DEV * rows * (2 * HD + STAT) * 2 + rows * (2 * HD + STAT) * 4 + rows * 2 * HD * 2,
        ),
    )(has, *slots, self_sum, self_stat)


def finish_rows(
    proj_sum,
    tok_float,
    tok_norm,
    extra_input,
    attn_gain,
    laurel_left,
    laurel_right,
    laurel_gain,
    layer_gate,
    layer_proj,
    layer_gain,
):
    laurel_low = jnp.dot(tok_norm, laurel_left, preferred_element_type=jnp.float32).astype(
        jnp.bfloat16
    )
    laurel_out = tok_norm.astype(jnp.float32) + normed(
        jnp.dot(laurel_low, laurel_right, preferred_element_type=jnp.float32),
        laurel_gain.astype(jnp.float32),
    )
    mixture = (tok_float + normed(proj_sum, attn_gain.astype(jnp.float32)) + laurel_out) * (
        1.0 / math.sqrt(2.0)
    )
    gate_act = jnp.dot(mixture.astype(jnp.bfloat16), layer_gate, preferred_element_type=jnp.float32)
    gate_out = (jax.nn.gelu(gate_act, approximate=True) * extra_input.astype(jnp.float32)).astype(
        jnp.bfloat16
    )
    return (
        mixture
        + normed(
            jnp.dot(gate_out, layer_proj, preferred_element_type=jnp.float32),
            layer_gain.astype(jnp.float32),
        )
    ).astype(jnp.bfloat16)


def schedule_table(distances, lengths):
    ids = jnp.arange(P_DEV, dtype=jnp.int32)
    before = (distances[None, :] < distances[:, None]) | (
        (distances[None, :] == distances[:, None]) & (ids[None, :] < ids[:, None])
    )
    rank = jnp.sum(before.astype(jnp.int32), axis=1)
    chosen = rank[:, None] == ids[None, :]
    order = jnp.sum(jnp.where(chosen, ids[:, None], 0), axis=0)
    slot = jnp.sum(jnp.where(chosen, distances[:, None], 0), axis=0)
    length = jnp.sum(jnp.where(chosen, lengths[:, None], 0), axis=0)
    minus = jnp.full((1,), -1, jnp.int32)
    first = (slot != jnp.concatenate([minus, slot[:-1]])).astype(jnp.int32)
    last = (slot != jnp.concatenate([slot[1:], minus])).astype(jnp.int32)
    return order, slot, length, first, last


def stage_table(sorted_rows, kv_head, low, high):
    order, slot, length, first, last = sorted_rows
    ids = jnp.arange(P_DEV, dtype=jnp.int32)
    start = jnp.sum((slot < low).astype(jnp.int32))
    count = jnp.sum(((slot >= low) & (slot <= high)).astype(jnp.int32))
    active = (ids < count).astype(jnp.int32)
    where = jnp.clip(start + jnp.minimum(ids, jnp.maximum(count, 1) - 1), 0, P_DEV - 1)
    rows = [jnp.take(x, where) for x in (order, slot - low, length, first, last)]
    kv_row = jnp.full((P_DEV,), kv_head, jnp.int32)
    return jnp.concatenate(rows + [active, kv_row]).astype(jnp.int32)


def body(
    tokens,
    layer_input,
    input_gain,
    q_weight,
    k_weight,
    v_weight,
    q_gain,
    k_gain,
    o_weight,
    attn_gain,
    laurel_left,
    laurel_right,
    laurel_gain,
    layer_gate,
    layer_proj,
    layer_gain,
    piece_keys,
    piece_values,
    piece_owner,
    piece_len,
    cache_keys,
    cache_values,
    cache_len,
):
    req_count = lax.axis_size("req")
    tp_count = lax.axis_size("tp")
    req_index = lax.axis_index("req")
    tp_index = lax.axis_index("tp")
    local_heads = H // tp_count
    kv_head = tp_index * local_heads // (H // KVH)
    full_o_weight = lax.all_gather(o_weight, "tp", axis=0, tiled=True)
    tok_float = tokens.astype(jnp.float32)
    tok_norm = normed(tok_float, input_gain.astype(jnp.float32)).astype(jnp.bfloat16)
    queries = jnp.dot(tok_norm, q_weight, preferred_element_type=jnp.float32).reshape(
        ROWS, local_heads, HD
    )
    queries = (
        normed(queries, q_gain.astype(jnp.float32))
        .astype(jnp.bfloat16)
        .reshape(ROWS, local_heads * HD)
    )
    key_cols = lax.dynamic_slice_in_dim(k_weight, kv_head * HD, HD, 1)
    value_cols = lax.dynamic_slice_in_dim(v_weight, kv_head * HD, HD, 1)
    new_keys = normed(
        jnp.dot(tok_norm, key_cols, preferred_element_type=jnp.float32), k_gain.astype(jnp.float32)
    ).astype(jnp.bfloat16)
    new_values = normed(
        jnp.dot(tok_norm, value_cols, preferred_element_type=jnp.float32), 1.0
    ).astype(jnp.bfloat16)
    own_block = queries[:CH]
    half = P_DEV // 2 + 1
    early = [passed_along(own_block, "req", d) for d in range(1, half)]
    held = lax.optimization_barrier((own_block, *early))[0]
    late = [passed_along(held, "req", d) for d in range(half, P_DEV)]
    self_sum, self_stat = self_attention(own_block, new_keys[:CH], new_values[:CH])

    owners = lax.dynamic_slice_in_dim(piece_owner, req_index * P_DEV, P_DEV)
    lengths = lax.dynamic_slice_in_dim(piece_len, req_index * P_DEV, P_DEV)
    distances = (req_index - owners + req_count) % req_count
    sorted_rows = schedule_table(distances, lengths)
    near = piece_attention(
        stage_table(sorted_rows, kv_head, 0, half - 1), [own_block] + early,
        piece_keys, piece_values, self_stat,
    )
    far = piece_attention(
        stage_table(sorted_rows, kv_head, half, P_DEV - 1), late,
        piece_keys, piece_values, near[0],
    )
    packed = list(near) + list(far)
    slots = [packed[0]] + [passed_along(packed[d], "req", -d) for d in range(1, P_DEV)]

    block_ids = (req_index + jnp.arange(P_DEV, dtype=jnp.int32)) % req_count
    block_owners = jnp.take(piece_owner.reshape(req_count, P_DEV), block_ids, axis=0)
    has = jnp.any(block_owners == req_index, axis=1).astype(jnp.int32)
    span_att = combine(has, slots, self_sum, self_stat)
    decode_q = queries[CH:].reshape(DEC_DEV, local_heads, HD)
    cache_key = lax.dynamic_slice_in_dim(cache_keys, kv_head * HD, HD, 2)
    cache_value = lax.dynamic_slice_in_dim(cache_values, kv_head * HD, HD, 2)
    cache_scores = (
        jnp.einsum("thd,tjd->thj", decode_q, cache_key, preferred_element_type=jnp.float32)
        * SCORE_SCALE
    )
    cache_valid = (
        lax.broadcasted_iota(jnp.int32, (DEC_DEV, 1, DCACHE), 2) < cache_len[:, None, None]
    )
    cache_scores = jnp.where(cache_valid, cache_scores, LOWEST)
    own_scores = (
        jnp.einsum("thd,td->th", decode_q, new_keys[CH:], preferred_element_type=jnp.float32)
        * SCORE_SCALE
    )
    decode_top = jnp.maximum(jnp.max(cache_scores, axis=-1), own_scores)
    cache_exp = jnp.exp(cache_scores - decode_top[:, :, None])
    own_exp = jnp.exp(own_scores - decode_top)
    decode_total = jnp.sum(cache_exp, axis=-1) + own_exp
    decode_sum = (
        jnp.einsum(
            "thj,tjd->thd",
            cache_exp.astype(jnp.bfloat16),
            cache_value,
            preferred_element_type=jnp.float32,
        )
        + rounded(own_exp).astype(jnp.float32)[:, :, None]
        * new_values[CH:].astype(jnp.float32)[:, None, :]
    )
    decode_att = (
        (decode_sum / decode_total[:, :, None])
        .reshape(DEC_DEV, local_heads * HD)
        .astype(jnp.bfloat16)
    )
    attended = jnp.concatenate([span_att, decode_att], axis=0)
    part = CH // tp_count

    def rows_of(x, owner):
        return jnp.concatenate(
            [lax.dynamic_slice_in_dim(x, owner * part, part, 0), x[CH:]], axis=0
        )

    proj_sum = jnp.dot(rows_of(attended, tp_index), o_weight, preferred_element_type=jnp.float32)
    for shift in range(1, tp_count):
        target = (tp_index + shift) % tp_count
        got_rows = passed_along(rows_of(attended, target), "tp", shift)
        got_weight = passed_along(o_weight, "tp", shift)
        proj_sum = proj_sum + jnp.dot(got_rows, got_weight, preferred_element_type=jnp.float32)
    mine = finish_rows(
        proj_sum,
        rows_of(tok_float, tp_index),
        rows_of(tok_norm, tp_index),
        rows_of(layer_input, tp_index),
        attn_gain,
        laurel_left,
        laurel_right,
        laurel_gain,
        layer_gate,
        layer_proj,
        layer_gain,
    )
    gathered = [mine] + [passed_along(mine, "tp", shift) for shift in range(1, tp_count)]

    def assemble(me):
        def build(*got):
            blocks = [got[(me - owner) % tp_count][:part] for owner in range(tp_count)]
            return jnp.concatenate(blocks + [got[me][part:]], axis=0)

        return build

    return lax.switch(tp_index, [assemble(me) for me in range(tp_count)], *gathered)


def solution(mesh):
    placed = (
        P("req", None),
        P("req", None),
        P(),
        P(None, "tp"),
        P(),
        P(),
        P(),
        P(),
        P("tp", None),
        P(),
        P(),
        P(),
        P(),
        P(),
        P(),
        P(),
        P("req", None, None),
        P("req", None, None),
        P(),
        P(),
        P("req", None, None),
        P("req", None, None),
        P("req"),
    )
    return jax.shard_map(
        body, mesh=mesh, in_specs=placed, out_specs=P("req", None), check_vma=False
    )
```

```python
import functools
import math

import jax
import jax.numpy as jnp
from jax import lax
from jax.experimental import pallas as pl
from jax.experimental.pallas import tpu as pltpu
from jax.sharding import PartitionSpec as P

H = 8
KVH = 2
HD = 256
CH = 512
DEC_DEV = 4
P_DEV = 8
PIECE = 1024
DCACHE = 512
ROWS = 516
STAT = 128
CHUNK = 256


LOWEST = -1e30
SCORE_SCALE = 1.0 / math.sqrt(HD)


def passed_along(x, axis, by):
    length = lax.axis_size(axis)
    return lax.ppermute(x, axis, [(i, (i + by) % length) for i in range(length)])


def rounded(x):
    return lax.optimization_barrier(x.astype(jnp.bfloat16))


def normed(x, scale_gain):
    return x * lax.rsqrt(jnp.mean(x * x, axis=-1, keepdims=True) + 1e-06) * scale_gain


def head_partial(q, keys, values, valid):
    scores = lax.dot_general(q, keys, (((1,), (1,)), ((), ())), preferred_element_type=jnp.float32)
    scores = jnp.where(valid, scores, LOWEST)
    top = jnp.max(scores, axis=1, keepdims=True)
    weights = jnp.exp((scores - top) * SCORE_SCALE)
    total = jnp.sum(weights, axis=1, keepdims=True)
    summed = jnp.dot(weights.astype(jnp.bfloat16), values, preferred_element_type=jnp.float32)
    return top * SCORE_SCALE, total, summed


def split3(x):
    hi = x.astype(jnp.bfloat16).astype(jnp.float32)
    rest = x - hi
    mid = rest.astype(jnp.bfloat16).astype(jnp.float32)
    lo = rest - mid
    return hi, mid, lo


def piece_kernel(slots, tab_ref, *refs):
    q_refs = refs[:slots]
    k_ref, v_ref = refs[slots:slots + 2]
    out_refs = refs[slots + 3:2 * slots + 3]
    scratch = refs[2 * slots + 3:]
    step = pl.program_id(0)

    @pl.when(tab_ref[5 * P_DEV + step] == 1)
    def _():
        piece_step(step, tab_ref, q_refs, k_ref, v_ref, out_refs, *scratch)


def piece_step(step, tab_ref, q_refs, k_ref, v_ref, out_refs, qbuf, fin, acc_m, acc_l, acc_n, sbuf, lbuf, nbuf):
    slots = len(q_refs)
    slot = tab_ref[P_DEV + step]
    length = tab_ref[2 * P_DEV + step]
    first = tab_ref[3 * P_DEV + step]
    last = tab_ref[4 * P_DEV + step]
    for k in range(slots):

        @pl.when(slot == k)
        def _(k=k):
            qbuf[...] = q_refs[k][...]

    rows = qbuf.shape[0]
    chunks = (length + CHUNK - 1) // CHUNK
    for h in range(2):
        q = qbuf[:, h * HD:(h + 1) * HD]

        def score_chunk(c, top, q=q):
            start = pl.multiple_of(c * CHUNK, CHUNK)
            scores = lax.dot_general(
                q, k_ref[0, pl.ds(start, CHUNK), :], (((1,), (1,)), ((), ())),
                preferred_element_type=jnp.float32,
            )
            valid = lax.broadcasted_iota(jnp.int32, (rows, CHUNK), 1) + start < length
            scores = jnp.where(valid, scores, LOWEST)
            sbuf[c] = scores
            return jnp.maximum(top, jnp.max(scores, axis=1, keepdims=True))

        top = lax.fori_loop(0, chunks, score_chunk, jnp.full((rows, 1), LOWEST, jnp.float32))
        lbuf[...] = jnp.zeros_like(lbuf)
        nbuf[...] = jnp.zeros_like(nbuf)

        @pl.loop(0, chunks)
        def _(c, top=top):
            start = pl.multiple_of(c * CHUNK, CHUNK)
            weights = jnp.exp((sbuf[c] - top) * SCORE_SCALE)
            lbuf[...] += jnp.sum(weights, axis=1, keepdims=True)
            nbuf[...] += jnp.dot(
                weights.astype(jnp.bfloat16), v_ref[0, pl.ds(start, CHUNK), :],
                preferred_element_type=jnp.float32,
            )

        top = top * SCORE_SCALE

        @pl.when(first == 1)
        def _(h=h, top=top):
            acc_m[h] = top
            acc_l[h] = lbuf[...]
            acc_n[h] = nbuf[...]

        @pl.when(first == 0)
        def _(h=h, top=top):
            old = acc_m[h]
            new = jnp.maximum(old, top)
            keep = jnp.exp(old - new)
            add = jnp.exp(top - new)
            acc_l[h] = acc_l[h] * keep + lbuf[...] * add
            acc_n[h] = acc_n[h] * keep + nbuf[...] * add
            acc_m[h] = new

    @pl.when(last == 1)
    def _():
        lane = lax.broadcasted_iota(jnp.int32, (rows, STAT), 1)
        stat = jnp.zeros((rows, STAT), jnp.float32)
        for h in range(2):
            total = acc_l[h]
            fin[:, h * HD:(h + 1) * HD] = (acc_n[h] / total).astype(jnp.bfloat16)
            for i, part in enumerate(split3(acc_m[h]) + split3(total)):
                stat = jnp.where(lane == 8 * h + i, part, stat)
        fin[:, 2 * HD:] = stat.astype(jnp.bfloat16)
        for k in range(slots):

            @pl.when(slot == k)
            def _(k=k):
                out_refs[k][...] = fin[...]


def piece_attention(table, windows, piece_keys, piece_values, after):
    rows = windows[0].shape[0]
    slots = len(windows)
    q_spec = pl.BlockSpec((rows, 2 * HD), lambda s, t: (0, 0))
    kv_spec = pl.BlockSpec((1, PIECE, HD), lambda s, t: (t[s], 0, t[6 * P_DEV]))
    out_spec = pl.BlockSpec((rows, 2 * HD + STAT), lambda s, t: (0, 0))
    grid_spec = pltpu.PrefetchScalarGridSpec(
        num_scalar_prefetch=1,
        grid=(P_DEV,),
        in_specs=[q_spec] * slots + [kv_spec, kv_spec, pl.BlockSpec(memory_space=pl.ANY)],
        out_specs=[out_spec] * slots,
        scratch_shapes=[
            pltpu.VMEM((rows, 2 * HD), jnp.bfloat16),
            pltpu.VMEM((rows, 2 * HD + STAT), jnp.bfloat16),
            pltpu.VMEM((2, rows, 1), jnp.float32),
            pltpu.VMEM((2, rows, 1), jnp.float32),
            pltpu.VMEM((2, rows, HD), jnp.float32),
            pltpu.VMEM((PIECE // CHUNK, rows, CHUNK), jnp.float32),
            pltpu.VMEM((rows, 1), jnp.float32),
            pltpu.VMEM((rows, HD), jnp.float32),
        ],
    )
    pieces = P_DEV // 2
    flops = pieces * 2 * 2 * 2 * rows * PIECE * HD
    return pl.pallas_call(
        functools.partial(piece_kernel, slots),
        grid_spec=grid_spec,
        out_shape=[jax.ShapeDtypeStruct((rows, 2 * HD + STAT), jnp.bfloat16)] * slots,
        compiler_params=pltpu.CompilerParams(
            dimension_semantics=("arbitrary",), vmem_limit_bytes=48 * 1024 * 1024
        ),
        cost_estimate=pl.CostEstimate(
            flops=flops,
            transcendentals=pieces * 2 * rows * PIECE,
            bytes_accessed=pieces * 2 * PIECE * HD * 2 + slots * rows * 2 * HD * 2 * 2,
        ),
    )(table, *windows, piece_keys, piece_values, after)


def self_kernel(q_ref, k_ref, v_ref, n_ref, stat_ref):
    rows = q_ref.shape[0]
    valid = lax.broadcasted_iota(jnp.int32, (rows, rows), 1) <= lax.broadcasted_iota(
        jnp.int32, (rows, rows), 0
    )
    lane = lax.broadcasted_iota(jnp.int32, (rows, STAT), 1)
    stat = jnp.zeros((rows, STAT), jnp.float32)
    keys = k_ref[...]
    values = v_ref[...]
    for h in range(2):
        top, total, summed = head_partial(q_ref[:, h * HD:(h + 1) * HD], keys, values, valid)
        n_ref[:, h * HD:(h + 1) * HD] = summed
        stat = jnp.where(lane == 8 * h, top, stat)
        stat = jnp.where(lane == 8 * h + 3, total, stat)
    stat_ref[...] = stat


def self_attention(q, keys, values):
    rows = q.shape[0]
    return pl.pallas_call(
        self_kernel,
        out_shape=(
            jax.ShapeDtypeStruct((rows, 2 * HD), jnp.float32),
            jax.ShapeDtypeStruct((rows, STAT), jnp.float32),
        ),
        compiler_params=pltpu.CompilerParams(vmem_limit_bytes=48 * 1024 * 1024),
        cost_estimate=pl.CostEstimate(
            flops=2 * 2 * 2 * rows * rows * HD,
            transcendentals=2 * rows * rows,
            bytes_accessed=rows * 2 * HD * 2 + 2 * rows * HD * 2 + rows * (2 * HD + STAT) * 4,
        ),
    )(q, keys, values)


def combine_kernel(has_ref, *refs):
    slot_refs = refs[:P_DEV]
    sum_ref, stat_ref, out_ref = refs[P_DEV:]
    rows = out_ref.shape[0]
    lane = lax.broadcasted_iota(jnp.int32, (rows, STAT), 1)
    near_stat = stat_ref[...]
    stats = [slot_refs[d][:, 2 * HD:].astype(jnp.float32) for d in range(P_DEV)]

    def pick(stat, first, count):
        chosen = (lane >= first) & (lane < first + count)
        return jnp.sum(jnp.where(chosen, stat, 0.0), axis=1, keepdims=True)

    for h in range(2):
        tops = [pick(stats[d], 8 * h, 3) for d in range(P_DEV)]
        totals = [pick(stats[d], 8 * h + 3, 3) for d in range(P_DEV)]
        far_top = jnp.full((rows, 1), LOWEST, jnp.float32)
        for d in range(P_DEV):
            far_top = jnp.maximum(far_top, jnp.where(has_ref[d] == 1, tops[d], LOWEST))
        far_total = jnp.zeros((rows, 1), jnp.float32)
        far_sum = jnp.zeros((rows, HD), jnp.float32)
        for d in range(P_DEV):
            live = has_ref[d] == 1
            weight = jnp.where(live, totals[d] * jnp.exp(tops[d] - far_top), 0.0)
            far_total = far_total + weight
            block = slot_refs[d][:, h * HD:(h + 1) * HD].astype(jnp.float32)
            far_sum = far_sum + jnp.where(live, weight * block, 0.0)
        near_top = pick(near_stat, 8 * h, 1)
        near_total = pick(near_stat, 8 * h + 3, 1)
        final_top = jnp.maximum(far_top, near_top)
        far_scale = jnp.exp(far_top - final_top)
        near_scale = jnp.exp(near_top - final_top)
        near_sum = sum_ref[:, h * HD:(h + 1) * HD]
        out_ref[:, h * HD:(h + 1) * HD] = (
            (far_sum * far_scale + near_sum * near_scale)
            / (far_total * far_scale + near_total * near_scale)
        ).astype(out_ref.dtype)


def combine(has, slots, self_sum, self_stat):
    rows = slots[0].shape[0]
    tile = 128
    slot_spec = pl.BlockSpec((tile, 2 * HD + STAT), lambda i, t: (i, 0))
    grid_spec = pltpu.PrefetchScalarGridSpec(
        num_scalar_prefetch=1,
        grid=(rows // tile,),
        in_specs=[slot_spec] * P_DEV
        + [
            pl.BlockSpec((tile, 2 * HD), lambda i, t: (i, 0)),
            pl.BlockSpec((tile, STAT), lambda i, t: (i, 0)),
        ],
        out_specs=pl.BlockSpec((tile, 2 * HD), lambda i, t: (i, 0)),
    )
    return pl.pallas_call(
        combine_kernel,
        grid_spec=grid_spec,
        out_shape=jax.ShapeDtypeStruct((rows, 2 * HD), jnp.bfloat16),
        compiler_params=pltpu.CompilerParams(dimension_semantics=("arbitrary",)),
        cost_estimate=pl.CostEstimate(
            flops=rows * 2 * HD * 3 * P_DEV,
            transcendentals=rows * 2 * P_DEV,
            bytes_accessed=P_DEV * rows * (2 * HD + STAT) * 2 + rows * (2 * HD + STAT) * 4 + rows * 2 * HD * 2,
        ),
    )(has, *slots, self_sum, self_stat)


def finish_rows(
    proj_sum,
    tok_float,
    tok_norm,
    extra_input,
    attn_gain,
    laurel_left,
    laurel_right,
    laurel_gain,
    layer_gate,
    layer_proj,
    layer_gain,
):
    laurel_low = jnp.dot(tok_norm, laurel_left, preferred_element_type=jnp.float32).astype(
        jnp.bfloat16
    )
    laurel_out = tok_norm.astype(jnp.float32) + normed(
        jnp.dot(laurel_low, laurel_right, preferred_element_type=jnp.float32),
        laurel_gain.astype(jnp.float32),
    )
    mixture = (tok_float + normed(proj_sum, attn_gain.astype(jnp.float32)) + laurel_out) * (
        1.0 / math.sqrt(2.0)
    )
    gate_act = jnp.dot(mixture.astype(jnp.bfloat16), layer_gate, preferred_element_type=jnp.float32)
    gate_out = (jax.nn.gelu(gate_act, approximate=True) * extra_input.astype(jnp.float32)).astype(
        jnp.bfloat16
    )
    return (
        mixture
        + normed(
            jnp.dot(gate_out, layer_proj, preferred_element_type=jnp.float32),
            layer_gain.astype(jnp.float32),
        )
    ).astype(jnp.bfloat16)


def schedule_table(distances, lengths):
    ids = jnp.arange(P_DEV, dtype=jnp.int32)
    before = (distances[None, :] < distances[:, None]) | (
        (distances[None, :] == distances[:, None]) & (ids[None, :] < ids[:, None])
    )
    rank = jnp.sum(before.astype(jnp.int32), axis=1)
    chosen = rank[:, None] == ids[None, :]
    order = jnp.sum(jnp.where(chosen, ids[:, None], 0), axis=0)
    slot = jnp.sum(jnp.where(chosen, distances[:, None], 0), axis=0)
    length = jnp.sum(jnp.where(chosen, lengths[:, None], 0), axis=0)
    minus = jnp.full((1,), -1, jnp.int32)
    first = (slot != jnp.concatenate([minus, slot[:-1]])).astype(jnp.int32)
    last = (slot != jnp.concatenate([slot[1:], minus])).astype(jnp.int32)
    return order, slot, length, first, last


def stage_table(sorted_rows, kv_head, low, high):
    order, slot, length, first, last = sorted_rows
    ids = jnp.arange(P_DEV, dtype=jnp.int32)
    start = jnp.sum((slot < low).astype(jnp.int32))
    count = jnp.sum(((slot >= low) & (slot <= high)).astype(jnp.int32))
    active = (ids < count).astype(jnp.int32)
    where = jnp.clip(start + jnp.minimum(ids, jnp.maximum(count, 1) - 1), 0, P_DEV - 1)
    rows = [jnp.take(x, where) for x in (order, slot - low, length, first, last)]
    kv_row = jnp.full((P_DEV,), kv_head, jnp.int32)
    return jnp.concatenate(rows + [active, kv_row]).astype(jnp.int32)


def body(
    tokens,
    layer_input,
    input_gain,
    q_weight,
    k_weight,
    v_weight,
    q_gain,
    k_gain,
    o_weight,
    attn_gain,
    laurel_left,
    laurel_right,
    laurel_gain,
    layer_gate,
    layer_proj,
    layer_gain,
    piece_keys,
    piece_values,
    piece_owner,
    piece_len,
    cache_keys,
    cache_values,
    cache_len,
):
    req_count = lax.axis_size("req")
    tp_count = lax.axis_size("tp")
    req_index = lax.axis_index("req")
    tp_index = lax.axis_index("tp")
    local_heads = H // tp_count
    kv_head = tp_index * local_heads // (H // KVH)
    full_o_weight = lax.all_gather(o_weight, "tp", axis=0, tiled=True)
    tok_float = tokens.astype(jnp.float32)
    tok_norm = normed(tok_float, input_gain.astype(jnp.float32)).astype(jnp.bfloat16)
    queries = jnp.dot(tok_norm, q_weight, preferred_element_type=jnp.float32).reshape(
        ROWS, local_heads, HD
    )
    queries = (
        normed(queries, q_gain.astype(jnp.float32))
        .astype(jnp.bfloat16)
        .reshape(ROWS, local_heads * HD)
    )
    key_cols = lax.dynamic_slice_in_dim(k_weight, kv_head * HD, HD, 1)
    value_cols = lax.dynamic_slice_in_dim(v_weight, kv_head * HD, HD, 1)
    new_keys = normed(
        jnp.dot(tok_norm, key_cols, preferred_element_type=jnp.float32), k_gain.astype(jnp.float32)
    ).astype(jnp.bfloat16)
    new_values = normed(
        jnp.dot(tok_norm, value_cols, preferred_element_type=jnp.float32), 1.0
    ).astype(jnp.bfloat16)
    own_block = queries[:CH]
    half = P_DEV // 2
    early = [passed_along(own_block, "req", d) for d in range(1, half)]
    held = lax.optimization_barrier((own_block, *early))[0]
    late = [passed_along(held, "req", d) for d in range(half, P_DEV)]
    self_sum, self_stat = self_attention(own_block, new_keys[:CH], new_values[:CH])

    owners = lax.dynamic_slice_in_dim(piece_owner, req_index * P_DEV, P_DEV)
    lengths = lax.dynamic_slice_in_dim(piece_len, req_index * P_DEV, P_DEV)
    distances = (req_index - owners + req_count) % req_count
    sorted_rows = schedule_table(distances, lengths)
    near = piece_attention(
        stage_table(sorted_rows, kv_head, 0, half - 1), [own_block] + early,
        piece_keys, piece_values, self_stat,
    )
    far = piece_attention(
        stage_table(sorted_rows, kv_head, half, P_DEV - 1), late,
        piece_keys, piece_values, near[0],
    )
    packed = list(near) + list(far)
    slots = [packed[0]] + [passed_along(packed[d], "req", -d) for d in range(1, P_DEV)]

    block_ids = (req_index + jnp.arange(P_DEV, dtype=jnp.int32)) % req_count
    block_owners = jnp.take(piece_owner.reshape(req_count, P_DEV), block_ids, axis=0)
    has = jnp.any(block_owners == req_index, axis=1).astype(jnp.int32)
    span_att = combine(has, slots, self_sum, self_stat)
    decode_q = queries[CH:].reshape(DEC_DEV, local_heads, HD)
    cache_key = lax.dynamic_slice_in_dim(cache_keys, kv_head * HD, HD, 2)
    cache_value = lax.dynamic_slice_in_dim(cache_values, kv_head * HD, HD, 2)
    cache_scores = (
        jnp.einsum("thd,tjd->thj", decode_q, cache_key, preferred_element_type=jnp.float32)
        * SCORE_SCALE
    )
    cache_valid = (
        lax.broadcasted_iota(jnp.int32, (DEC_DEV, 1, DCACHE), 2) < cache_len[:, None, None]
    )
    cache_scores = jnp.where(cache_valid, cache_scores, LOWEST)
    own_scores = (
        jnp.einsum("thd,td->th", decode_q, new_keys[CH:], preferred_element_type=jnp.float32)
        * SCORE_SCALE
    )
    decode_top = jnp.maximum(jnp.max(cache_scores, axis=-1), own_scores)
    cache_exp = jnp.exp(cache_scores - decode_top[:, :, None])
    own_exp = jnp.exp(own_scores - decode_top)
    decode_total = jnp.sum(cache_exp, axis=-1) + own_exp
    decode_sum = (
        jnp.einsum(
            "thj,tjd->thd",
            cache_exp.astype(jnp.bfloat16),
            cache_value,
            preferred_element_type=jnp.float32,
        )
        + rounded(own_exp).astype(jnp.float32)[:, :, None]
        * new_values[CH:].astype(jnp.float32)[:, None, :]
    )
    decode_att = (
        (decode_sum / decode_total[:, :, None])
        .reshape(DEC_DEV, local_heads * HD)
        .astype(jnp.bfloat16)
    )
    attended = jnp.concatenate([span_att, decode_att], axis=0)
    part = CH // tp_count

    def rows_of(x, owner):
        return jnp.concatenate(
            [lax.dynamic_slice_in_dim(x, owner * part, part, 0), x[CH:]], axis=0
        )

    row_parts = [rows_of(attended, tp_index)]
    weight_parts = [o_weight]
    for shift in range(1, tp_count):
        target = (tp_index + shift) % tp_count
        row_parts.append(passed_along(rows_of(attended, target), "tp", shift))
        weight_parts.append(passed_along(o_weight, "tp", shift))
    proj_sum = jnp.dot(
        jnp.concatenate(row_parts, axis=1),
        jnp.concatenate(weight_parts, axis=0),
        preferred_element_type=jnp.float32,
    )
    mine = finish_rows(
        proj_sum,
        rows_of(tok_float, tp_index),
        rows_of(tok_norm, tp_index),
        rows_of(layer_input, tp_index),
        attn_gain,
        laurel_left,
        laurel_right,
        laurel_gain,
        layer_gate,
        layer_proj,
        layer_gain,
    )
    gathered = [mine] + [passed_along(mine, "tp", shift) for shift in range(1, tp_count)]

    def assemble(me):
        def build(*got):
            blocks = [got[(me - owner) % tp_count][:part] for owner in range(tp_count)]
            return jnp.concatenate(blocks + [got[me][part:]], axis=0)

        return build

    return lax.switch(tp_index, [assemble(me) for me in range(tp_count)], *gathered)


def solution(mesh):
    placed = (
        P("req", None),
        P("req", None),
        P(),
        P(None, "tp"),
        P(),
        P(),
        P(),
        P(),
        P("tp", None),
        P(),
        P(),
        P(),
        P(),
        P(),
        P(),
        P(),
        P("req", None, None),
        P("req", None, None),
        P(),
        P(),
        P("req", None, None),
        P("req", None, None),
        P("req"),
    )
    return jax.shard_map(
        body, mesh=mesh, in_specs=placed, out_specs=P("req", None), check_vma=False
    )
```

```python
import functools
import math

import jax
import jax.numpy as jnp
from jax import lax
from jax.experimental import pallas as pl
from jax.experimental.pallas import tpu as pltpu
from jax.sharding import PartitionSpec as P

H = 8
KVH = 2
HD = 256
CH = 512
DEC_DEV = 4
P_DEV = 8
PIECE = 1024
DCACHE = 512
ROWS = 516
STAT = 128
CHUNK = 256


LOWEST = -1e30
SCORE_SCALE = 1.0 / math.sqrt(HD)


def passed_along(x, axis, by):
    length = lax.axis_size(axis)
    return lax.ppermute(x, axis, [(i, (i + by) % length) for i in range(length)])


def rounded(x):
    return lax.optimization_barrier(x.astype(jnp.bfloat16))


def normed(x, scale_gain):
    return x * lax.rsqrt(jnp.mean(x * x, axis=-1, keepdims=True) + 1e-06) * scale_gain


def head_partial(q, keys, values, valid):
    scores = lax.dot_general(q, keys, (((1,), (1,)), ((), ())), preferred_element_type=jnp.float32)
    scores = jnp.where(valid, scores, LOWEST)
    top = jnp.max(scores, axis=1, keepdims=True)
    weights = jnp.exp((scores - top) * SCORE_SCALE)
    total = jnp.sum(weights, axis=1, keepdims=True)
    summed = jnp.dot(weights.astype(jnp.bfloat16), values, preferred_element_type=jnp.float32)
    return top * SCORE_SCALE, total, summed


def split3(x):
    hi = x.astype(jnp.bfloat16).astype(jnp.float32)
    rest = x - hi
    mid = rest.astype(jnp.bfloat16).astype(jnp.float32)
    lo = rest - mid
    return hi, mid, lo


def piece_kernel(slots, tab_ref, *refs):
    q_refs = refs[:slots]
    k_ref, v_ref = refs[slots:slots + 2]
    out_refs = refs[slots + 3:2 * slots + 3]
    scratch = refs[2 * slots + 3:]
    step = pl.program_id(0)

    @pl.when(tab_ref[5 * P_DEV + step] == 1)
    def _():
        piece_step(step, tab_ref, q_refs, k_ref, v_ref, out_refs, *scratch)


def piece_step(step, tab_ref, q_refs, k_ref, v_ref, out_refs, qbuf, fin, acc_m, acc_l, acc_n, sbuf, lbuf, nbuf):
    slots = len(q_refs)
    slot = tab_ref[P_DEV + step]
    length = tab_ref[2 * P_DEV + step]
    first = tab_ref[3 * P_DEV + step]
    last = tab_ref[4 * P_DEV + step]
    for k in range(slots):

        @pl.when(slot == k)
        def _(k=k):
            qbuf[...] = q_refs[k][...]

    rows = qbuf.shape[0]
    chunks = (length + CHUNK - 1) // CHUNK
    for h in range(2):
        q = qbuf[:, h * HD:(h + 1) * HD]

        def score_chunk(c, top, q=q):
            start = pl.multiple_of(c * CHUNK, CHUNK)
            scores = lax.dot_general(
                q, k_ref[0, pl.ds(start, CHUNK), :], (((1,), (1,)), ((), ())),
                preferred_element_type=jnp.float32,
            )
            sbuf[c] = scores

            @pl.when(start + CHUNK > length)
            def _():
                valid = lax.broadcasted_iota(jnp.int32, (rows, CHUNK), 1) + start < length
                sbuf[c] = jnp.where(valid, sbuf[c], LOWEST)

            return jnp.maximum(top, jnp.max(sbuf[c], axis=1, keepdims=True))

        top = lax.fori_loop(0, chunks, score_chunk, jnp.full((rows, 1), LOWEST, jnp.float32))
        lbuf[...] = jnp.zeros_like(lbuf)
        nbuf[...] = jnp.zeros_like(nbuf)

        @pl.loop(0, chunks)
        def _(c, top=top):
            start = pl.multiple_of(c * CHUNK, CHUNK)
            weights = jnp.exp((sbuf[c] - top) * SCORE_SCALE)
            lbuf[...] += jnp.sum(weights, axis=1, keepdims=True)
            nbuf[...] += jnp.dot(
                weights.astype(jnp.bfloat16), v_ref[0, pl.ds(start, CHUNK), :],
                preferred_element_type=jnp.float32,
            )

        top = top * SCORE_SCALE

        @pl.when(first == 1)
        def _(h=h, top=top):
            acc_m[h] = top
            acc_l[h] = lbuf[...]
            acc_n[h] = nbuf[...]

        @pl.when(first == 0)
        def _(h=h, top=top):
            old = acc_m[h]
            new = jnp.maximum(old, top)
            keep = jnp.exp(old - new)
            add = jnp.exp(top - new)
            acc_l[h] = acc_l[h] * keep + lbuf[...] * add
            acc_n[h] = acc_n[h] * keep + nbuf[...] * add
            acc_m[h] = new

    @pl.when(last == 1)
    def _():
        lane = lax.broadcasted_iota(jnp.int32, (rows, STAT), 1)
        stat = jnp.zeros((rows, STAT), jnp.float32)
        for h in range(2):
            total = acc_l[h]
            fin[:, h * HD:(h + 1) * HD] = (acc_n[h] / total).astype(jnp.bfloat16)
            for i, part in enumerate(split3(acc_m[h]) + split3(total)):
                stat = jnp.where(lane == 8 * h + i, part, stat)
        fin[:, 2 * HD:] = stat.astype(jnp.bfloat16)
        for k in range(slots):

            @pl.when(slot == k)
            def _(k=k):
                out_refs[k][...] = fin[...]


def piece_attention(table, windows, piece_keys, piece_values, after):
    rows = windows[0].shape[0]
    slots = len(windows)
    q_spec = pl.BlockSpec((rows, 2 * HD), lambda s, t: (0, 0))
    kv_spec = pl.BlockSpec((1, PIECE, HD), lambda s, t: (t[s], 0, t[6 * P_DEV]))
    out_spec = pl.BlockSpec((rows, 2 * HD + STAT), lambda s, t: (0, 0))
    grid_spec = pltpu.PrefetchScalarGridSpec(
        num_scalar_prefetch=1,
        grid=(P_DEV,),
        in_specs=[q_spec] * slots + [kv_spec, kv_spec, pl.BlockSpec(memory_space=pl.ANY)],
        out_specs=[out_spec] * slots,
        scratch_shapes=[
            pltpu.VMEM((rows, 2 * HD), jnp.bfloat16),
            pltpu.VMEM((rows, 2 * HD + STAT), jnp.bfloat16),
            pltpu.VMEM((2, rows, 1), jnp.float32),
            pltpu.VMEM((2, rows, 1), jnp.float32),
            pltpu.VMEM((2, rows, HD), jnp.float32),
            pltpu.VMEM((PIECE // CHUNK, rows, CHUNK), jnp.float32),
            pltpu.VMEM((rows, 1), jnp.float32),
            pltpu.VMEM((rows, HD), jnp.float32),
        ],
    )
    pieces = P_DEV // 2
    flops = pieces * 2 * 2 * 2 * rows * PIECE * HD
    return pl.pallas_call(
        functools.partial(piece_kernel, slots),
        grid_spec=grid_spec,
        out_shape=[jax.ShapeDtypeStruct((rows, 2 * HD + STAT), jnp.bfloat16)] * slots,
        compiler_params=pltpu.CompilerParams(
            dimension_semantics=("arbitrary",), vmem_limit_bytes=48 * 1024 * 1024
        ),
        cost_estimate=pl.CostEstimate(
            flops=flops,
            transcendentals=pieces * 2 * rows * PIECE,
            bytes_accessed=pieces * 2 * PIECE * HD * 2 + slots * rows * 2 * HD * 2 * 2,
        ),
    )(table, *windows, piece_keys, piece_values, after)


def self_kernel(q_ref, k_ref, v_ref, n_ref, stat_ref):
    rows = q_ref.shape[0]
    valid = lax.broadcasted_iota(jnp.int32, (rows, rows), 1) <= lax.broadcasted_iota(
        jnp.int32, (rows, rows), 0
    )
    lane = lax.broadcasted_iota(jnp.int32, (rows, STAT), 1)
    stat = jnp.zeros((rows, STAT), jnp.float32)
    keys = k_ref[...]
    values = v_ref[...]
    for h in range(2):
        top, total, summed = head_partial(q_ref[:, h * HD:(h + 1) * HD], keys, values, valid)
        n_ref[:, h * HD:(h + 1) * HD] = summed
        stat = jnp.where(lane == 8 * h, top, stat)
        stat = jnp.where(lane == 8 * h + 3, total, stat)
    stat_ref[...] = stat


def self_attention(q, keys, values):
    rows = q.shape[0]
    return pl.pallas_call(
        self_kernel,
        out_shape=(
            jax.ShapeDtypeStruct((rows, 2 * HD), jnp.float32),
            jax.ShapeDtypeStruct((rows, STAT), jnp.float32),
        ),
        compiler_params=pltpu.CompilerParams(vmem_limit_bytes=48 * 1024 * 1024),
        cost_estimate=pl.CostEstimate(
            flops=2 * 2 * 2 * rows * rows * HD,
            transcendentals=2 * rows * rows,
            bytes_accessed=rows * 2 * HD * 2 + 2 * rows * HD * 2 + rows * (2 * HD + STAT) * 4,
        ),
    )(q, keys, values)


def combine_kernel(has_ref, *refs):
    slot_refs = refs[:P_DEV]
    sum_ref, stat_ref, out_ref = refs[P_DEV:]
    rows = out_ref.shape[0]
    lane = lax.broadcasted_iota(jnp.int32, (rows, STAT), 1)
    near_stat = stat_ref[...]
    stats = [slot_refs[d][:, 2 * HD:].astype(jnp.float32) for d in range(P_DEV)]

    def pick(stat, first, count):
        chosen = (lane >= first) & (lane < first + count)
        return jnp.sum(jnp.where(chosen, stat, 0.0), axis=1, keepdims=True)

    for h in range(2):
        tops = [pick(stats[d], 8 * h, 3) for d in range(P_DEV)]
        totals = [pick(stats[d], 8 * h + 3, 3) for d in range(P_DEV)]
        far_top = jnp.full((rows, 1), LOWEST, jnp.float32)
        for d in range(P_DEV):
            far_top = jnp.maximum(far_top, jnp.where(has_ref[d] == 1, tops[d], LOWEST))
        far_total = jnp.zeros((rows, 1), jnp.float32)
        far_sum = jnp.zeros((rows, HD), jnp.float32)
        for d in range(P_DEV):
            live = has_ref[d] == 1
            weight = jnp.where(live, totals[d] * jnp.exp(tops[d] - far_top), 0.0)
            far_total = far_total + weight
            block = slot_refs[d][:, h * HD:(h + 1) * HD].astype(jnp.float32)
            far_sum = far_sum + jnp.where(live, weight * block, 0.0)
        near_top = pick(near_stat, 8 * h, 1)
        near_total = pick(near_stat, 8 * h + 3, 1)
        final_top = jnp.maximum(far_top, near_top)
        far_scale = jnp.exp(far_top - final_top)
        near_scale = jnp.exp(near_top - final_top)
        near_sum = sum_ref[:, h * HD:(h + 1) * HD]
        out_ref[:, h * HD:(h + 1) * HD] = (
            (far_sum * far_scale + near_sum * near_scale)
            / (far_total * far_scale + near_total * near_scale)
        ).astype(out_ref.dtype)


def combine(has, slots, self_sum, self_stat):
    rows = slots[0].shape[0]
    tile = 128
    slot_spec = pl.BlockSpec((tile, 2 * HD + STAT), lambda i, t: (i, 0))
    grid_spec = pltpu.PrefetchScalarGridSpec(
        num_scalar_prefetch=1,
        grid=(rows // tile,),
        in_specs=[slot_spec] * P_DEV
        + [
            pl.BlockSpec((tile, 2 * HD), lambda i, t: (i, 0)),
            pl.BlockSpec((tile, STAT), lambda i, t: (i, 0)),
        ],
        out_specs=pl.BlockSpec((tile, 2 * HD), lambda i, t: (i, 0)),
    )
    return pl.pallas_call(
        combine_kernel,
        grid_spec=grid_spec,
        out_shape=jax.ShapeDtypeStruct((rows, 2 * HD), jnp.bfloat16),
        compiler_params=pltpu.CompilerParams(dimension_semantics=("arbitrary",)),
        cost_estimate=pl.CostEstimate(
            flops=rows * 2 * HD * 3 * P_DEV,
            transcendentals=rows * 2 * P_DEV,
            bytes_accessed=P_DEV * rows * (2 * HD + STAT) * 2 + rows * (2 * HD + STAT) * 4 + rows * 2 * HD * 2,
        ),
    )(has, *slots, self_sum, self_stat)


def finish_rows(
    proj_sum,
    tok_float,
    tok_norm,
    extra_input,
    attn_gain,
    laurel_left,
    laurel_right,
    laurel_gain,
    layer_gate,
    layer_proj,
    layer_gain,
):
    laurel_low = jnp.dot(tok_norm, laurel_left, preferred_element_type=jnp.float32).astype(
        jnp.bfloat16
    )
    laurel_out = tok_norm.astype(jnp.float32) + normed(
        jnp.dot(laurel_low, laurel_right, preferred_element_type=jnp.float32),
        laurel_gain.astype(jnp.float32),
    )
    mixture = (tok_float + normed(proj_sum, attn_gain.astype(jnp.float32)) + laurel_out) * (
        1.0 / math.sqrt(2.0)
    )
    gate_act = jnp.dot(mixture.astype(jnp.bfloat16), layer_gate, preferred_element_type=jnp.float32)
    gate_out = (jax.nn.gelu(gate_act, approximate=True) * extra_input.astype(jnp.float32)).astype(
        jnp.bfloat16
    )
    return (
        mixture
        + normed(
            jnp.dot(gate_out, layer_proj, preferred_element_type=jnp.float32),
            layer_gain.astype(jnp.float32),
        )
    ).astype(jnp.bfloat16)


def schedule_table(distances, lengths):
    ids = jnp.arange(P_DEV, dtype=jnp.int32)
    before = (distances[None, :] < distances[:, None]) | (
        (distances[None, :] == distances[:, None]) & (ids[None, :] < ids[:, None])
    )
    rank = jnp.sum(before.astype(jnp.int32), axis=1)
    chosen = rank[:, None] == ids[None, :]
    order = jnp.sum(jnp.where(chosen, ids[:, None], 0), axis=0)
    slot = jnp.sum(jnp.where(chosen, distances[:, None], 0), axis=0)
    length = jnp.sum(jnp.where(chosen, lengths[:, None], 0), axis=0)
    minus = jnp.full((1,), -1, jnp.int32)
    first = (slot != jnp.concatenate([minus, slot[:-1]])).astype(jnp.int32)
    last = (slot != jnp.concatenate([slot[1:], minus])).astype(jnp.int32)
    return order, slot, length, first, last


def stage_table(sorted_rows, kv_head, low, high):
    order, slot, length, first, last = sorted_rows
    ids = jnp.arange(P_DEV, dtype=jnp.int32)
    start = jnp.sum((slot < low).astype(jnp.int32))
    count = jnp.sum(((slot >= low) & (slot <= high)).astype(jnp.int32))
    active = (ids < count).astype(jnp.int32)
    where = jnp.clip(start + jnp.minimum(ids, jnp.maximum(count, 1) - 1), 0, P_DEV - 1)
    rows = [jnp.take(x, where) for x in (order, slot - low, length, first, last)]
    kv_row = jnp.full((P_DEV,), kv_head, jnp.int32)
    return jnp.concatenate(rows + [active, kv_row]).astype(jnp.int32)


def body(
    tokens,
    layer_input,
    input_gain,
    q_weight,
    k_weight,
    v_weight,
    q_gain,
    k_gain,
    o_weight,
    attn_gain,
    laurel_left,
    laurel_right,
    laurel_gain,
    layer_gate,
    layer_proj,
    layer_gain,
    piece_keys,
    piece_values,
    piece_owner,
    piece_len,
    cache_keys,
    cache_values,
    cache_len,
):
    req_count = lax.axis_size("req")
    tp_count = lax.axis_size("tp")
    req_index = lax.axis_index("req")
    tp_index = lax.axis_index("tp")
    local_heads = H // tp_count
    kv_head = tp_index * local_heads // (H // KVH)
    full_o_weight = lax.all_gather(o_weight, "tp", axis=0, tiled=True)
    tok_float = tokens.astype(jnp.float32)
    tok_norm = normed(tok_float, input_gain.astype(jnp.float32)).astype(jnp.bfloat16)
    queries = jnp.dot(tok_norm, q_weight, preferred_element_type=jnp.float32).reshape(
        ROWS, local_heads, HD
    )
    queries = (
        normed(queries, q_gain.astype(jnp.float32))
        .astype(jnp.bfloat16)
        .reshape(ROWS, local_heads * HD)
    )
    key_cols = lax.dynamic_slice_in_dim(k_weight, kv_head * HD, HD, 1)
    value_cols = lax.dynamic_slice_in_dim(v_weight, kv_head * HD, HD, 1)
    new_keys = normed(
        jnp.dot(tok_norm, key_cols, preferred_element_type=jnp.float32), k_gain.astype(jnp.float32)
    ).astype(jnp.bfloat16)
    new_values = normed(
        jnp.dot(tok_norm, value_cols, preferred_element_type=jnp.float32), 1.0
    ).astype(jnp.bfloat16)
    own_block = queries[:CH]
    half = P_DEV // 2
    early = [passed_along(own_block, "req", d) for d in range(1, half)]
    held = lax.optimization_barrier((own_block, *early))[0]
    late = [passed_along(held, "req", d) for d in range(half, P_DEV)]
    self_sum, self_stat = self_attention(own_block, new_keys[:CH], new_values[:CH])

    owners = lax.dynamic_slice_in_dim(piece_owner, req_index * P_DEV, P_DEV)
    lengths = lax.dynamic_slice_in_dim(piece_len, req_index * P_DEV, P_DEV)
    distances = (req_index - owners + req_count) % req_count
    sorted_rows = schedule_table(distances, lengths)
    near = piece_attention(
        stage_table(sorted_rows, kv_head, 0, half - 1), [own_block] + early,
        piece_keys, piece_values, self_stat,
    )
    far = piece_attention(
        stage_table(sorted_rows, kv_head, half, P_DEV - 1), late,
        piece_keys, piece_values, near[0],
    )
    packed = list(near) + list(far)
    slots = [packed[0]] + [passed_along(packed[d], "req", -d) for d in range(1, P_DEV)]

    block_ids = (req_index + jnp.arange(P_DEV, dtype=jnp.int32)) % req_count
    block_owners = jnp.take(piece_owner.reshape(req_count, P_DEV), block_ids, axis=0)
    has = jnp.any(block_owners == req_index, axis=1).astype(jnp.int32)
    span_att = combine(has, slots, self_sum, self_stat)
    decode_q = queries[CH:].reshape(DEC_DEV, local_heads, HD)
    cache_key = lax.dynamic_slice_in_dim(cache_keys, kv_head * HD, HD, 2)
    cache_value = lax.dynamic_slice_in_dim(cache_values, kv_head * HD, HD, 2)
    cache_scores = (
        jnp.einsum("thd,tjd->thj", decode_q, cache_key, preferred_element_type=jnp.float32)
        * SCORE_SCALE
    )
    cache_valid = (
        lax.broadcasted_iota(jnp.int32, (DEC_DEV, 1, DCACHE), 2) < cache_len[:, None, None]
    )
    cache_scores = jnp.where(cache_valid, cache_scores, LOWEST)
    own_scores = (
        jnp.einsum("thd,td->th", decode_q, new_keys[CH:], preferred_element_type=jnp.float32)
        * SCORE_SCALE
    )
    decode_top = jnp.maximum(jnp.max(cache_scores, axis=-1), own_scores)
    cache_exp = jnp.exp(cache_scores - decode_top[:, :, None])
    own_exp = jnp.exp(own_scores - decode_top)
    decode_total = jnp.sum(cache_exp, axis=-1) + own_exp
    decode_sum = (
        jnp.einsum(
            "thj,tjd->thd",
            cache_exp.astype(jnp.bfloat16),
            cache_value,
            preferred_element_type=jnp.float32,
        )
        + rounded(own_exp).astype(jnp.float32)[:, :, None]
        * new_values[CH:].astype(jnp.float32)[:, None, :]
    )
    decode_att = (
        (decode_sum / decode_total[:, :, None])
        .reshape(DEC_DEV, local_heads * HD)
        .astype(jnp.bfloat16)
    )
    attended = jnp.concatenate([span_att, decode_att], axis=0)
    part = CH // tp_count

    def rows_of(x, owner):
        return jnp.concatenate(
            [lax.dynamic_slice_in_dim(x, owner * part, part, 0), x[CH:]], axis=0
        )

    proj_sum = jnp.dot(rows_of(attended, tp_index), o_weight, preferred_element_type=jnp.float32)
    for shift in range(1, tp_count):
        target = (tp_index + shift) % tp_count
        got_rows = passed_along(rows_of(attended, target), "tp", shift)
        got_weight = passed_along(o_weight, "tp", shift)
        proj_sum = proj_sum + jnp.dot(got_rows, got_weight, preferred_element_type=jnp.float32)
    mine = finish_rows(
        proj_sum,
        rows_of(tok_float, tp_index),
        rows_of(tok_norm, tp_index),
        rows_of(layer_input, tp_index),
        attn_gain,
        laurel_left,
        laurel_right,
        laurel_gain,
        layer_gate,
        layer_proj,
        layer_gain,
    )
    gathered = [mine] + [passed_along(mine, "tp", shift) for shift in range(1, tp_count)]

    def assemble(me):
        def build(*got):
            blocks = [got[(me - owner) % tp_count][:part] for owner in range(tp_count)]
            return jnp.concatenate(blocks + [got[me][part:]], axis=0)

        return build

    return lax.switch(tp_index, [assemble(me) for me in range(tp_count)], *gathered)


def solution(mesh):
    placed = (
        P("req", None),
        P("req", None),
        P(),
        P(None, "tp"),
        P(),
        P(),
        P(),
        P(),
        P("tp", None),
        P(),
        P(),
        P(),
        P(),
        P(),
        P(),
        P(),
        P("req", None, None),
        P("req", None, None),
        P(),
        P(),
        P("req", None, None),
        P("req", None, None),
        P("req"),
    )
    return jax.shard_map(
        body, mesh=mesh, in_specs=placed, out_specs=P("req", None), check_vma=False
    )
```

```python
import functools
import math

import jax
import jax.numpy as jnp
from jax import lax
from jax.experimental import pallas as pl
from jax.experimental.pallas import tpu as pltpu
from jax.sharding import PartitionSpec as P

H = 8
KVH = 2
HD = 256
CH = 512
DEC_DEV = 4
P_DEV = 8
PIECE = 1024
DCACHE = 512
ROWS = 516
STAT = 128
CHUNK = 256


LOWEST = -1e30
SCORE_SCALE = 1.0 / math.sqrt(HD)


def passed_along(x, axis, by):
    length = lax.axis_size(axis)
    return lax.ppermute(x, axis, [(i, (i + by) % length) for i in range(length)])


def rounded(x):
    return lax.optimization_barrier(x.astype(jnp.bfloat16))


def normed(x, scale_gain):
    return x * lax.rsqrt(jnp.mean(x * x, axis=-1, keepdims=True) + 1e-06) * scale_gain


def head_partial(q, keys, values, valid):
    scores = lax.dot_general(q, keys, (((1,), (1,)), ((), ())), preferred_element_type=jnp.float32)
    scores = jnp.where(valid, scores, LOWEST)
    top = jnp.max(scores, axis=1, keepdims=True)
    weights = jnp.exp((scores - top) * SCORE_SCALE)
    total = jnp.sum(weights, axis=1, keepdims=True)
    summed = jnp.dot(weights.astype(jnp.bfloat16), values, preferred_element_type=jnp.float32)
    return top * SCORE_SCALE, total, summed


def split3(x):
    hi = x.astype(jnp.bfloat16).astype(jnp.float32)
    rest = x - hi
    mid = rest.astype(jnp.bfloat16).astype(jnp.float32)
    lo = rest - mid
    return hi, mid, lo


def piece_kernel(slots, tab_ref, *refs):
    q_refs = refs[:slots]
    k_ref, v_ref = refs[slots:slots + 2]
    out_refs = refs[slots + 3:2 * slots + 3]
    scratch = refs[2 * slots + 3:]
    step = pl.program_id(0)

    @pl.when(tab_ref[5 * P_DEV + step] == 1)
    def _():
        piece_step(step, tab_ref, q_refs, k_ref, v_ref, out_refs, *scratch)


def piece_step(step, tab_ref, q_refs, k_ref, v_ref, out_refs, qbuf, fin, acc_m, acc_l, acc_n, sbuf, lbuf, nbuf):
    slots = len(q_refs)
    slot = tab_ref[P_DEV + step]
    length = tab_ref[2 * P_DEV + step]
    first = tab_ref[3 * P_DEV + step]
    last = tab_ref[4 * P_DEV + step]
    for k in range(slots):

        @pl.when(slot == k)
        def _(k=k):
            qbuf[...] = q_refs[k][...]

    rows = qbuf.shape[0]
    chunks = (length + CHUNK - 1) // CHUNK
    for h in range(2):
        q = qbuf[:, h * HD:(h + 1) * HD]

        def score_chunk(c, top, q=q):
            start = pl.multiple_of(c * CHUNK, CHUNK)
            scores = lax.dot_general(
                q, k_ref[0, pl.ds(start, CHUNK), :], (((1,), (1,)), ((), ())),
                preferred_element_type=jnp.float32,
            )
            sbuf[c] = scores

            @pl.when(start + CHUNK > length)
            def _():
                valid = lax.broadcasted_iota(jnp.int32, (rows, CHUNK), 1) + start < length
                sbuf[c] = jnp.where(valid, sbuf[c], LOWEST)

            return jnp.maximum(top, jnp.max(sbuf[c], axis=1, keepdims=True))

        top = lax.fori_loop(0, chunks, score_chunk, jnp.full((rows, 1), LOWEST, jnp.float32))
        lbuf[...] = jnp.zeros_like(lbuf)
        nbuf[...] = jnp.zeros_like(nbuf)

        @pl.loop(0, chunks)
        def _(c, top=top):
            start = pl.multiple_of(c * CHUNK, CHUNK)
            weights = jnp.exp((sbuf[c] - top) * SCORE_SCALE)
            lbuf[...] += jnp.sum(weights, axis=1, keepdims=True)
            nbuf[...] += jnp.dot(
                weights.astype(jnp.bfloat16), v_ref[0, pl.ds(start, CHUNK), :],
                preferred_element_type=jnp.float32,
            )

        top = top * SCORE_SCALE

        @pl.when(first == 1)
        def _(h=h, top=top):
            acc_m[h] = top
            acc_l[h] = lbuf[...]
            acc_n[h] = nbuf[...]

        @pl.when(first == 0)
        def _(h=h, top=top):
            old = acc_m[h]
            new = jnp.maximum(old, top)
            keep = jnp.exp(old - new)
            add = jnp.exp(top - new)
            acc_l[h] = acc_l[h] * keep + lbuf[...] * add
            acc_n[h] = acc_n[h] * keep + nbuf[...] * add
            acc_m[h] = new

    @pl.when(last == 1)
    def _():
        lane = lax.broadcasted_iota(jnp.int32, (rows, STAT), 1)
        stat = jnp.zeros((rows, STAT), jnp.float32)
        for h in range(2):
            total = acc_l[h]
            fin[:, h * HD:(h + 1) * HD] = (acc_n[h] / total).astype(jnp.bfloat16)
            for i, part in enumerate(split3(acc_m[h]) + split3(total)):
                stat = jnp.where(lane == 8 * h + i, part, stat)
        fin[:, 2 * HD:] = stat.astype(jnp.bfloat16)
        for k in range(slots):

            @pl.when(slot == k)
            def _(k=k):
                out_refs[k][...] = fin[...]


def piece_attention(table, windows, piece_keys, piece_values, after):
    rows = windows[0].shape[0]
    slots = len(windows)
    q_spec = pl.BlockSpec((rows, 2 * HD), lambda s, t: (0, 0))
    kv_spec = pl.BlockSpec((1, PIECE, HD), lambda s, t: (t[s], 0, t[6 * P_DEV]))
    out_spec = pl.BlockSpec((rows, 2 * HD + STAT), lambda s, t: (0, 0))
    grid_spec = pltpu.PrefetchScalarGridSpec(
        num_scalar_prefetch=1,
        grid=(P_DEV,),
        in_specs=[q_spec] * slots + [kv_spec, kv_spec, pl.BlockSpec(memory_space=pl.ANY)],
        out_specs=[out_spec] * slots,
        scratch_shapes=[
            pltpu.VMEM((rows, 2 * HD), jnp.bfloat16),
            pltpu.VMEM((rows, 2 * HD + STAT), jnp.bfloat16),
            pltpu.VMEM((2, rows, 1), jnp.float32),
            pltpu.VMEM((2, rows, 1), jnp.float32),
            pltpu.VMEM((2, rows, HD), jnp.float32),
            pltpu.VMEM((PIECE // CHUNK, rows, CHUNK), jnp.float32),
            pltpu.VMEM((rows, 1), jnp.float32),
            pltpu.VMEM((rows, HD), jnp.float32),
        ],
    )
    pieces = P_DEV // 2
    flops = pieces * 2 * 2 * 2 * rows * PIECE * HD
    return pl.pallas_call(
        functools.partial(piece_kernel, slots),
        grid_spec=grid_spec,
        out_shape=[jax.ShapeDtypeStruct((rows, 2 * HD + STAT), jnp.bfloat16)] * slots,
        compiler_params=pltpu.CompilerParams(
            dimension_semantics=("arbitrary",), vmem_limit_bytes=48 * 1024 * 1024
        ),
        cost_estimate=pl.CostEstimate(
            flops=flops,
            transcendentals=pieces * 2 * rows * PIECE,
            bytes_accessed=pieces * 2 * PIECE * HD * 2 + slots * rows * 2 * HD * 2 * 2,
        ),
    )(table, *windows, piece_keys, piece_values, after)


def self_kernel(q_ref, k_ref, v_ref, n_ref, stat_ref):
    rows = q_ref.shape[0]
    valid = lax.broadcasted_iota(jnp.int32, (rows, rows), 1) <= lax.broadcasted_iota(
        jnp.int32, (rows, rows), 0
    )
    lane = lax.broadcasted_iota(jnp.int32, (rows, STAT), 1)
    stat = jnp.zeros((rows, STAT), jnp.float32)
    keys = k_ref[...]
    values = v_ref[...]
    for h in range(2):
        top, total, summed = head_partial(q_ref[:, h * HD:(h + 1) * HD], keys, values, valid)
        n_ref[:, h * HD:(h + 1) * HD] = summed
        stat = jnp.where(lane == 8 * h, top, stat)
        stat = jnp.where(lane == 8 * h + 3, total, stat)
    stat_ref[...] = stat


def self_attention(q, keys, values):
    rows = q.shape[0]
    return pl.pallas_call(
        self_kernel,
        out_shape=(
            jax.ShapeDtypeStruct((rows, 2 * HD), jnp.float32),
            jax.ShapeDtypeStruct((rows, STAT), jnp.float32),
        ),
        compiler_params=pltpu.CompilerParams(vmem_limit_bytes=48 * 1024 * 1024),
        cost_estimate=pl.CostEstimate(
            flops=2 * 2 * 2 * rows * rows * HD,
            transcendentals=2 * rows * rows,
            bytes_accessed=rows * 2 * HD * 2 + 2 * rows * HD * 2 + rows * (2 * HD + STAT) * 4,
        ),
    )(q, keys, values)


def combine_kernel(has_ref, *refs):
    slot_refs = refs[:P_DEV]
    sum_ref, stat_ref, out_ref = refs[P_DEV:]
    rows = out_ref.shape[0]
    lane = lax.broadcasted_iota(jnp.int32, (rows, STAT), 1)
    near_stat = stat_ref[...]
    stats = [slot_refs[d][:, 2 * HD:].astype(jnp.float32) for d in range(P_DEV)]

    def pick(stat, first, count):
        chosen = (lane >= first) & (lane < first + count)
        return jnp.sum(jnp.where(chosen, stat, 0.0), axis=1, keepdims=True)

    for h in range(2):
        tops = [pick(stats[d], 8 * h, 3) for d in range(P_DEV)]
        totals = [pick(stats[d], 8 * h + 3, 3) for d in range(P_DEV)]
        far_top = jnp.full((rows, 1), LOWEST, jnp.float32)
        for d in range(P_DEV):
            far_top = jnp.maximum(far_top, jnp.where(has_ref[d] == 1, tops[d], LOWEST))
        far_total = jnp.zeros((rows, 1), jnp.float32)
        far_sum = jnp.zeros((rows, HD), jnp.float32)
        for d in range(P_DEV):
            live = has_ref[d] == 1
            weight = jnp.where(live, totals[d] * jnp.exp(tops[d] - far_top), 0.0)
            far_total = far_total + weight
            block = slot_refs[d][:, h * HD:(h + 1) * HD].astype(jnp.float32)
            far_sum = far_sum + jnp.where(live, weight * block, 0.0)
        near_top = pick(near_stat, 8 * h, 1)
        near_total = pick(near_stat, 8 * h + 3, 1)
        final_top = jnp.maximum(far_top, near_top)
        far_scale = jnp.exp(far_top - final_top)
        near_scale = jnp.exp(near_top - final_top)
        near_sum = sum_ref[:, h * HD:(h + 1) * HD]
        out_ref[:, h * HD:(h + 1) * HD] = (
            (far_sum * far_scale + near_sum * near_scale)
            / (far_total * far_scale + near_total * near_scale)
        ).astype(out_ref.dtype)


def combine(has, slots, self_sum, self_stat):
    rows = slots[0].shape[0]
    tile = 128
    slot_spec = pl.BlockSpec((tile, 2 * HD + STAT), lambda i, t: (i, 0))
    grid_spec = pltpu.PrefetchScalarGridSpec(
        num_scalar_prefetch=1,
        grid=(rows // tile,),
        in_specs=[slot_spec] * P_DEV
        + [
            pl.BlockSpec((tile, 2 * HD), lambda i, t: (i, 0)),
            pl.BlockSpec((tile, STAT), lambda i, t: (i, 0)),
        ],
        out_specs=pl.BlockSpec((tile, 2 * HD), lambda i, t: (i, 0)),
    )
    return pl.pallas_call(
        combine_kernel,
        grid_spec=grid_spec,
        out_shape=jax.ShapeDtypeStruct((rows, 2 * HD), jnp.bfloat16),
        compiler_params=pltpu.CompilerParams(dimension_semantics=("arbitrary",)),
        cost_estimate=pl.CostEstimate(
            flops=rows * 2 * HD * 3 * P_DEV,
            transcendentals=rows * 2 * P_DEV,
            bytes_accessed=P_DEV * rows * (2 * HD + STAT) * 2 + rows * (2 * HD + STAT) * 4 + rows * 2 * HD * 2,
        ),
    )(has, *slots, self_sum, self_stat)


def finish_rows(
    proj_sum,
    tok_float,
    tok_norm,
    extra_input,
    attn_gain,
    laurel_left,
    laurel_right,
    laurel_gain,
    layer_gate,
    layer_proj,
    layer_gain,
):
    laurel_low = jnp.dot(tok_norm, laurel_left, preferred_element_type=jnp.float32).astype(
        jnp.bfloat16
    )
    laurel_out = tok_norm.astype(jnp.float32) + normed(
        jnp.dot(laurel_low, laurel_right, preferred_element_type=jnp.float32),
        laurel_gain.astype(jnp.float32),
    )
    mixture = (tok_float + normed(proj_sum, attn_gain.astype(jnp.float32)) + laurel_out) * (
        1.0 / math.sqrt(2.0)
    )
    gate_act = jnp.dot(mixture.astype(jnp.bfloat16), layer_gate, preferred_element_type=jnp.float32)
    gate_out = (jax.nn.gelu(gate_act, approximate=True) * extra_input.astype(jnp.float32)).astype(
        jnp.bfloat16
    )
    return (
        mixture
        + normed(
            jnp.dot(gate_out, layer_proj, preferred_element_type=jnp.float32),
            layer_gain.astype(jnp.float32),
        )
    ).astype(jnp.bfloat16)


def schedule_table(distances, lengths):
    ids = jnp.arange(P_DEV, dtype=jnp.int32)
    before = (distances[None, :] < distances[:, None]) | (
        (distances[None, :] == distances[:, None]) & (ids[None, :] < ids[:, None])
    )
    rank = jnp.sum(before.astype(jnp.int32), axis=1)
    chosen = rank[:, None] == ids[None, :]
    order = jnp.sum(jnp.where(chosen, ids[:, None], 0), axis=0)
    slot = jnp.sum(jnp.where(chosen, distances[:, None], 0), axis=0)
    length = jnp.sum(jnp.where(chosen, lengths[:, None], 0), axis=0)
    minus = jnp.full((1,), -1, jnp.int32)
    first = (slot != jnp.concatenate([minus, slot[:-1]])).astype(jnp.int32)
    last = (slot != jnp.concatenate([slot[1:], minus])).astype(jnp.int32)
    return order, slot, length, first, last


def stage_table(sorted_rows, kv_head, low, high):
    order, slot, length, first, last = sorted_rows
    ids = jnp.arange(P_DEV, dtype=jnp.int32)
    start = jnp.sum((slot < low).astype(jnp.int32))
    count = jnp.sum(((slot >= low) & (slot <= high)).astype(jnp.int32))
    active = (ids < count).astype(jnp.int32)
    where = jnp.clip(start + jnp.minimum(ids, jnp.maximum(count, 1) - 1), 0, P_DEV - 1)
    rows = [jnp.take(x, where) for x in (order, slot - low, length, first, last)]
    kv_row = jnp.full((P_DEV,), kv_head, jnp.int32)
    return jnp.concatenate(rows + [active, kv_row]).astype(jnp.int32)


def body(
    tokens,
    layer_input,
    input_gain,
    q_weight,
    k_weight,
    v_weight,
    q_gain,
    k_gain,
    o_weight,
    attn_gain,
    laurel_left,
    laurel_right,
    laurel_gain,
    layer_gate,
    layer_proj,
    layer_gain,
    piece_keys,
    piece_values,
    piece_owner,
    piece_len,
    cache_keys,
    cache_values,
    cache_len,
):
    req_count = lax.axis_size("req")
    tp_count = lax.axis_size("tp")
    req_index = lax.axis_index("req")
    tp_index = lax.axis_index("tp")
    local_heads = H // tp_count
    kv_head = tp_index * local_heads // (H // KVH)
    full_o_weight = lax.all_gather(o_weight, "tp", axis=0, tiled=True)
    tok_float = tokens.astype(jnp.float32)
    tok_norm = normed(tok_float, input_gain.astype(jnp.float32)).astype(jnp.bfloat16)
    queries = jnp.dot(tok_norm, q_weight, preferred_element_type=jnp.float32).reshape(
        ROWS, local_heads, HD
    )
    queries = (
        normed(queries, q_gain.astype(jnp.float32))
        .astype(jnp.bfloat16)
        .reshape(ROWS, local_heads * HD)
    )
    key_cols = lax.dynamic_slice_in_dim(k_weight, kv_head * HD, HD, 1)
    value_cols = lax.dynamic_slice_in_dim(v_weight, kv_head * HD, HD, 1)
    new_keys = normed(
        jnp.dot(tok_norm, key_cols, preferred_element_type=jnp.float32), k_gain.astype(jnp.float32)
    ).astype(jnp.bfloat16)
    new_values = normed(
        jnp.dot(tok_norm, value_cols, preferred_element_type=jnp.float32), 1.0
    ).astype(jnp.bfloat16)
    own_block = queries[:CH]
    half = P_DEV // 2
    early = [passed_along(own_block, "req", d) for d in range(1, half)]
    held = lax.optimization_barrier((own_block, *early))[0]
    late = [passed_along(held, "req", d) for d in range(half, P_DEV)]
    self_sum, self_stat = self_attention(own_block, new_keys[:CH], new_values[:CH])

    owners = lax.dynamic_slice_in_dim(piece_owner, req_index * P_DEV, P_DEV)
    lengths = lax.dynamic_slice_in_dim(piece_len, req_index * P_DEV, P_DEV)
    distances = (req_index - owners + req_count) % req_count
    sorted_rows = schedule_table(distances, lengths)
    near = piece_attention(
        stage_table(sorted_rows, kv_head, 0, half - 1), [own_block] + early,
        piece_keys, piece_values, self_stat,
    )
    far = piece_attention(
        stage_table(sorted_rows, kv_head, half, P_DEV - 1), late,
        piece_keys, piece_values, near[0],
    )
    packed = list(near) + list(far)
    slots = [packed[0]] + [passed_along(packed[d], "req", -d) for d in range(1, P_DEV)]

    block_ids = (req_index + jnp.arange(P_DEV, dtype=jnp.int32)) % req_count
    block_owners = jnp.take(piece_owner.reshape(req_count, P_DEV), block_ids, axis=0)
    has = jnp.any(block_owners == req_index, axis=1).astype(jnp.int32)
    span_att = combine(has, slots, self_sum, self_stat)
    decode_q = queries[CH:].reshape(DEC_DEV, local_heads, HD)
    cache_key = lax.dynamic_slice_in_dim(cache_keys, kv_head * HD, HD, 2)
    cache_value = lax.dynamic_slice_in_dim(cache_values, kv_head * HD, HD, 2)
    cache_scores = (
        jnp.einsum("thd,tjd->thj", decode_q, cache_key, preferred_element_type=jnp.float32)
        * SCORE_SCALE
    )
    cache_valid = (
        lax.broadcasted_iota(jnp.int32, (DEC_DEV, 1, DCACHE), 2) < cache_len[:, None, None]
    )
    cache_scores = jnp.where(cache_valid, cache_scores, LOWEST)
    own_scores = (
        jnp.einsum("thd,td->th", decode_q, new_keys[CH:], preferred_element_type=jnp.float32)
        * SCORE_SCALE
    )
    decode_top = jnp.maximum(jnp.max(cache_scores, axis=-1), own_scores)
    cache_exp = jnp.exp(cache_scores - decode_top[:, :, None])
    own_exp = jnp.exp(own_scores - decode_top)
    decode_total = jnp.sum(cache_exp, axis=-1) + own_exp
    decode_sum = (
        jnp.einsum(
            "thj,tjd->thd",
            cache_exp.astype(jnp.bfloat16),
            cache_value,
            preferred_element_type=jnp.float32,
        )
        + rounded(own_exp).astype(jnp.float32)[:, :, None]
        * new_values[CH:].astype(jnp.float32)[:, None, :]
    )
    decode_att = (
        (decode_sum / decode_total[:, :, None])
        .reshape(DEC_DEV, local_heads * HD)
        .astype(jnp.bfloat16)
    )
    attended = jnp.concatenate([span_att, decode_att], axis=0)
    part = CH // tp_count

    def rows_of(x, owner):
        return jnp.concatenate(
            [lax.dynamic_slice_in_dim(x, owner * part, part, 0), x[CH:]], axis=0
        )

    row_parts = [rows_of(attended, tp_index)]
    weight_parts = [o_weight]
    for shift in range(1, tp_count):
        target = (tp_index + shift) % tp_count
        row_parts.append(passed_along(rows_of(attended, target), "tp", shift))
        weight_parts.append(passed_along(o_weight, "tp", shift))
    proj_sum = jnp.dot(
        jnp.concatenate(row_parts, axis=1),
        jnp.concatenate(weight_parts, axis=0),
        preferred_element_type=jnp.float32,
    )
    mine = finish_rows(
        proj_sum,
        rows_of(tok_float, tp_index),
        rows_of(tok_norm, tp_index),
        rows_of(layer_input, tp_index),
        attn_gain,
        laurel_left,
        laurel_right,
        laurel_gain,
        layer_gate,
        layer_proj,
        layer_gain,
    )
    gathered = [mine] + [passed_along(mine, "tp", shift) for shift in range(1, tp_count)]

    def assemble(me):
        def build(*got):
            blocks = [got[(me - owner) % tp_count][:part] for owner in range(tp_count)]
            return jnp.concatenate(blocks + [got[me][part:]], axis=0)

        return build

    return lax.switch(tp_index, [assemble(me) for me in range(tp_count)], *gathered)


def solution(mesh):
    placed = (
        P("req", None),
        P("req", None),
        P(),
        P(None, "tp"),
        P(),
        P(),
        P(),
        P(),
        P("tp", None),
        P(),
        P(),
        P(),
        P(),
        P(),
        P(),
        P(),
        P("req", None, None),
        P("req", None, None),
        P(),
        P(),
        P("req", None, None),
        P("req", None, None),
        P("req"),
    )
    return jax.shard_map(
        body, mesh=mesh, in_specs=placed, out_specs=P("req", None), check_vma=False
    )
```

```python
import functools
import math

import jax
import jax.numpy as jnp
from jax import lax
from jax.experimental import pallas as pl
from jax.experimental.pallas import tpu as pltpu
from jax.sharding import PartitionSpec as P

H = 8
KVH = 2
HD = 256
CH = 512
DEC_DEV = 4
P_DEV = 8
PIECE = 1024
DCACHE = 512
ROWS = 516
STAT = 128
CHUNK = 256


LOWEST = -1e30
SCORE_SCALE = 1.0 / math.sqrt(HD)


def passed_along(x, axis, by):
    length = lax.axis_size(axis)
    return lax.ppermute(x, axis, [(i, (i + by) % length) for i in range(length)])


def rounded(x):
    return lax.optimization_barrier(x.astype(jnp.bfloat16))


def normed(x, scale_gain):
    return x * lax.rsqrt(jnp.mean(x * x, axis=-1, keepdims=True) + 1e-06) * scale_gain


def head_partial(q, keys, values, valid):
    scores = lax.dot_general(q, keys, (((1,), (1,)), ((), ())), preferred_element_type=jnp.float32)
    scores = jnp.where(valid, scores, LOWEST)
    top = jnp.max(scores, axis=1, keepdims=True)
    weights = jnp.exp((scores - top) * SCORE_SCALE)
    total = jnp.sum(weights, axis=1, keepdims=True)
    summed = jnp.dot(weights.astype(jnp.bfloat16), values, preferred_element_type=jnp.float32)
    return top * SCORE_SCALE, total, summed


def split3(x):
    hi = x.astype(jnp.bfloat16).astype(jnp.float32)
    rest = x - hi
    mid = rest.astype(jnp.bfloat16).astype(jnp.float32)
    lo = rest - mid
    return hi, mid, lo


def piece_kernel(slots, tab_ref, *refs):
    q_refs = refs[:slots]
    k_ref, v_ref = refs[slots:slots + 2]
    out_refs = refs[slots + 3:2 * slots + 3]
    scratch = refs[2 * slots + 3:]
    step = pl.program_id(0)

    @pl.when(tab_ref[5 * P_DEV + step] == 1)
    def _():
        piece_step(step, tab_ref, q_refs, k_ref, v_ref, out_refs, *scratch)


def piece_step(step, tab_ref, q_refs, k_ref, v_ref, out_refs, qbuf, fin, acc_m, acc_l, acc_n, sbuf, lbuf, nbuf):
    slots = len(q_refs)
    slot = tab_ref[P_DEV + step]
    length = tab_ref[2 * P_DEV + step]
    first = tab_ref[3 * P_DEV + step]
    last = tab_ref[4 * P_DEV + step]
    for k in range(slots):

        @pl.when(slot == k)
        def _(k=k):
            qbuf[...] = q_refs[k][...]

    rows = qbuf.shape[0]
    chunks = (length + CHUNK - 1) // CHUNK
    for h in range(2):
        q = qbuf[:, h * HD:(h + 1) * HD]

        def score_chunk(c, top, q=q):
            start = pl.multiple_of(c * CHUNK, CHUNK)
            scores = lax.dot_general(
                q, k_ref[0, pl.ds(start, CHUNK), :], (((1,), (1,)), ((), ())),
                preferred_element_type=jnp.float32,
            )
            valid = lax.broadcasted_iota(jnp.int32, (rows, CHUNK), 1) + start < length
            scores = jnp.where(valid, scores, LOWEST)
            sbuf[c] = scores
            return jnp.maximum(top, jnp.max(scores, axis=1, keepdims=True))

        top = lax.fori_loop(0, chunks, score_chunk, jnp.full((rows, 1), LOWEST, jnp.float32))
        lbuf[...] = jnp.zeros_like(lbuf)
        nbuf[...] = jnp.zeros_like(nbuf)

        @pl.loop(0, chunks)
        def _(c, top=top):
            start = pl.multiple_of(c * CHUNK, CHUNK)
            weights = jnp.exp((sbuf[c] - top) * SCORE_SCALE)
            lbuf[...] += jnp.sum(weights, axis=1, keepdims=True)
            nbuf[...] += jnp.dot(
                weights.astype(jnp.bfloat16), v_ref[0, pl.ds(start, CHUNK), :],
                preferred_element_type=jnp.float32,
            )

        top = top * SCORE_SCALE

        @pl.when(first == 1)
        def _(h=h, top=top):
            acc_m[h] = top
            acc_l[h] = lbuf[...]
            acc_n[h] = nbuf[...]

        @pl.when(first == 0)
        def _(h=h, top=top):
            old = acc_m[h]
            new = jnp.maximum(old, top)
            keep = jnp.exp(old - new)
            add = jnp.exp(top - new)
            acc_l[h] = acc_l[h] * keep + lbuf[...] * add
            acc_n[h] = acc_n[h] * keep + nbuf[...] * add
            acc_m[h] = new

    @pl.when(last == 1)
    def _():
        lane = lax.broadcasted_iota(jnp.int32, (rows, STAT), 1)
        stat = jnp.zeros((rows, STAT), jnp.float32)
        for h in range(2):
            total = acc_l[h]
            fin[:, h * HD:(h + 1) * HD] = (acc_n[h] / total).astype(jnp.bfloat16)
            for i, part in enumerate(split3(acc_m[h]) + split3(total)):
                stat = jnp.where(lane == 8 * h + i, part, stat)
        fin[:, 2 * HD:] = stat.astype(jnp.bfloat16)
        for k in range(slots):

            @pl.when(slot == k)
            def _(k=k):
                out_refs[k][...] = fin[...]


def piece_attention(table, windows, piece_keys, piece_values, after):
    rows = windows[0].shape[0]
    slots = len(windows)
    q_spec = pl.BlockSpec((rows, 2 * HD), lambda s, t: (0, 0))
    kv_spec = pl.BlockSpec((1, PIECE, HD), lambda s, t: (t[s], 0, t[6 * P_DEV]))
    out_spec = pl.BlockSpec((rows, 2 * HD + STAT), lambda s, t: (0, 0))
    grid_spec = pltpu.PrefetchScalarGridSpec(
        num_scalar_prefetch=1,
        grid=(P_DEV,),
        in_specs=[q_spec] * slots + [kv_spec, kv_spec, pl.BlockSpec(memory_space=pl.ANY)],
        out_specs=[out_spec] * slots,
        scratch_shapes=[
            pltpu.VMEM((rows, 2 * HD), jnp.bfloat16),
            pltpu.VMEM((rows, 2 * HD + STAT), jnp.bfloat16),
            pltpu.VMEM((2, rows, 1), jnp.float32),
            pltpu.VMEM((2, rows, 1), jnp.float32),
            pltpu.VMEM((2, rows, HD), jnp.float32),
            pltpu.VMEM((PIECE // CHUNK, rows, CHUNK), jnp.float32),
            pltpu.VMEM((rows, 1), jnp.float32),
            pltpu.VMEM((rows, HD), jnp.float32),
        ],
    )
    pieces = P_DEV // 2
    flops = pieces * 2 * 2 * 2 * rows * PIECE * HD
    return pl.pallas_call(
        functools.partial(piece_kernel, slots),
        grid_spec=grid_spec,
        out_shape=[jax.ShapeDtypeStruct((rows, 2 * HD + STAT), jnp.bfloat16)] * slots,
        compiler_params=pltpu.CompilerParams(
            dimension_semantics=("arbitrary",), vmem_limit_bytes=48 * 1024 * 1024
        ),
        cost_estimate=pl.CostEstimate(
            flops=flops,
            transcendentals=pieces * 2 * rows * PIECE,
            bytes_accessed=pieces * 2 * PIECE * HD * 2 + slots * rows * 2 * HD * 2 * 2,
        ),
    )(table, *windows, piece_keys, piece_values, after)


def self_kernel(q_ref, k_ref, v_ref, n_ref, stat_ref):
    rows = q_ref.shape[0]
    valid = lax.broadcasted_iota(jnp.int32, (rows, rows), 1) <= lax.broadcasted_iota(
        jnp.int32, (rows, rows), 0
    )
    lane = lax.broadcasted_iota(jnp.int32, (rows, STAT), 1)
    stat = jnp.zeros((rows, STAT), jnp.float32)
    keys = k_ref[...]
    values = v_ref[...]
    for h in range(2):
        top, total, summed = head_partial(q_ref[:, h * HD:(h + 1) * HD], keys, values, valid)
        n_ref[:, h * HD:(h + 1) * HD] = summed
        stat = jnp.where(lane == 8 * h, top, stat)
        stat = jnp.where(lane == 8 * h + 3, total, stat)
    stat_ref[...] = stat


def self_attention(q, keys, values):
    rows = q.shape[0]
    return pl.pallas_call(
        self_kernel,
        out_shape=(
            jax.ShapeDtypeStruct((rows, 2 * HD), jnp.float32),
            jax.ShapeDtypeStruct((rows, STAT), jnp.float32),
        ),
        compiler_params=pltpu.CompilerParams(vmem_limit_bytes=48 * 1024 * 1024),
        cost_estimate=pl.CostEstimate(
            flops=2 * 2 * 2 * rows * rows * HD,
            transcendentals=2 * rows * rows,
            bytes_accessed=rows * 2 * HD * 2 + 2 * rows * HD * 2 + rows * (2 * HD + STAT) * 4,
        ),
    )(q, keys, values)


def combine_kernel(has_ref, *refs):
    slot_refs = refs[:P_DEV]
    sum_ref, stat_ref, out_ref = refs[P_DEV:]
    rows = out_ref.shape[0]
    lane = lax.broadcasted_iota(jnp.int32, (rows, STAT), 1)
    near_stat = stat_ref[...]
    stats = [slot_refs[d][:, 2 * HD:].astype(jnp.float32) for d in range(P_DEV)]

    def pick(stat, first, count):
        chosen = (lane >= first) & (lane < first + count)
        return jnp.sum(jnp.where(chosen, stat, 0.0), axis=1, keepdims=True)

    for h in range(2):
        tops = [pick(stats[d], 8 * h, 3) for d in range(P_DEV)]
        totals = [pick(stats[d], 8 * h + 3, 3) for d in range(P_DEV)]
        far_top = jnp.full((rows, 1), LOWEST, jnp.float32)
        for d in range(P_DEV):
            far_top = jnp.maximum(far_top, jnp.where(has_ref[d] == 1, tops[d], LOWEST))
        far_total = jnp.zeros((rows, 1), jnp.float32)
        far_sum = jnp.zeros((rows, HD), jnp.float32)
        for d in range(P_DEV):
            live = has_ref[d] == 1
            weight = jnp.where(live, totals[d] * jnp.exp(tops[d] - far_top), 0.0)
            far_total = far_total + weight
            block = slot_refs[d][:, h * HD:(h + 1) * HD].astype(jnp.float32)
            far_sum = far_sum + jnp.where(live, weight * block, 0.0)
        near_top = pick(near_stat, 8 * h, 1)
        near_total = pick(near_stat, 8 * h + 3, 1)
        final_top = jnp.maximum(far_top, near_top)
        far_scale = jnp.exp(far_top - final_top)
        near_scale = jnp.exp(near_top - final_top)
        near_sum = sum_ref[:, h * HD:(h + 1) * HD]
        out_ref[:, h * HD:(h + 1) * HD] = (
            (far_sum * far_scale + near_sum * near_scale)
            / (far_total * far_scale + near_total * near_scale)
        ).astype(out_ref.dtype)


def combine(has, slots, self_sum, self_stat):
    rows = slots[0].shape[0]
    tile = 256
    slot_spec = pl.BlockSpec((tile, 2 * HD + STAT), lambda i, t: (i, 0))
    grid_spec = pltpu.PrefetchScalarGridSpec(
        num_scalar_prefetch=1,
        grid=(rows // tile,),
        in_specs=[slot_spec] * P_DEV
        + [
            pl.BlockSpec((tile, 2 * HD), lambda i, t: (i, 0)),
            pl.BlockSpec((tile, STAT), lambda i, t: (i, 0)),
        ],
        out_specs=pl.BlockSpec((tile, 2 * HD), lambda i, t: (i, 0)),
    )
    return pl.pallas_call(
        combine_kernel,
        grid_spec=grid_spec,
        out_shape=jax.ShapeDtypeStruct((rows, 2 * HD), jnp.bfloat16),
        compiler_params=pltpu.CompilerParams(dimension_semantics=("arbitrary",)),
        cost_estimate=pl.CostEstimate(
            flops=rows * 2 * HD * 3 * P_DEV,
            transcendentals=rows * 2 * P_DEV,
            bytes_accessed=P_DEV * rows * (2 * HD + STAT) * 2 + rows * (2 * HD + STAT) * 4 + rows * 2 * HD * 2,
        ),
    )(has, *slots, self_sum, self_stat)


def finish_rows(
    proj_sum,
    tok_float,
    tok_norm,
    extra_input,
    attn_gain,
    laurel_left,
    laurel_right,
    laurel_gain,
    layer_gate,
    layer_proj,
    layer_gain,
):
    laurel_low = jnp.dot(tok_norm, laurel_left, preferred_element_type=jnp.float32).astype(
        jnp.bfloat16
    )
    laurel_out = tok_norm.astype(jnp.float32) + normed(
        jnp.dot(laurel_low, laurel_right, preferred_element_type=jnp.float32),
        laurel_gain.astype(jnp.float32),
    )
    mixture = (tok_float + normed(proj_sum, attn_gain.astype(jnp.float32)) + laurel_out) * (
        1.0 / math.sqrt(2.0)
    )
    gate_act = jnp.dot(mixture.astype(jnp.bfloat16), layer_gate, preferred_element_type=jnp.float32)
    gate_out = (jax.nn.gelu(gate_act, approximate=True) * extra_input.astype(jnp.float32)).astype(
        jnp.bfloat16
    )
    return (
        mixture
        + normed(
            jnp.dot(gate_out, layer_proj, preferred_element_type=jnp.float32),
            layer_gain.astype(jnp.float32),
        )
    ).astype(jnp.bfloat16)


def schedule_table(distances, lengths):
    ids = jnp.arange(P_DEV, dtype=jnp.int32)
    before = (distances[None, :] < distances[:, None]) | (
        (distances[None, :] == distances[:, None]) & (ids[None, :] < ids[:, None])
    )
    rank = jnp.sum(before.astype(jnp.int32), axis=1)
    chosen = rank[:, None] == ids[None, :]
    order = jnp.sum(jnp.where(chosen, ids[:, None], 0), axis=0)
    slot = jnp.sum(jnp.where(chosen, distances[:, None], 0), axis=0)
    length = jnp.sum(jnp.where(chosen, lengths[:, None], 0), axis=0)
    minus = jnp.full((1,), -1, jnp.int32)
    first = (slot != jnp.concatenate([minus, slot[:-1]])).astype(jnp.int32)
    last = (slot != jnp.concatenate([slot[1:], minus])).astype(jnp.int32)
    return order, slot, length, first, last


def stage_table(sorted_rows, kv_head, low, high):
    order, slot, length, first, last = sorted_rows
    ids = jnp.arange(P_DEV, dtype=jnp.int32)
    start = jnp.sum((slot < low).astype(jnp.int32))
    count = jnp.sum(((slot >= low) & (slot <= high)).astype(jnp.int32))
    active = (ids < count).astype(jnp.int32)
    where = jnp.clip(start + jnp.minimum(ids, jnp.maximum(count, 1) - 1), 0, P_DEV - 1)
    rows = [jnp.take(x, where) for x in (order, slot - low, length, first, last)]
    kv_row = jnp.full((P_DEV,), kv_head, jnp.int32)
    return jnp.concatenate(rows + [active, kv_row]).astype(jnp.int32)


def body(
    tokens,
    layer_input,
    input_gain,
    q_weight,
    k_weight,
    v_weight,
    q_gain,
    k_gain,
    o_weight,
    attn_gain,
    laurel_left,
    laurel_right,
    laurel_gain,
    layer_gate,
    layer_proj,
    layer_gain,
    piece_keys,
    piece_values,
    piece_owner,
    piece_len,
    cache_keys,
    cache_values,
    cache_len,
):
    req_count = lax.axis_size("req")
    tp_count = lax.axis_size("tp")
    req_index = lax.axis_index("req")
    tp_index = lax.axis_index("tp")
    local_heads = H // tp_count
    kv_head = tp_index * local_heads // (H // KVH)
    full_o_weight = lax.all_gather(o_weight, "tp", axis=0, tiled=True)
    tok_float = tokens.astype(jnp.float32)
    tok_norm = normed(tok_float, input_gain.astype(jnp.float32)).astype(jnp.bfloat16)
    queries = jnp.dot(tok_norm, q_weight, preferred_element_type=jnp.float32).reshape(
        ROWS, local_heads, HD
    )
    queries = (
        normed(queries, q_gain.astype(jnp.float32))
        .astype(jnp.bfloat16)
        .reshape(ROWS, local_heads * HD)
    )
    key_cols = lax.dynamic_slice_in_dim(k_weight, kv_head * HD, HD, 1)
    value_cols = lax.dynamic_slice_in_dim(v_weight, kv_head * HD, HD, 1)
    new_keys = normed(
        jnp.dot(tok_norm, key_cols, preferred_element_type=jnp.float32), k_gain.astype(jnp.float32)
    ).astype(jnp.bfloat16)
    new_values = normed(
        jnp.dot(tok_norm, value_cols, preferred_element_type=jnp.float32), 1.0
    ).astype(jnp.bfloat16)
    own_block = queries[:CH]
    half = P_DEV // 2
    early = [passed_along(own_block, "req", d) for d in range(1, half)]
    held = lax.optimization_barrier((own_block, *early))[0]
    late = [passed_along(held, "req", d) for d in range(half, P_DEV)]
    self_sum, self_stat = self_attention(own_block, new_keys[:CH], new_values[:CH])

    owners = lax.dynamic_slice_in_dim(piece_owner, req_index * P_DEV, P_DEV)
    lengths = lax.dynamic_slice_in_dim(piece_len, req_index * P_DEV, P_DEV)
    distances = (req_index - owners + req_count) % req_count
    sorted_rows = schedule_table(distances, lengths)
    near = piece_attention(
        stage_table(sorted_rows, kv_head, 0, half - 1), [own_block] + early,
        piece_keys, piece_values, self_stat,
    )
    far = piece_attention(
        stage_table(sorted_rows, kv_head, half, P_DEV - 1), late,
        piece_keys, piece_values, near[0],
    )
    packed = list(near) + list(far)
    slots = [packed[0]] + [passed_along(packed[d], "req", -d) for d in range(1, P_DEV)]

    block_ids = (req_index + jnp.arange(P_DEV, dtype=jnp.int32)) % req_count
    block_owners = jnp.take(piece_owner.reshape(req_count, P_DEV), block_ids, axis=0)
    has = jnp.any(block_owners == req_index, axis=1).astype(jnp.int32)
    span_att = combine(has, slots, self_sum, self_stat)
    decode_q = queries[CH:].reshape(DEC_DEV, local_heads, HD)
    cache_key = lax.dynamic_slice_in_dim(cache_keys, kv_head * HD, HD, 2)
    cache_value = lax.dynamic_slice_in_dim(cache_values, kv_head * HD, HD, 2)
    cache_scores = (
        jnp.einsum("thd,tjd->thj", decode_q, cache_key, preferred_element_type=jnp.float32)
        * SCORE_SCALE
    )
    cache_valid = (
        lax.broadcasted_iota(jnp.int32, (DEC_DEV, 1, DCACHE), 2) < cache_len[:, None, None]
    )
    cache_scores = jnp.where(cache_valid, cache_scores, LOWEST)
    own_scores = (
        jnp.einsum("thd,td->th", decode_q, new_keys[CH:], preferred_element_type=jnp.float32)
        * SCORE_SCALE
    )
    decode_top = jnp.maximum(jnp.max(cache_scores, axis=-1), own_scores)
    cache_exp = jnp.exp(cache_scores - decode_top[:, :, None])
    own_exp = jnp.exp(own_scores - decode_top)
    decode_total = jnp.sum(cache_exp, axis=-1) + own_exp
    decode_sum = (
        jnp.einsum(
            "thj,tjd->thd",
            cache_exp.astype(jnp.bfloat16),
            cache_value,
            preferred_element_type=jnp.float32,
        )
        + rounded(own_exp).astype(jnp.float32)[:, :, None]
        * new_values[CH:].astype(jnp.float32)[:, None, :]
    )
    decode_att = (
        (decode_sum / decode_total[:, :, None])
        .reshape(DEC_DEV, local_heads * HD)
        .astype(jnp.bfloat16)
    )
    attended = jnp.concatenate([span_att, decode_att], axis=0)
    part = CH // tp_count

    def rows_of(x, owner):
        return jnp.concatenate(
            [lax.dynamic_slice_in_dim(x, owner * part, part, 0), x[CH:]], axis=0
        )

    proj_sum = jnp.dot(rows_of(attended, tp_index), o_weight, preferred_element_type=jnp.float32)
    for shift in range(1, tp_count):
        target = (tp_index + shift) % tp_count
        got_rows = passed_along(rows_of(attended, target), "tp", shift)
        got_weight = passed_along(o_weight, "tp", shift)
        proj_sum = proj_sum + jnp.dot(got_rows, got_weight, preferred_element_type=jnp.float32)
    mine = finish_rows(
        proj_sum,
        rows_of(tok_float, tp_index),
        rows_of(tok_norm, tp_index),
        rows_of(layer_input, tp_index),
        attn_gain,
        laurel_left,
        laurel_right,
        laurel_gain,
        layer_gate,
        layer_proj,
        layer_gain,
    )
    gathered = [mine] + [passed_along(mine, "tp", shift) for shift in range(1, tp_count)]

    def assemble(me):
        def build(*got):
            blocks = [got[(me - owner) % tp_count][:part] for owner in range(tp_count)]
            return jnp.concatenate(blocks + [got[me][part:]], axis=0)

        return build

    return lax.switch(tp_index, [assemble(me) for me in range(tp_count)], *gathered)


def solution(mesh):
    placed = (
        P("req", None),
        P("req", None),
        P(),
        P(None, "tp"),
        P(),
        P(),
        P(),
        P(),
        P("tp", None),
        P(),
        P(),
        P(),
        P(),
        P(),
        P(),
        P(),
        P("req", None, None),
        P("req", None, None),
        P(),
        P(),
        P("req", None, None),
        P("req", None, None),
        P("req"),
    )
    return jax.shard_map(
        body, mesh=mesh, in_specs=placed, out_specs=P("req", None), check_vma=False
    )
```

```python
import functools
import math

import jax
import jax.numpy as jnp
from jax import lax
from jax.experimental import pallas as pl
from jax.experimental.pallas import tpu as pltpu
from jax.sharding import PartitionSpec as P

H = 8
KVH = 2
HD = 256
CH = 512
DEC_DEV = 4
P_DEV = 8
PIECE = 1024
DCACHE = 512
ROWS = 516
STAT = 128
CHUNK = 256


LOWEST = -1e30
SCORE_SCALE = 1.0 / math.sqrt(HD)


def passed_along(x, axis, by):
    length = lax.axis_size(axis)
    return lax.ppermute(x, axis, [(i, (i + by) % length) for i in range(length)])


def rounded(x):
    return lax.optimization_barrier(x.astype(jnp.bfloat16))


def normed(x, scale_gain):
    return x * lax.rsqrt(jnp.mean(x * x, axis=-1, keepdims=True) + 1e-06) * scale_gain


def head_partial(q, keys, values, valid):
    scores = lax.dot_general(q, keys, (((1,), (1,)), ((), ())), preferred_element_type=jnp.float32)
    scores = jnp.where(valid, scores, LOWEST)
    top = jnp.max(scores, axis=1, keepdims=True)
    weights = jnp.exp((scores - top) * SCORE_SCALE)
    total = jnp.sum(weights, axis=1, keepdims=True)
    summed = jnp.dot(weights.astype(jnp.bfloat16), values, preferred_element_type=jnp.float32)
    return top * SCORE_SCALE, total, summed


def split3(x):
    hi = x.astype(jnp.bfloat16).astype(jnp.float32)
    rest = x - hi
    mid = rest.astype(jnp.bfloat16).astype(jnp.float32)
    lo = rest - mid
    return hi, mid, lo


def piece_kernel(slots, tab_ref, *refs):
    q_refs = refs[:slots]
    k_ref, v_ref = refs[slots:slots + 2]
    out_refs = refs[slots + 3:2 * slots + 3]
    scratch = refs[2 * slots + 3:]
    step = pl.program_id(0)

    @pl.when(tab_ref[5 * P_DEV + step] == 1)
    def _():
        piece_step(step, tab_ref, q_refs, k_ref, v_ref, out_refs, *scratch)


def piece_step(step, tab_ref, q_refs, k_ref, v_ref, out_refs, qbuf, fin, acc_m, acc_l, acc_n, sbuf, lbuf, nbuf):
    slots = len(q_refs)
    slot = tab_ref[P_DEV + step]
    length = tab_ref[2 * P_DEV + step]
    first = tab_ref[3 * P_DEV + step]
    last = tab_ref[4 * P_DEV + step]
    for k in range(slots):

        @pl.when(slot == k)
        def _(k=k):
            qbuf[...] = q_refs[k][...]

    rows = qbuf.shape[0]
    chunks = (length + CHUNK - 1) // CHUNK
    for h in range(2):
        q = qbuf[:, h * HD:(h + 1) * HD]

        def score_chunk(c, top, q=q):
            start = pl.multiple_of(c * CHUNK, CHUNK)
            scores = lax.dot_general(
                q, k_ref[0, pl.ds(start, CHUNK), :], (((1,), (1,)), ((), ())),
                preferred_element_type=jnp.float32,
            )
            valid = lax.broadcasted_iota(jnp.int32, (rows, CHUNK), 1) + start < length
            scores = jnp.where(valid, scores, LOWEST)
            sbuf[c] = scores
            return jnp.maximum(top, jnp.max(scores, axis=1, keepdims=True))

        top = lax.fori_loop(0, chunks, score_chunk, jnp.full((rows, 1), LOWEST, jnp.float32))
        lbuf[...] = jnp.zeros_like(lbuf)
        nbuf[...] = jnp.zeros_like(nbuf)

        @pl.loop(0, chunks)
        def _(c, top=top):
            start = pl.multiple_of(c * CHUNK, CHUNK)
            weights = jnp.exp((sbuf[c] - top) * SCORE_SCALE)
            lbuf[...] += jnp.sum(weights, axis=1, keepdims=True)
            nbuf[...] += jnp.dot(
                weights.astype(jnp.bfloat16), v_ref[0, pl.ds(start, CHUNK), :],
                preferred_element_type=jnp.float32,
            )

        top = top * SCORE_SCALE

        @pl.when(first == 1)
        def _(h=h, top=top):
            acc_m[h] = top
            acc_l[h] = lbuf[...]
            acc_n[h] = nbuf[...]

        @pl.when(first == 0)
        def _(h=h, top=top):
            old = acc_m[h]
            new = jnp.maximum(old, top)
            keep = jnp.exp(old - new)
            add = jnp.exp(top - new)
            acc_l[h] = acc_l[h] * keep + lbuf[...] * add
            acc_n[h] = acc_n[h] * keep + nbuf[...] * add
            acc_m[h] = new

    @pl.when(last == 1)
    def _():
        lane = lax.broadcasted_iota(jnp.int32, (rows, STAT), 1)
        stat = jnp.zeros((rows, STAT), jnp.float32)
        for h in range(2):
            total = acc_l[h]
            fin[:, h * HD:(h + 1) * HD] = (acc_n[h] / total).astype(jnp.bfloat16)
            for i, part in enumerate(split3(acc_m[h]) + split3(total)):
                stat = jnp.where(lane == 8 * h + i, part, stat)
        fin[:, 2 * HD:] = stat.astype(jnp.bfloat16)
        for k in range(slots):

            @pl.when(slot == k)
            def _(k=k):
                out_refs[k][...] = fin[...]


def piece_attention(table, windows, piece_keys, piece_values, after):
    rows = windows[0].shape[0]
    slots = len(windows)
    q_spec = pl.BlockSpec((rows, 2 * HD), lambda s, t: (0, 0))
    kv_spec = pl.BlockSpec((1, PIECE, HD), lambda s, t: (t[s], 0, t[6 * P_DEV]))
    out_spec = pl.BlockSpec((rows, 2 * HD + STAT), lambda s, t: (0, 0))
    grid_spec = pltpu.PrefetchScalarGridSpec(
        num_scalar_prefetch=1,
        grid=(P_DEV,),
        in_specs=[q_spec] * slots + [kv_spec, kv_spec, pl.BlockSpec(memory_space=pl.ANY)],
        out_specs=[out_spec] * slots,
        scratch_shapes=[
            pltpu.VMEM((rows, 2 * HD), jnp.bfloat16),
            pltpu.VMEM((rows, 2 * HD + STAT), jnp.bfloat16),
            pltpu.VMEM((2, rows, 1), jnp.float32),
            pltpu.VMEM((2, rows, 1), jnp.float32),
            pltpu.VMEM((2, rows, HD), jnp.float32),
            pltpu.VMEM((PIECE // CHUNK, rows, CHUNK), jnp.float32),
            pltpu.VMEM((rows, 1), jnp.float32),
            pltpu.VMEM((rows, HD), jnp.float32),
        ],
    )
    pieces = P_DEV // 2
    flops = pieces * 2 * 2 * 2 * rows * PIECE * HD
    return pl.pallas_call(
        functools.partial(piece_kernel, slots),
        grid_spec=grid_spec,
        out_shape=[jax.ShapeDtypeStruct((rows, 2 * HD + STAT), jnp.bfloat16)] * slots,
        compiler_params=pltpu.CompilerParams(
            dimension_semantics=("arbitrary",), vmem_limit_bytes=48 * 1024 * 1024
        ),
        cost_estimate=pl.CostEstimate(
            flops=flops,
            transcendentals=pieces * 2 * rows * PIECE,
            bytes_accessed=pieces * 2 * PIECE * HD * 2 + slots * rows * 2 * HD * 2 * 2,
        ),
    )(table, *windows, piece_keys, piece_values, after)


def self_kernel(q_ref, k_ref, v_ref, n_ref, stat_ref):
    rows = q_ref.shape[0]
    valid = lax.broadcasted_iota(jnp.int32, (rows, rows), 1) <= lax.broadcasted_iota(
        jnp.int32, (rows, rows), 0
    )
    lane = lax.broadcasted_iota(jnp.int32, (rows, STAT), 1)
    stat = jnp.zeros((rows, STAT), jnp.float32)
    keys = k_ref[...]
    values = v_ref[...]
    for h in range(2):
        top, total, summed = head_partial(q_ref[:, h * HD:(h + 1) * HD], keys, values, valid)
        n_ref[:, h * HD:(h + 1) * HD] = summed
        stat = jnp.where(lane == 8 * h, top, stat)
        stat = jnp.where(lane == 8 * h + 3, total, stat)
    stat_ref[...] = stat


def self_attention(q, keys, values):
    rows = q.shape[0]
    return pl.pallas_call(
        self_kernel,
        out_shape=(
            jax.ShapeDtypeStruct((rows, 2 * HD), jnp.float32),
            jax.ShapeDtypeStruct((rows, STAT), jnp.float32),
        ),
        compiler_params=pltpu.CompilerParams(vmem_limit_bytes=48 * 1024 * 1024),
        cost_estimate=pl.CostEstimate(
            flops=2 * 2 * 2 * rows * rows * HD,
            transcendentals=2 * rows * rows,
            bytes_accessed=rows * 2 * HD * 2 + 2 * rows * HD * 2 + rows * (2 * HD + STAT) * 4,
        ),
    )(q, keys, values)


def combine_kernel(has_ref, *refs):
    slot_refs = refs[:P_DEV]
    sum_ref, stat_ref, out_ref = refs[P_DEV:]
    rows = out_ref.shape[0]
    lane = lax.broadcasted_iota(jnp.int32, (rows, STAT), 1)
    near_stat = stat_ref[...]
    stats = [slot_refs[d][:, 2 * HD:].astype(jnp.float32) for d in range(P_DEV)]

    def pick(stat, first, count):
        chosen = (lane >= first) & (lane < first + count)
        return jnp.sum(jnp.where(chosen, stat, 0.0), axis=1, keepdims=True)

    for h in range(2):
        tops = [pick(stats[d], 8 * h, 3) for d in range(P_DEV)]
        totals = [pick(stats[d], 8 * h + 3, 3) for d in range(P_DEV)]
        far_top = jnp.full((rows, 1), LOWEST, jnp.float32)
        for d in range(P_DEV):
            far_top = jnp.maximum(far_top, jnp.where(has_ref[d] == 1, tops[d], LOWEST))
        far_total = jnp.zeros((rows, 1), jnp.float32)
        far_sum = jnp.zeros((rows, HD), jnp.float32)
        for d in range(P_DEV):
            live = has_ref[d] == 1
            weight = jnp.where(live, totals[d] * jnp.exp(tops[d] - far_top), 0.0)
            far_total = far_total + weight
            block = slot_refs[d][:, h * HD:(h + 1) * HD].astype(jnp.float32)
            far_sum = far_sum + jnp.where(live, weight * block, 0.0)
        near_top = pick(near_stat, 8 * h, 1)
        near_total = pick(near_stat, 8 * h + 3, 1)
        final_top = jnp.maximum(far_top, near_top)
        far_scale = jnp.exp(far_top - final_top)
        near_scale = jnp.exp(near_top - final_top)
        near_sum = sum_ref[:, h * HD:(h + 1) * HD]
        out_ref[:, h * HD:(h + 1) * HD] = (
            (far_sum * far_scale + near_sum * near_scale)
            / (far_total * far_scale + near_total * near_scale)
        ).astype(out_ref.dtype)


def combine(has, slots, self_sum, self_stat):
    rows = slots[0].shape[0]
    tile = 512
    slot_spec = pl.BlockSpec((tile, 2 * HD + STAT), lambda i, t: (i, 0))
    grid_spec = pltpu.PrefetchScalarGridSpec(
        num_scalar_prefetch=1,
        grid=(rows // tile,),
        in_specs=[slot_spec] * P_DEV
        + [
            pl.BlockSpec((tile, 2 * HD), lambda i, t: (i, 0)),
            pl.BlockSpec((tile, STAT), lambda i, t: (i, 0)),
        ],
        out_specs=pl.BlockSpec((tile, 2 * HD), lambda i, t: (i, 0)),
    )
    return pl.pallas_call(
        combine_kernel,
        grid_spec=grid_spec,
        out_shape=jax.ShapeDtypeStruct((rows, 2 * HD), jnp.bfloat16),
        compiler_params=pltpu.CompilerParams(
            dimension_semantics=("arbitrary",), vmem_limit_bytes=48 * 1024 * 1024
        ),
        cost_estimate=pl.CostEstimate(
            flops=rows * 2 * HD * 3 * P_DEV,
            transcendentals=rows * 2 * P_DEV,
            bytes_accessed=P_DEV * rows * (2 * HD + STAT) * 2 + rows * (2 * HD + STAT) * 4 + rows * 2 * HD * 2,
        ),
    )(has, *slots, self_sum, self_stat)


def finish_rows(
    proj_sum,
    tok_float,
    tok_norm,
    extra_input,
    attn_gain,
    laurel_left,
    laurel_right,
    laurel_gain,
    layer_gate,
    layer_proj,
    layer_gain,
):
    laurel_low = jnp.dot(tok_norm, laurel_left, preferred_element_type=jnp.float32).astype(
        jnp.bfloat16
    )
    laurel_out = tok_norm.astype(jnp.float32) + normed(
        jnp.dot(laurel_low, laurel_right, preferred_element_type=jnp.float32),
        laurel_gain.astype(jnp.float32),
    )
    mixture = (tok_float + normed(proj_sum, attn_gain.astype(jnp.float32)) + laurel_out) * (
        1.0 / math.sqrt(2.0)
    )
    gate_act = jnp.dot(mixture.astype(jnp.bfloat16), layer_gate, preferred_element_type=jnp.float32)
    gate_out = (jax.nn.gelu(gate_act, approximate=True) * extra_input.astype(jnp.float32)).astype(
        jnp.bfloat16
    )
    return (
        mixture
        + normed(
            jnp.dot(gate_out, layer_proj, preferred_element_type=jnp.float32),
            layer_gain.astype(jnp.float32),
        )
    ).astype(jnp.bfloat16)


def schedule_table(distances, lengths):
    ids = jnp.arange(P_DEV, dtype=jnp.int32)
    before = (distances[None, :] < distances[:, None]) | (
        (distances[None, :] == distances[:, None]) & (ids[None, :] < ids[:, None])
    )
    rank = jnp.sum(before.astype(jnp.int32), axis=1)
    chosen = rank[:, None] == ids[None, :]
    order = jnp.sum(jnp.where(chosen, ids[:, None], 0), axis=0)
    slot = jnp.sum(jnp.where(chosen, distances[:, None], 0), axis=0)
    length = jnp.sum(jnp.where(chosen, lengths[:, None], 0), axis=0)
    minus = jnp.full((1,), -1, jnp.int32)
    first = (slot != jnp.concatenate([minus, slot[:-1]])).astype(jnp.int32)
    last = (slot != jnp.concatenate([slot[1:], minus])).astype(jnp.int32)
    return order, slot, length, first, last


def stage_table(sorted_rows, kv_head, low, high):
    order, slot, length, first, last = sorted_rows
    ids = jnp.arange(P_DEV, dtype=jnp.int32)
    start = jnp.sum((slot < low).astype(jnp.int32))
    count = jnp.sum(((slot >= low) & (slot <= high)).astype(jnp.int32))
    active = (ids < count).astype(jnp.int32)
    where = jnp.clip(start + jnp.minimum(ids, jnp.maximum(count, 1) - 1), 0, P_DEV - 1)
    rows = [jnp.take(x, where) for x in (order, slot - low, length, first, last)]
    kv_row = jnp.full((P_DEV,), kv_head, jnp.int32)
    return jnp.concatenate(rows + [active, kv_row]).astype(jnp.int32)


def body(
    tokens,
    layer_input,
    input_gain,
    q_weight,
    k_weight,
    v_weight,
    q_gain,
    k_gain,
    o_weight,
    attn_gain,
    laurel_left,
    laurel_right,
    laurel_gain,
    layer_gate,
    layer_proj,
    layer_gain,
    piece_keys,
    piece_values,
    piece_owner,
    piece_len,
    cache_keys,
    cache_values,
    cache_len,
):
    req_count = lax.axis_size("req")
    tp_count = lax.axis_size("tp")
    req_index = lax.axis_index("req")
    tp_index = lax.axis_index("tp")
    local_heads = H // tp_count
    kv_head = tp_index * local_heads // (H // KVH)
    full_o_weight = lax.all_gather(o_weight, "tp", axis=0, tiled=True)
    tok_float = tokens.astype(jnp.float32)
    tok_norm = normed(tok_float, input_gain.astype(jnp.float32)).astype(jnp.bfloat16)
    queries = jnp.dot(tok_norm, q_weight, preferred_element_type=jnp.float32).reshape(
        ROWS, local_heads, HD
    )
    queries = (
        normed(queries, q_gain.astype(jnp.float32))
        .astype(jnp.bfloat16)
        .reshape(ROWS, local_heads * HD)
    )
    key_cols = lax.dynamic_slice_in_dim(k_weight, kv_head * HD, HD, 1)
    value_cols = lax.dynamic_slice_in_dim(v_weight, kv_head * HD, HD, 1)
    new_keys = normed(
        jnp.dot(tok_norm, key_cols, preferred_element_type=jnp.float32), k_gain.astype(jnp.float32)
    ).astype(jnp.bfloat16)
    new_values = normed(
        jnp.dot(tok_norm, value_cols, preferred_element_type=jnp.float32), 1.0
    ).astype(jnp.bfloat16)
    own_block = queries[:CH]
    half = P_DEV // 2
    early = [passed_along(own_block, "req", d) for d in range(1, half)]
    held = lax.optimization_barrier((own_block, *early))[0]
    late = [passed_along(held, "req", d) for d in range(half, P_DEV)]
    self_sum, self_stat = self_attention(own_block, new_keys[:CH], new_values[:CH])

    owners = lax.dynamic_slice_in_dim(piece_owner, req_index * P_DEV, P_DEV)
    lengths = lax.dynamic_slice_in_dim(piece_len, req_index * P_DEV, P_DEV)
    distances = (req_index - owners + req_count) % req_count
    sorted_rows = schedule_table(distances, lengths)
    near = piece_attention(
        stage_table(sorted_rows, kv_head, 0, half - 1), [own_block] + early,
        piece_keys, piece_values, self_stat,
    )
    far = piece_attention(
        stage_table(sorted_rows, kv_head, half, P_DEV - 1), late,
        piece_keys, piece_values, near[0],
    )
    packed = list(near) + list(far)
    slots = [packed[0]] + [passed_along(packed[d], "req", -d) for d in range(1, P_DEV)]

    block_ids = (req_index + jnp.arange(P_DEV, dtype=jnp.int32)) % req_count
    block_owners = jnp.take(piece_owner.reshape(req_count, P_DEV), block_ids, axis=0)
    has = jnp.any(block_owners == req_index, axis=1).astype(jnp.int32)
    span_att = combine(has, slots, self_sum, self_stat)
    decode_q = queries[CH:].reshape(DEC_DEV, local_heads, HD)
    cache_key = lax.dynamic_slice_in_dim(cache_keys, kv_head * HD, HD, 2)
    cache_value = lax.dynamic_slice_in_dim(cache_values, kv_head * HD, HD, 2)
    cache_scores = (
        jnp.einsum("thd,tjd->thj", decode_q, cache_key, preferred_element_type=jnp.float32)
        * SCORE_SCALE
    )
    cache_valid = (
        lax.broadcasted_iota(jnp.int32, (DEC_DEV, 1, DCACHE), 2) < cache_len[:, None, None]
    )
    cache_scores = jnp.where(cache_valid, cache_scores, LOWEST)
    own_scores = (
        jnp.einsum("thd,td->th", decode_q, new_keys[CH:], preferred_element_type=jnp.float32)
        * SCORE_SCALE
    )
    decode_top = jnp.maximum(jnp.max(cache_scores, axis=-1), own_scores)
    cache_exp = jnp.exp(cache_scores - decode_top[:, :, None])
    own_exp = jnp.exp(own_scores - decode_top)
    decode_total = jnp.sum(cache_exp, axis=-1) + own_exp
    decode_sum = (
        jnp.einsum(
            "thj,tjd->thd",
            cache_exp.astype(jnp.bfloat16),
            cache_value,
            preferred_element_type=jnp.float32,
        )
        + rounded(own_exp).astype(jnp.float32)[:, :, None]
        * new_values[CH:].astype(jnp.float32)[:, None, :]
    )
    decode_att = (
        (decode_sum / decode_total[:, :, None])
        .reshape(DEC_DEV, local_heads * HD)
        .astype(jnp.bfloat16)
    )
    attended = jnp.concatenate([span_att, decode_att], axis=0)
    part = CH // tp_count

    def rows_of(x, owner):
        return jnp.concatenate(
            [lax.dynamic_slice_in_dim(x, owner * part, part, 0), x[CH:]], axis=0
        )

    proj_sum = jnp.dot(rows_of(attended, tp_index), o_weight, preferred_element_type=jnp.float32)
    for shift in range(1, tp_count):
        target = (tp_index + shift) % tp_count
        got_rows = passed_along(rows_of(attended, target), "tp", shift)
        got_weight = passed_along(o_weight, "tp", shift)
        proj_sum = proj_sum + jnp.dot(got_rows, got_weight, preferred_element_type=jnp.float32)
    mine = finish_rows(
        proj_sum,
        rows_of(tok_float, tp_index),
        rows_of(tok_norm, tp_index),
        rows_of(layer_input, tp_index),
        attn_gain,
        laurel_left,
        laurel_right,
        laurel_gain,
        layer_gate,
        layer_proj,
        layer_gain,
    )
    gathered = [mine] + [passed_along(mine, "tp", shift) for shift in range(1, tp_count)]

    def assemble(me):
        def build(*got):
            blocks = [got[(me - owner) % tp_count][:part] for owner in range(tp_count)]
            return jnp.concatenate(blocks + [got[me][part:]], axis=0)

        return build

    return lax.switch(tp_index, [assemble(me) for me in range(tp_count)], *gathered)


def solution(mesh):
    placed = (
        P("req", None),
        P("req", None),
        P(),
        P(None, "tp"),
        P(),
        P(),
        P(),
        P(),
        P("tp", None),
        P(),
        P(),
        P(),
        P(),
        P(),
        P(),
        P(),
        P("req", None, None),
        P("req", None, None),
        P(),
        P(),
        P("req", None, None),
        P("req", None, None),
        P("req"),
    )
    return jax.shard_map(
        body, mesh=mesh, in_specs=placed, out_specs=P("req", None), check_vma=False
    )
```
